128 devices in a mesh: space: 16 (over y, z), tm: 8 (over x, core).
Axes of the slice: x: 4, y: 4, z: 4, core: 2. Of those that a mesh axis runs over, the one named last changes fastest.
Arguments:
- voxels: bfloat16 [2, 32, 96, 9216], P(None, 'tm', 'space'), may hold values from -6 to 6
- brain_list: int32 [2, 4096], P(None, 'space'), may hold values from -1 to 255, as said below
- owner_slot: int32 [2, 4096], P(None, 'space'), may hold values from -1 to 2047, as said below
- embed_weight: bfloat16 [864, 1024], P(None, 'tm'), may hold values from -0.21875 to 0.21875
- qkv_weight: bfloat16 [1024, 3072], P('space', 'tm'), may hold values from -3.75 to 3.75
- cotangent: bfloat16 [2, 8, 2048, 1024], P(None, 'tm', 'space'), may hold values from -6 to 6
Outputs:
- d_qkv_weight: float32 [1024, 3072], P('space', 'tm')
- d_embed_weight: float32 [864, 1024], P(None, 'tm')
The draws below stay inside these ranges and needn't reach their ends.
Inputs may be any that keep to these rules, and one draw needn't show every extreme that they name: `brain_list`: in each block of 256 entries (one slab of one window) the listed patch numbers are distinct and stand first, -1 after them; a slab lists 128 // 2 to 192 patches, both ends reached in every window, and the slabs of a window list 2048 in all. `owner_slot`: -1 exactly where brain_list is -1. In a window each slot 0 to 2047 occurs once. Taking the window's listed patches slab by slab in list order, their owners (slot // 128) are dealt in turn, so one slab sends at most 12 patches to one owner, and in every window some slab sends exactly 12 to every owner.
All inputs are finite; a program needn't handle non-finite values.
Results may differ from the reference program's by a relative error of at most 0.018.
Values may be sent and summed in bfloat16 or wider, within the bound.
No kernel may reach another device: no remote copies, remote signals or barrier semaphores. Data moves between devices by JAX's collectives and lax.ppermute only.
A program may use at most 128 MiB of HBM per device.

```python
import jax
import jax.numpy as jnp
from jax import lax

D = 1024
HEADS = 16
HD = 64
PATCH = 864
GY = 96
GZ = 96
OWN = 128
WIN = 2
PSLAB = 256
SLABS = 16
TB = 8
GX = 96
FR = 32
SEQ = 2048


def brain_tables(key):
    start_key = jax.random.fold_in(key, 9001)
    key_pair, key_rise, key_pick, key_turn, key_slot = jax.random.split(start_key, 5)
    half_own = OWN // 2
    raises = jax.random.randint(key_rise, (WIN, SLABS // 2), 0, half_own + 1).astype(jnp.int32)
    raises = raises.at[:, 0].set(half_own)
    signed = jnp.stack([raises, -raises], axis=2).reshape(WIN, SLABS)
    slab_scores = jax.random.randint(key_pair, (WIN, SLABS), 0, 1 << 20).astype(jnp.int32) * SLABS + jnp.arange(SLABS, dtype=jnp.int32)[None, :]
    slab_order = jnp.argsort(slab_scores, axis=1).astype(jnp.int32)
    window_rows = jnp.arange(WIN, dtype=jnp.int32)[:, None]
    shifts = jnp.zeros((WIN, SLABS), jnp.int32).at[window_rows, slab_order].set(signed)
    counts = OWN + shifts
    starts = jnp.cumsum(counts, axis=1) - counts
    patch_scores = jax.random.randint(key_pick, (WIN, SLABS, PSLAB), 0, 1 << 20).astype(jnp.int32) * PSLAB + jnp.arange(PSLAB, dtype=jnp.int32)[None, None, :]
    patch_order = jnp.argsort(patch_scores, axis=2).astype(jnp.int32)
    position = jnp.arange(PSLAB, dtype=jnp.int32)[None, None, :]
    listed = position < counts[:, :, None]
    brain_rows = jnp.where(listed, patch_order, -1)
    global_rank = starts[:, :, None] + position
    rotation = jax.random.randint(key_turn, (WIN, 1, 1), 0, SLABS).astype(jnp.int32)
    owner_of = (global_rank + rotation) % SLABS
    within = jnp.minimum(global_rank // SLABS, OWN - 1)
    slot_scores = jax.random.randint(key_slot, (WIN, OWN), 0, 1 << 20).astype(jnp.int32) * OWN + jnp.arange(OWN, dtype=jnp.int32)[None, :]
    shuffle = jnp.argsort(slot_scores, axis=1).astype(jnp.int32)
    shuffled = jnp.take_along_axis(shuffle, within.reshape(WIN, SLABS * PSLAB), axis=1).reshape(WIN, SLABS, PSLAB)
    destination = jnp.where(listed, owner_of * OWN + shuffled, -1)
    return (brain_rows.reshape(WIN, SLABS * PSLAB).astype(jnp.int32), destination.reshape(WIN, SLABS * PSLAB).astype(jnp.int32))


def draw_brain_list(key, part):
    return brain_tables(key)[0]


def draw_owner_slot(key, part):
    return brain_tables(key)[1]


def draw_qkv_weight(key, part):
    normal_draw = jnp.clip(jax.random.normal(jax.random.fold_in(key, 4242), (D, 3 * D), jnp.float32), -4.0, 4.0) * D ** (-0.5)
    return normal_draw.astype(jnp.bfloat16)


def steps_of(stream_key, shape, pieces, least, largest):
    def one(dim, parts):
        steps = jax.random.uniform(jax.random.fold_in(jax.random.fold_in(stream_key, 6), dim), (parts,), jnp.float32, least / len(pieces), largest / len(pieces))
        return jnp.repeat(jnp.exp(steps), shape[dim] // parts).reshape((-1,) + (1,) * (len(shape) - dim - 1))

    gain = one(*pieces[0])
    for cut in pieces[1:]:
        gain = gain * one(*cut)
    return gain


def bell_draw(own_key, shape, width, limit, cuts=(), kind=jnp.bfloat16):
    level = steps_of(own_key, shape, cuts, -0.22, 0.18) if cuts else 1.0
    drawn = jax.random.normal(own_key, shape, jnp.float32) * width * level
    return jnp.minimum(jnp.maximum(drawn, -limit), limit).astype(kind)


def setup_inputs(seed: int = 0) -> dict:
    seeds = jax.random.split(jax.random.key(seed), 7)
    voxels = bell_draw(seeds[0], (WIN, FR, GX, GY * GZ), 1.0, 6.0, ((1, 8), (2, 16)))
    brain_list = draw_brain_list(jax.random.fold_in(seeds[6], 71), 0)
    owner_slot = draw_owner_slot(jax.random.fold_in(seeds[6], 71), 0)
    embed_weight = bell_draw(seeds[3], (PATCH, D), PATCH ** -0.5, 0.21875, ((1, 8),))
    qkv_weight = draw_qkv_weight(jax.random.fold_in(seeds[6], 71), 0)
    cotangent = bell_draw(seeds[5], (WIN, TB, SEQ, D), 0.5, 6.0, ((1, 8), (2, 16)))
    return {"voxels": voxels, "brain_list": brain_list, "owner_slot": owner_slot, "embed_weight": embed_weight, "qkv_weight": qkv_weight, "cotangent": cotangent}


def contract(left, right, left_dim, right_dim):
    return lax.dot_general(left, right, (((left_dim,), (right_dim,)), ((), ())), preferred_element_type=jnp.float32)

def head_grads(queries, key_rows, value_rows, upstream):
    factor = HD ** (-0.5)
    scores = contract(queries, key_rows, 1, 1) * factor
    raised = jnp.exp(scores - lax.optimization_barrier(jnp.max(scores, axis=1, keepdims=True)))
    attention = raised / lax.optimization_barrier(jnp.sum(raised, axis=1, keepdims=True))
    d_attention = contract(upstream, value_rows, 1, 1)
    inner_sum = lax.optimization_barrier(jnp.sum(attention * d_attention, axis=1, keepdims=True))
    d_scores = (attention * (d_attention - inner_sum) * factor).astype(jnp.bfloat16)
    grad_query = contract(d_scores, key_rows, 1, 0).astype(jnp.bfloat16)
    grad_key = contract(d_scores, queries, 0, 0).astype(jnp.bfloat16)
    grad_value = contract(attention.astype(jnp.bfloat16), upstream, 0, 0).astype(jnp.bfloat16)
    return (grad_query, grad_key, grad_value)

def one_head(inputs):
    grad_query, grad_key, grad_value = head_grads(inputs[0], inputs[1], inputs[2], inputs[3])
    return jnp.stack([grad_query, grad_key, grad_value])

def reference(voxels, brain_list, owner_slot, embed_weight, qkv_weight, cotangent):
    side_y = GY // 6
    side_z = GZ // 6
    grid_view = voxels.reshape(WIN, TB, 4, SLABS, 6, side_y, 6, side_z, 6)
    patches = grid_view.transpose(0, 1, 3, 5, 7, 2, 4, 6, 8).reshape(WIN, TB, SLABS * PSLAB, PATCH)
    entry_index = jnp.arange(SLABS * PSLAB, dtype=jnp.int32)
    source = (entry_index // PSLAB * PSLAB)[None, :] + brain_list.astype(jnp.int32)
    target = jnp.where(owner_slot >= 0, owner_slot, SEQ).astype(jnp.int32)
    window_rows = jnp.arange(WIN, dtype=jnp.int32)[:, None]
    slot_source = jnp.zeros((WIN, SEQ), jnp.int32).at[window_rows, target].set(source.astype(jnp.int32), mode='drop')
    window_index = jnp.arange(WIN, dtype=jnp.int32)[:, None, None]
    time_index = jnp.arange(TB, dtype=jnp.int32)[None, :, None]
    chosen = patches[window_index, time_index, slot_source[:, None, :]]
    chosen_flat = chosen.reshape(WIN * TB * SEQ, PATCH)
    tokens = jnp.dot(chosen_flat, embed_weight, preferred_element_type=jnp.float32).astype(jnp.bfloat16)
    widened = tokens.astype(jnp.float32)
    center = widened - lax.optimization_barrier(jnp.mean(widened, axis=1, keepdims=True))
    inverse = lax.rsqrt(lax.optimization_barrier(jnp.mean(center * center, axis=1, keepdims=True)) + 1e-05)
    normed = center * inverse
    hidden = normed.astype(jnp.bfloat16)
    packed = jnp.dot(hidden, qkv_weight, preferred_element_type=jnp.float32).astype(jnp.bfloat16)
    lanes = packed.reshape(WIN * TB, SEQ, 3, HEADS, HD).transpose(2, 0, 3, 1, 4).reshape(3, WIN * TB * HEADS, SEQ, HD)
    upstream = cotangent.reshape(WIN * TB, SEQ, HEADS, HD).transpose(0, 2, 1, 3).reshape(WIN * TB * HEADS, SEQ, HD)
    grads = lax.map(one_head, (lanes[0], lanes[1], lanes[2], upstream))
    d_packed = grads.reshape(WIN * TB, HEADS, 3, SEQ, HD).transpose(0, 3, 2, 1, 4).reshape(WIN * TB * SEQ, 3 * D)
    d_qkv_weight = contract(hidden, d_packed, 0, 0)
    d_hidden = contract(d_packed, qkv_weight, 1, 1)
    first_mean = lax.optimization_barrier(jnp.mean(d_hidden, axis=1, keepdims=True))
    second_mean = lax.optimization_barrier(jnp.mean(d_hidden * normed, axis=1, keepdims=True))
    d_tokens = (inverse * (d_hidden - first_mean - normed * second_mean)).astype(jnp.bfloat16)
    d_embed_weight = contract(chosen_flat, d_tokens, 0, 0)
    return (d_qkv_weight, d_embed_weight)
```

```python
import jax
import jax.numpy as jnp
from jax import lax
from jax.sharding import PartitionSpec as P
from jax.experimental import pallas as pl
from jax.experimental.pallas import tpu as pltpu

D = 1024
HD = 64
PATCH = 864
GY = 96
GZ = 96
OWN = 128
PSLAB = 256


def for_sending(array):

    def short(part):
        return part.astype(jnp.bfloat16) if part.dtype == jnp.float32 else part

    return jax.tree.map(short, array)


def contract(left, right, left_dim, right_dim):
    return lax.dot_general(
        left, right, (((left_dim,), (right_dim,)), ((), ())), preferred_element_type=jnp.float32
    )


def bucket_index(slots, slab_count, capacity):
    owner_of = jnp.where(slots >= 0, slots // OWN, slab_count)
    hits = (owner_of[..., None] == jnp.arange(slab_count, dtype=jnp.int32)).astype(jnp.int32)
    earlier = jnp.cumsum(hits, axis=-2) - hits
    position = jnp.sum(earlier * hits, axis=-1)
    return jnp.where(slots >= 0, owner_of * capacity + position, slab_count * capacity)


QUERY_BLOCK = 256


def attention_kernel(q_ref, k_ref, v_ref, g_ref, dq_ref, dk_ref, dv_ref, dk_acc, dv_acc):
    step = pl.program_id(1)
    factor = HD ** (-0.5)

    @pl.when(step == 0)
    def _():
        dk_acc[...] = jnp.zeros_like(dk_acc)
        dv_acc[...] = jnp.zeros_like(dv_acc)

    queries = q_ref[0]
    key_rows = k_ref[0]
    value_rows = v_ref[0]
    upstream = g_ref[0]
    scores = contract(queries, key_rows, 1, 1) * factor
    raised = jnp.exp(scores - jnp.max(scores, axis=1, keepdims=True))
    attention = raised / jnp.sum(raised, axis=1, keepdims=True)
    d_attention = contract(upstream, value_rows, 1, 1)
    inner_sum = jnp.sum(attention * d_attention, axis=1, keepdims=True)
    d_scores = (attention * (d_attention - inner_sum) * factor).astype(jnp.bfloat16)
    dq_ref[0] = contract(d_scores, key_rows, 1, 0).astype(jnp.bfloat16)
    dk_acc[...] += contract(d_scores, queries, 0, 0)
    dv_acc[...] += contract(attention.astype(jnp.bfloat16), upstream, 0, 0)

    @pl.when(step == pl.num_programs(1) - 1)
    def _():
        dk_ref[0] = dk_acc[...].astype(jnp.bfloat16)
        dv_ref[0] = dv_acc[...].astype(jnp.bfloat16)


def attention_grads(queries, key_rows, value_rows, upstream):
    windows, length, width = queries.shape
    block = min(QUERY_BLOCK, length)
    row_spec = pl.BlockSpec((1, block, width), lambda w, i: (w, i, 0))
    full_spec = pl.BlockSpec((1, length, width), lambda w, i: (w, 0, 0))
    shape = jax.ShapeDtypeStruct((windows, length, width), jnp.bfloat16)
    flops = 10 * windows * length * length * width
    return pl.pallas_call(
        attention_kernel,
        grid=(windows, length // block),
        in_specs=[row_spec, full_spec, full_spec, row_spec],
        out_specs=[row_spec, full_spec, full_spec],
        out_shape=[shape, shape, shape],
        scratch_shapes=[
            pltpu.VMEM((length, width), jnp.float32),
            pltpu.VMEM((length, width), jnp.float32),
        ],
        compiler_params=pltpu.CompilerParams(
            dimension_semantics=("arbitrary", "arbitrary"),
            vmem_limit_bytes=48 * 1024 * 1024,
        ),
        cost_estimate=pl.CostEstimate(
            flops=flops,
            transcendentals=windows * length * length,
            bytes_accessed=7 * windows * length * width * 2,
        ),
    )(queries, key_rows, value_rows, upstream)


def heads_grad(exchanged):
    lanes, upstream = exchanged
    grad_query, grad_key, grad_value = attention_grads(
        lanes[:, :, 0, :], lanes[:, :, 1, :], lanes[:, :, 2, :], upstream[:, :, 0, :]
    )
    result = jnp.stack([grad_query, grad_key, grad_value], axis=2)
    return lax.all_to_all(result, "space", split_axis=1, concat_axis=3, tiled=True)


def body(voxels, brain_list, owner_slot, embed_weight, qkv_weight, cotangent):
    slab_count = lax.axis_size("space")
    my_slab = lax.axis_index("space")
    capacity = 3 * OWN // (2 * slab_count)
    windows = voxels.shape[0]
    row_total = windows * OWN
    side_y = GY // 6
    side_z = GZ // 6
    local_patches = (
        voxels.reshape(windows, 4, 6, side_y, 6, side_z, 6)
        .transpose(0, 3, 5, 1, 2, 4, 6)
        .reshape(windows, side_y * side_z, PATCH)
    )
    window_rows = jnp.arange(windows, dtype=jnp.int32)[:, None]
    my_buckets = bucket_index(owner_slot, slab_count, capacity)
    entries = jnp.broadcast_to(jnp.arange(PSLAB, dtype=jnp.int32)[None, :], (windows, PSLAB))
    sender = (
        jnp.full((windows, slab_count * capacity), -1, jnp.int32)
        .at[window_rows, my_buckets]
        .set(entries, mode="drop")
    )
    patch_id = brain_list[window_rows, jnp.maximum(sender, 0)]
    patch_rows = local_patches[window_rows, jnp.maximum(patch_id, 0)]
    patch_rows = jnp.where((sender >= 0)[:, :, None], patch_rows, jnp.zeros_like(patch_rows))
    all_slots = lax.all_gather(owner_slot, "space", axis=1, tiled=True).reshape(
        windows, slab_count, PSLAB
    )
    their_buckets = bucket_index(all_slots, slab_count, capacity)
    arrival = (
        jnp.arange(slab_count, dtype=jnp.int32)[None, :, None] * capacity + their_buckets % capacity
    )
    mine_flag = (all_slots >= 0) & (all_slots // OWN == my_slab)
    target = jnp.where(mine_flag, all_slots % OWN, OWN)
    placement = (
        jnp.zeros((windows, OWN), jnp.int32)
        .at[window_rows[:, :, None], target]
        .set(arrival, mode="drop")
    )
    sent_tokens = (
        jnp.einsum(
            "wnp,pd->wnd",
            patch_rows,
            lax.all_gather(embed_weight, "tm", axis=1, tiled=True),
            preferred_element_type=jnp.float32,
        )
        .astype(jnp.bfloat16)
        .reshape(windows, slab_count, capacity, D)
    )
    arrived = lax.all_to_all(sent_tokens, "space", split_axis=1, concat_axis=1, tiled=True).reshape(
        windows, slab_count * capacity, D
    )
    tokens = arrived[window_rows, placement]
    widened = tokens.reshape(row_total, D).astype(jnp.float32)
    center = widened - jnp.mean(widened, axis=1, keepdims=True)
    inverse = lax.rsqrt(jnp.mean(center * center, axis=1, keepdims=True) + 1e-05)
    normed = center * inverse
    hidden = normed.astype(jnp.bfloat16)
    wide_rows = lax.all_gather(qkv_weight, "tm", axis=1, tiled=True)
    section = hidden
    packed = jnp.dot(
        section,
        lax.all_gather(wide_rows, "space", axis=0, tiled=True),
        preferred_element_type=jnp.float32,
    ).astype(jnp.bfloat16)
    lanes_in = packed.reshape(windows, OWN, 3, D)
    upstream_in = cotangent.reshape(windows, OWN, 1, D)
    d_packed = heads_grad(
        (
            lax.all_to_all(lanes_in, "space", split_axis=3, concat_axis=1, tiled=True),
            lax.all_to_all(upstream_in, "space", split_axis=3, concat_axis=1, tiled=True),
        )
    ).reshape(row_total, 3 * D)
    d_hidden = contract(d_packed, lax.all_gather(wide_rows, "space", axis=0, tiled=True), 1, 1)
    tm_count = lax.axis_size("tm")
    partial = contract(hidden, d_packed, 0, 0).astype(jnp.bfloat16)
    row_block = D // slab_count
    col_block = 3 * D // tm_count
    blocks = (
        partial.reshape(slab_count, row_block, tm_count, col_block)
        .transpose(0, 2, 1, 3)
        .reshape(slab_count * tm_count, row_block, col_block)
    )
    d_qkv_weight = (
        lax.psum_scatter(blocks, ("space", "tm"), scatter_dimension=0, tiled=True)
        .reshape(row_block, col_block)
        .astype(jnp.float32)
    )
    first_mean = jnp.mean(d_hidden, axis=1, keepdims=True)
    second_mean = jnp.mean(d_hidden * normed, axis=1, keepdims=True)
    d_tokens = (
        (inverse * (d_hidden - first_mean - normed * second_mean))
        .astype(jnp.bfloat16)
        .reshape(windows, OWN, D)
    )
    returned = (
        jnp.zeros((windows, slab_count * capacity, D), jnp.bfloat16)
        .at[window_rows, placement]
        .set(d_tokens)
    )
    came_back = lax.all_to_all(
        returned.reshape(windows, slab_count, capacity, D),
        "space",
        split_axis=1,
        concat_axis=1,
        tiled=True,
    ).reshape(windows, slab_count * capacity, D)
    embed_partial = jnp.einsum(
        "wnp,wnd->pd", patch_rows, came_back, preferred_element_type=jnp.float32
    )
    embed_cols_sum = lax.psum_scatter(
        embed_partial.astype(jnp.bfloat16), "tm", scatter_dimension=1, tiled=True
    )
    d_embed_weight = lax.psum(embed_cols_sum, "space").astype(jnp.float32)
    return (d_qkv_weight, d_embed_weight)


def solution(mesh):
    placed = (
        P(None, "tm", "space", None),
        P(None, "space"),
        P(None, "space"),
        P(None, "tm"),
        P("space", "tm"),
        P(None, "tm", "space", None),
    )
    return jax.shard_map(
        body,
        mesh=mesh,
        in_specs=placed,
        out_specs=(P("space", "tm"), P(None, "tm")),
        check_vma=False,
    )
```

```python
import jax
import jax.numpy as jnp
from jax import lax
from jax.sharding import PartitionSpec as P
from jax.experimental import pallas as pl
from jax.experimental.pallas import tpu as pltpu

D = 1024
HD = 64
PATCH = 864
GY = 96
GZ = 96
OWN = 128
PSLAB = 256


def for_sending(array):

    def short(part):
        return part.astype(jnp.bfloat16) if part.dtype == jnp.float32 else part

    return jax.tree.map(short, array)


def contract(left, right, left_dim, right_dim):
    return lax.dot_general(
        left, right, (((left_dim,), (right_dim,)), ((), ())), preferred_element_type=jnp.float32
    )


def select(onehot, rows):
    return jnp.einsum("wab,wbc->wac", onehot, rows, preferred_element_type=jnp.float32)


def bucket_index(slots, slab_count, capacity):
    entries = slots.shape[-1]
    owner_of = jnp.where(slots >= 0, slots // OWN, slab_count)
    hits = (owner_of[..., None] == jnp.arange(slab_count, dtype=jnp.int32)).astype(jnp.bfloat16)
    order = jnp.arange(entries, dtype=jnp.int32)
    before = (order[None, :] < order[:, None]).astype(jnp.bfloat16)
    earlier = jnp.einsum("ij,wjo->wio", before, hits, preferred_element_type=jnp.float32)
    position = jnp.sum(earlier * hits.astype(jnp.float32), axis=-1).astype(jnp.int32)
    return jnp.where(slots >= 0, owner_of * capacity + position, slab_count * capacity)


QUERY_BLOCK = 256


def attention_kernel(q_ref, k_ref, v_ref, g_ref, dq_ref, dk_ref, dv_ref, dk_acc, dv_acc):
    step = pl.program_id(1)
    factor = HD ** (-0.5)

    @pl.when(step == 0)
    def _():
        dk_acc[...] = jnp.zeros_like(dk_acc)
        dv_acc[...] = jnp.zeros_like(dv_acc)

    queries = q_ref[0]
    key_rows = k_ref[0]
    value_rows = v_ref[0]
    upstream = g_ref[0]
    scores = contract(queries, key_rows, 1, 1) * factor
    raised = jnp.exp(scores - jnp.max(scores, axis=1, keepdims=True))
    attention = raised / jnp.sum(raised, axis=1, keepdims=True)
    d_attention = contract(upstream, value_rows, 1, 1)
    inner_sum = jnp.sum(attention * d_attention, axis=1, keepdims=True)
    d_scores = (attention * (d_attention - inner_sum) * factor).astype(jnp.bfloat16)
    dq_ref[0] = contract(d_scores, key_rows, 1, 0).astype(jnp.bfloat16)
    dk_acc[...] += contract(d_scores, queries, 0, 0)
    dv_acc[...] += contract(attention.astype(jnp.bfloat16), upstream, 0, 0)

    @pl.when(step == pl.num_programs(1) - 1)
    def _():
        dk_ref[0] = dk_acc[...].astype(jnp.bfloat16)
        dv_ref[0] = dv_acc[...].astype(jnp.bfloat16)


def attention_grads(queries, key_rows, value_rows, upstream):
    windows, length, width = queries.shape
    block = min(QUERY_BLOCK, length)
    row_spec = pl.BlockSpec((1, block, width), lambda w, i: (w, i, 0))
    full_spec = pl.BlockSpec((1, length, width), lambda w, i: (w, 0, 0))
    shape = jax.ShapeDtypeStruct((windows, length, width), jnp.bfloat16)
    flops = 10 * windows * length * length * width
    return pl.pallas_call(
        attention_kernel,
        grid=(windows, length // block),
        in_specs=[row_spec, full_spec, full_spec, row_spec],
        out_specs=[row_spec, full_spec, full_spec],
        out_shape=[shape, shape, shape],
        scratch_shapes=[
            pltpu.VMEM((length, width), jnp.float32),
            pltpu.VMEM((length, width), jnp.float32),
        ],
        compiler_params=pltpu.CompilerParams(
            dimension_semantics=("arbitrary", "arbitrary"),
            vmem_limit_bytes=48 * 1024 * 1024,
        ),
        cost_estimate=pl.CostEstimate(
            flops=flops,
            transcendentals=windows * length * length,
            bytes_accessed=7 * windows * length * width * 2,
        ),
    )(queries, key_rows, value_rows, upstream)


def heads_grad(exchanged):
    lanes, upstream = exchanged
    grad_query, grad_key, grad_value = attention_grads(
        lanes[:, :, 0, :], lanes[:, :, 1, :], lanes[:, :, 2, :], upstream[:, :, 0, :]
    )
    result = jnp.stack([grad_query, grad_key, grad_value], axis=2)
    return lax.all_to_all(result, "space", split_axis=1, concat_axis=3, tiled=True)


def body(voxels, brain_list, owner_slot, embed_weight, qkv_weight, cotangent):
    slab_count = lax.axis_size("space")
    tm_count = lax.axis_size("tm")
    capacity = 3 * OWN // (2 * slab_count)
    buckets = slab_count * capacity
    windows = voxels.shape[0]
    row_total = windows * OWN
    side_y = GY // 6
    side_z = GZ // 6
    local_patches = (
        voxels.reshape(windows, 4, 6, side_y, 6, side_z, 6)
        .transpose(0, 3, 5, 1, 2, 4, 6)
        .reshape(windows, side_y * side_z, PATCH)
    )
    my_buckets = bucket_index(owner_slot, slab_count, capacity)
    to_bucket = (
        my_buckets[:, None, :] == jnp.arange(buckets, dtype=jnp.int32)[None, :, None]
    ).astype(jnp.bfloat16)
    is_patch = (
        brain_list[:, :, None] == jnp.arange(PSLAB, dtype=jnp.int32)[None, None, :]
    ).astype(jnp.bfloat16)
    picks = select(to_bucket, is_patch).astype(jnp.bfloat16)
    slot_code = (jnp.where(owner_slot >= 0, owner_slot % OWN, -1) + 1).astype(jnp.bfloat16)
    bucket_code = select(to_bucket, slot_code[:, :, None])
    width = -(-(PATCH + 1) // 128) * 128
    payload = jnp.concatenate(
        [
            select(picks, local_patches).astype(jnp.bfloat16),
            bucket_code.astype(jnp.bfloat16),
            jnp.zeros((windows, buckets, width - PATCH - 1), jnp.bfloat16),
        ],
        axis=2,
    ).reshape(windows, slab_count, capacity, width)
    arrived = lax.all_to_all(payload, "space", split_axis=1, concat_axis=1, tiled=True).reshape(
        windows, buckets, width
    )
    arrival_slot = arrived[:, :, PATCH].astype(jnp.int32) - 1
    to_slot = (
        arrival_slot[:, None, :] == jnp.arange(OWN, dtype=jnp.int32)[None, :, None]
    ).astype(jnp.bfloat16)
    chosen = select(to_slot, arrived[:, :, :PATCH]).astype(jnp.bfloat16).reshape(row_total, PATCH)
    full_embed = lax.all_gather(embed_weight, "tm", axis=1, tiled=True)
    tokens = jnp.dot(chosen, full_embed, preferred_element_type=jnp.float32).astype(jnp.bfloat16)
    widened = tokens.astype(jnp.float32)
    center = widened - jnp.mean(widened, axis=1, keepdims=True)
    inverse = lax.rsqrt(jnp.mean(center * center, axis=1, keepdims=True) + 1e-05)
    normed = center * inverse
    hidden = normed.astype(jnp.bfloat16)
    wide_rows = lax.all_gather(qkv_weight, "tm", axis=1, tiled=True)
    full_qkv = lax.all_gather(wide_rows, "space", axis=0, tiled=True)
    packed = jnp.dot(hidden, full_qkv, preferred_element_type=jnp.float32).astype(jnp.bfloat16)
    lanes_in = packed.reshape(windows, OWN, 3, D)
    upstream_in = cotangent.reshape(windows, OWN, 1, D)
    d_packed = heads_grad(
        (
            lax.all_to_all(lanes_in, "space", split_axis=3, concat_axis=1, tiled=True),
            lax.all_to_all(upstream_in, "space", split_axis=3, concat_axis=1, tiled=True),
        )
    ).reshape(row_total, 3 * D)
    my_rows = lax.psum_scatter(
        contract(hidden, d_packed, 0, 0).astype(jnp.bfloat16),
        "space",
        scatter_dimension=0,
        tiled=True,
    )
    d_qkv_weight = lax.psum_scatter(my_rows, "tm", scatter_dimension=1, tiled=True).astype(
        jnp.float32
    )
    d_hidden = contract(d_packed, full_qkv, 1, 1)
    first_mean = jnp.mean(d_hidden, axis=1, keepdims=True)
    second_mean = jnp.mean(d_hidden * normed, axis=1, keepdims=True)
    d_tokens = (inverse * (d_hidden - first_mean - normed * second_mean)).astype(jnp.bfloat16)
    embed_partial = contract(chosen, d_tokens, 0, 0)
    embed_cols = lax.psum_scatter(
        embed_partial.astype(jnp.bfloat16), "tm", scatter_dimension=1, tiled=True
    )
    chunk = -(-PATCH // slab_count)
    padded = jnp.pad(embed_cols, ((0, chunk * slab_count - PATCH), (0, 0)))
    spread = lax.all_to_all(
        padded.reshape(slab_count, chunk, -1), "space", split_axis=0, concat_axis=0, tiled=True
    )
    reduced = jnp.sum(spread.astype(jnp.float32), axis=0)
    gathered = lax.all_to_all(
        jnp.broadcast_to(reduced[None], (slab_count,) + reduced.shape),
        "space",
        split_axis=0,
        concat_axis=0,
        tiled=True,
    )
    d_embed_weight = gathered.reshape(chunk * slab_count, -1)[:PATCH]
    return (d_qkv_weight, d_embed_weight)


def solution(mesh):
    placed = (
        P(None, "tm", "space", None),
        P(None, "space"),
        P(None, "space"),
        P(None, "tm"),
        P("space", "tm"),
        P(None, "tm", "space", None),
    )
    return jax.shard_map(
        body,
        mesh=mesh,
        in_specs=placed,
        out_specs=(P("space", "tm"), P(None, "tm")),
        check_vma=False,
    )
```

```python
import jax
import jax.numpy as jnp
from jax import lax
from jax.sharding import PartitionSpec as P
from jax.experimental import pallas as pl
from jax.experimental.pallas import tpu as pltpu

D = 1024
HD = 64
PATCH = 864
GY = 96
GZ = 96
OWN = 128
PSLAB = 256


def for_sending(array):

    def short(part):
        return part.astype(jnp.bfloat16) if part.dtype == jnp.float32 else part

    return jax.tree.map(short, array)


def contract(left, right, left_dim, right_dim):
    return lax.dot_general(
        left, right, (((left_dim,), (right_dim,)), ((), ())), preferred_element_type=jnp.float32
    )


def select(onehot, rows):
    return jnp.einsum("wab,wbc->wac", onehot, rows, preferred_element_type=jnp.float32)


def bucket_index(slots, slab_count, capacity):
    entries = slots.shape[-1]
    owner_of = jnp.where(slots >= 0, slots // OWN, slab_count)
    hits = (owner_of[..., None] == jnp.arange(slab_count, dtype=jnp.int32)).astype(jnp.bfloat16)
    order = jnp.arange(entries, dtype=jnp.int32)
    before = (order[None, :] < order[:, None]).astype(jnp.bfloat16)
    earlier = jnp.einsum("ij,wjo->wio", before, hits, preferred_element_type=jnp.float32)
    position = jnp.sum(earlier * hits.astype(jnp.float32), axis=-1).astype(jnp.int32)
    return jnp.where(slots >= 0, owner_of * capacity + position, slab_count * capacity)


QUERY_BLOCK = 256


def attention_kernel(lanes_ref, g_ref, out_ref, k_s, v_s, dk_acc, dv_acc):
    step = pl.program_id(1)
    owners, _, slots, _ = lanes_ref.shape
    per_block = g_ref.shape[0]
    length = owners * slots
    block = per_block * slots
    factor = HD ** (-0.5)

    @pl.when(step == 0)
    def _():
        k_s[...] = lanes_ref[:, 0, :, HD : 2 * HD].reshape(length, HD)
        v_s[...] = lanes_ref[:, 0, :, 2 * HD : 3 * HD].reshape(length, HD)
        dk_acc[...] = jnp.zeros_like(dk_acc)
        dv_acc[...] = jnp.zeros_like(dv_acc)

    first = pl.multiple_of(step * per_block, per_block)
    queries = lanes_ref[pl.ds(first, per_block), 0, :, 0:HD].reshape(block, HD)
    upstream = g_ref[:, 0, :, :].reshape(block, HD)
    key_rows = k_s[...]
    value_rows = v_s[...]
    scores = contract(queries, key_rows, 1, 1) * factor
    raised = jnp.exp(scores - jnp.max(scores, axis=1, keepdims=True))
    attention = raised / jnp.sum(raised, axis=1, keepdims=True)
    d_attention = contract(upstream, value_rows, 1, 1)
    inner_sum = jnp.sum(attention * d_attention, axis=1, keepdims=True)
    d_scores = (attention * (d_attention - inner_sum) * factor).astype(jnp.bfloat16)
    grad_query = contract(d_scores, key_rows, 1, 0).astype(jnp.bfloat16)
    out_ref[pl.ds(first, per_block), 0, :, 0:HD] = grad_query.reshape(per_block, slots, HD)
    dk_acc[...] += contract(d_scores, queries, 0, 0)
    dv_acc[...] += contract(attention.astype(jnp.bfloat16), upstream, 0, 0)

    @pl.when(step == pl.num_programs(1) - 1)
    def _():
        out_ref[:, 0, :, HD : 2 * HD] = dk_acc[...].astype(jnp.bfloat16).reshape(owners, slots, HD)
        out_ref[:, 0, :, 2 * HD : 3 * HD] = dv_acc[...].astype(jnp.bfloat16).reshape(owners, slots, HD)


def attention_grads(lanes, upstream):
    owners, windows, slots, width = lanes.shape
    length = owners * slots
    per_block = max(1, QUERY_BLOCK // slots)
    lanes_spec = pl.BlockSpec((owners, 1, slots, width), lambda w, i: (0, w, 0, 0))
    g_spec = pl.BlockSpec((per_block, 1, slots, HD), lambda w, i: (i, w, 0, 0))
    flops = 10 * windows * length * length * HD
    return pl.pallas_call(
        attention_kernel,
        grid=(windows, owners // per_block),
        in_specs=[lanes_spec, g_spec],
        out_specs=lanes_spec,
        out_shape=jax.ShapeDtypeStruct(lanes.shape, jnp.bfloat16),
        scratch_shapes=[
            pltpu.VMEM((length, HD), jnp.bfloat16),
            pltpu.VMEM((length, HD), jnp.bfloat16),
            pltpu.VMEM((length, HD), jnp.float32),
            pltpu.VMEM((length, HD), jnp.float32),
        ],
        compiler_params=pltpu.CompilerParams(
            dimension_semantics=("arbitrary", "arbitrary"),
            vmem_limit_bytes=48 * 1024 * 1024,
        ),
        cost_estimate=pl.CostEstimate(
            flops=flops,
            transcendentals=windows * length * length,
            bytes_accessed=7 * windows * length * HD * 2,
        ),
    )(lanes, upstream)


def body(voxels, brain_list, owner_slot, embed_weight, qkv_weight, cotangent):
    slab_count = lax.axis_size("space")
    tm_count = lax.axis_size("tm")
    capacity = 3 * OWN // (2 * slab_count)
    buckets = slab_count * capacity
    windows = voxels.shape[0]
    row_total = windows * OWN
    side_y = GY // 6
    side_z = GZ // 6
    local_patches = (
        voxels.reshape(windows, 4, 6, side_y, 6, side_z, 6)
        .transpose(0, 3, 5, 1, 2, 4, 6)
        .reshape(windows, side_y * side_z, PATCH)
    )
    my_buckets = bucket_index(owner_slot, slab_count, capacity)
    to_bucket = (
        my_buckets[:, None, :] == jnp.arange(buckets, dtype=jnp.int32)[None, :, None]
    ).astype(jnp.bfloat16)
    is_patch = (
        brain_list[:, :, None] == jnp.arange(PSLAB, dtype=jnp.int32)[None, None, :]
    ).astype(jnp.bfloat16)
    picks = select(to_bucket, is_patch).astype(jnp.bfloat16)
    slot_code = (jnp.where(owner_slot >= 0, owner_slot % OWN, -1) + 1).astype(jnp.bfloat16)
    bucket_code = select(to_bucket, slot_code[:, :, None])
    width = -(-(PATCH + 1) // 128) * 128
    payload = jnp.concatenate(
        [
            select(picks, local_patches).astype(jnp.bfloat16),
            bucket_code.astype(jnp.bfloat16),
            jnp.zeros((windows, buckets, width - PATCH - 1), jnp.bfloat16),
        ],
        axis=2,
    ).reshape(windows, slab_count, capacity, width)
    arrived = lax.all_to_all(payload, "space", split_axis=1, concat_axis=1, tiled=True).reshape(
        windows, buckets, width
    )
    arrival_slot = arrived[:, :, PATCH].astype(jnp.int32) - 1
    to_slot = (
        arrival_slot[:, None, :] == jnp.arange(OWN, dtype=jnp.int32)[None, :, None]
    ).astype(jnp.bfloat16)
    chosen = select(to_slot, arrived[:, :, :PATCH]).astype(jnp.bfloat16).reshape(row_total, PATCH)
    full_embed = lax.all_gather(embed_weight, "tm", axis=1, tiled=True)
    tokens = jnp.dot(chosen, full_embed, preferred_element_type=jnp.float32).astype(jnp.bfloat16)
    widened = tokens.astype(jnp.float32)
    center = widened - jnp.mean(widened, axis=1, keepdims=True)
    inverse = lax.rsqrt(jnp.mean(center * center, axis=1, keepdims=True) + 1e-05)
    normed = center * inverse
    hidden = normed.astype(jnp.bfloat16)
    wide_rows = lax.all_gather(qkv_weight, "tm", axis=1, tiled=True)
    full_qkv = lax.all_gather(wide_rows, "space", axis=0, tiled=True)
    heads = D // HD
    head_qkv = full_qkv.reshape(D, 3, heads, HD).transpose(0, 2, 1, 3).reshape(D, 3 * D)
    packed = jnp.dot(hidden, head_qkv, preferred_element_type=jnp.float32).astype(jnp.bfloat16)
    lanes_out = packed.reshape(windows, OWN, heads, 3 * HD).transpose(2, 0, 1, 3)
    upstream_out = cotangent.reshape(windows, OWN, heads, HD).transpose(2, 0, 1, 3)
    lanes = lax.all_to_all(lanes_out, "space", split_axis=0, concat_axis=0, tiled=True)
    upstream = lax.all_to_all(upstream_out, "space", split_axis=0, concat_axis=0, tiled=True)
    grads = attention_grads(lanes, upstream)
    returned = lax.all_to_all(grads, "space", split_axis=0, concat_axis=0, tiled=True)
    d_packed = (
        returned.reshape(heads, windows, OWN, 3, HD)
        .transpose(1, 2, 3, 0, 4)
        .reshape(row_total, 3 * D)
    )
    my_rows = lax.psum_scatter(
        contract(hidden, d_packed, 0, 0).astype(jnp.bfloat16),
        "space",
        scatter_dimension=0,
        tiled=True,
    )
    row_block = my_rows.shape[0]
    col_block = 3 * D // tm_count
    qkv_parts = lax.all_to_all(
        my_rows.reshape(row_block, tm_count, col_block).transpose(1, 0, 2),
        "tm",
        split_axis=0,
        concat_axis=0,
        tiled=True,
    )
    d_qkv_weight = jnp.sum(qkv_parts.astype(jnp.float32), axis=0)
    d_hidden = contract(d_packed, full_qkv, 1, 1)
    first_mean = jnp.mean(d_hidden, axis=1, keepdims=True)
    second_mean = jnp.mean(d_hidden * normed, axis=1, keepdims=True)
    d_tokens = (inverse * (d_hidden - first_mean - normed * second_mean)).astype(jnp.bfloat16)
    embed_partial = contract(chosen, d_tokens, 0, 0)
    embed_block = D // tm_count
    embed_parts = lax.all_to_all(
        embed_partial.astype(jnp.bfloat16).reshape(PATCH, tm_count, embed_block).transpose(1, 0, 2),
        "tm",
        split_axis=0,
        concat_axis=0,
        tiled=True,
    )
    embed_cols = jnp.sum(embed_parts.astype(jnp.float32), axis=0)
    chunk = -(-PATCH // slab_count)
    padded = jnp.pad(embed_cols, ((0, chunk * slab_count - PATCH), (0, 0)))
    spread = lax.all_to_all(
        padded.reshape(slab_count, chunk, -1), "space", split_axis=0, concat_axis=0, tiled=True
    )
    reduced = jnp.sum(spread, axis=0)
    gathered = lax.all_to_all(
        jnp.broadcast_to(reduced[None], (slab_count,) + reduced.shape),
        "space",
        split_axis=0,
        concat_axis=0,
        tiled=True,
    )
    d_embed_weight = gathered.reshape(chunk * slab_count, -1)[:PATCH]
    return (d_qkv_weight, d_embed_weight)


def solution(mesh):
    placed = (
        P(None, "tm", "space", None),
        P(None, "space"),
        P(None, "space"),
        P(None, "tm"),
        P("space", "tm"),
        P(None, "tm", "space", None),
    )
    return jax.shard_map(
        body,
        mesh=mesh,
        in_specs=placed,
        out_specs=(P("space", "tm"), P(None, "tm")),
        check_vma=False,
    )
```

```python
import jax
import jax.numpy as jnp
from jax import lax
from jax.sharding import PartitionSpec as P
from jax.experimental import pallas as pl
from jax.experimental.pallas import tpu as pltpu

D = 1024
HD = 64
PATCH = 864
GY = 96
GZ = 96
OWN = 128
PSLAB = 256


def for_sending(array):

    def short(part):
        return part.astype(jnp.bfloat16) if part.dtype == jnp.float32 else part

    return jax.tree.map(short, array)


def contract(left, right, left_dim, right_dim):
    return lax.dot_general(
        left, right, (((left_dim,), (right_dim,)), ((), ())), preferred_element_type=jnp.float32
    )


def select(onehot, rows):
    return jnp.einsum("wab,wbc->wac", onehot, rows, preferred_element_type=jnp.float32)


def bucket_index(slots, slab_count, capacity):
    entries = slots.shape[-1]
    owner_of = jnp.where(slots >= 0, slots // OWN, slab_count)
    hits = (owner_of[..., None] == jnp.arange(slab_count, dtype=jnp.int32)).astype(jnp.bfloat16)
    order = jnp.arange(entries, dtype=jnp.int32)
    before = (order[None, :] < order[:, None]).astype(jnp.bfloat16)
    earlier = jnp.einsum("ij,wjo->wio", before, hits, preferred_element_type=jnp.float32)
    position = jnp.sum(earlier * hits.astype(jnp.float32), axis=-1).astype(jnp.int32)
    return jnp.where(slots >= 0, owner_of * capacity + position, slab_count * capacity)


QUERY_BLOCK = 256


def attention_kernel(lanes_ref, g_ref, out_ref, k_s, v_s, dk_acc, dv_acc):
    step = pl.program_id(1)
    owners, _, slots, _ = lanes_ref.shape
    per_block = g_ref.shape[0]
    length = owners * slots
    block = per_block * slots
    factor = HD ** (-0.5)

    @pl.when(step == 0)
    def _():
        k_s[...] = lanes_ref[:, 0, :, HD : 2 * HD].reshape(length, HD)
        v_s[...] = lanes_ref[:, 0, :, 2 * HD : 3 * HD].reshape(length, HD)
        dk_acc[...] = jnp.zeros_like(dk_acc)
        dv_acc[...] = jnp.zeros_like(dv_acc)

    first = pl.multiple_of(step * per_block, per_block)
    queries = lanes_ref[pl.ds(first, per_block), 0, :, 0:HD].reshape(block, HD)
    upstream = g_ref[:, 0, :, :].reshape(block, HD)
    key_rows = k_s[...]
    value_rows = v_s[...]
    scores = contract(queries, key_rows, 1, 1) * factor
    raised = jnp.exp(scores - jnp.max(scores, axis=1, keepdims=True))
    attention = raised / jnp.sum(raised, axis=1, keepdims=True)
    d_attention = contract(upstream, value_rows, 1, 1)
    inner_sum = jnp.sum(attention * d_attention, axis=1, keepdims=True)
    d_scores = (attention * (d_attention - inner_sum) * factor).astype(jnp.bfloat16)
    grad_query = contract(d_scores, key_rows, 1, 0).astype(jnp.bfloat16)
    out_ref[pl.ds(first, per_block), 0, :, 0:HD] = grad_query.reshape(per_block, slots, HD)
    dk_acc[...] += contract(d_scores, queries, 0, 0)
    dv_acc[...] += contract(attention.astype(jnp.bfloat16), upstream, 0, 0)

    @pl.when(step == pl.num_programs(1) - 1)
    def _():
        out_ref[:, 0, :, HD : 2 * HD] = dk_acc[...].astype(jnp.bfloat16).reshape(owners, slots, HD)
        out_ref[:, 0, :, 2 * HD : 3 * HD] = dv_acc[...].astype(jnp.bfloat16).reshape(owners, slots, HD)


def attention_grads(lanes, upstream):
    owners, windows, slots, width = lanes.shape
    length = owners * slots
    per_block = max(1, QUERY_BLOCK // slots)
    lanes_spec = pl.BlockSpec((owners, 1, slots, width), lambda w, i: (0, w, 0, 0))
    g_spec = pl.BlockSpec((per_block, 1, slots, HD), lambda w, i: (i, w, 0, 0))
    flops = 10 * windows * length * length * HD
    return pl.pallas_call(
        attention_kernel,
        grid=(windows, owners // per_block),
        in_specs=[lanes_spec, g_spec],
        out_specs=lanes_spec,
        out_shape=jax.ShapeDtypeStruct(lanes.shape, jnp.bfloat16),
        scratch_shapes=[
            pltpu.VMEM((length, HD), jnp.bfloat16),
            pltpu.VMEM((length, HD), jnp.bfloat16),
            pltpu.VMEM((length, HD), jnp.float32),
            pltpu.VMEM((length, HD), jnp.float32),
        ],
        compiler_params=pltpu.CompilerParams(
            dimension_semantics=("arbitrary", "arbitrary"),
            vmem_limit_bytes=48 * 1024 * 1024,
        ),
        cost_estimate=pl.CostEstimate(
            flops=flops,
            transcendentals=windows * length * length,
            bytes_accessed=7 * windows * length * HD * 2,
        ),
    )(lanes, upstream)


def body(voxels, brain_list, owner_slot, embed_weight, qkv_weight, cotangent):
    slab_count = lax.axis_size("space")
    tm_count = lax.axis_size("tm")
    capacity = 3 * OWN // (2 * slab_count)
    buckets = slab_count * capacity
    windows = voxels.shape[0]
    row_total = windows * OWN
    side_y = GY // 6
    side_z = GZ // 6
    frames = voxels.shape[1]
    depth = voxels.shape[2]
    lanes_b = -(-buckets // 128) * 128
    my_buckets = bucket_index(owner_slot, slab_count, capacity)
    to_bucket = (
        my_buckets[:, None, :] == jnp.arange(lanes_b, dtype=jnp.int32)[None, :, None]
    ).astype(jnp.bfloat16)
    slot_code = (jnp.where(owner_slot >= 0, owner_slot % OWN, -1) + 1).astype(jnp.bfloat16)
    bucket_code = select(to_bucket, slot_code[:, :, None])[:, :buckets]
    patch_code = select(to_bucket, (brain_list + 1).astype(jnp.float32)[:, :, None].astype(jnp.bfloat16))
    patch_of = patch_code[:, :, 0].astype(jnp.int32) - 1
    py_of = jnp.where(patch_of >= 0, patch_of // side_z, -1)
    pz_of = jnp.where(patch_of >= 0, patch_of % side_z, -1)
    z_index = jnp.arange(GZ, dtype=jnp.int32)
    inner = jnp.arange(6, dtype=jnp.int32)
    pick_z = (
        z_index[None, :, None, None]
        == pz_of[:, None, None, :] * 6 + inner[None, None, :, None]
    ).astype(jnp.bfloat16).reshape(windows, GZ, 6 * lanes_b)
    rows = voxels.reshape(windows, frames * depth * GY, GZ)
    by_z = jnp.einsum("wrz,wzk->wrk", rows, pick_z, preferred_element_type=jnp.float32)
    by_z = by_z.astype(jnp.bfloat16).reshape(windows, frames * depth, GY, 6, lanes_b)
    y_index = jnp.arange(GY, dtype=jnp.int32)
    keep_y = (y_index[None, :, None] // 6 == py_of[:, None, :]).astype(jnp.bfloat16)
    masked = by_z * keep_y[:, None, :, None, :]
    fold_y = (y_index[None, :] % 6 == inner[:, None]).astype(jnp.bfloat16)
    by_y = jnp.einsum("iy,wfyjb->wifjb", fold_y, masked, preferred_element_type=jnp.float32)
    columns = by_y.astype(jnp.bfloat16).reshape(windows, PATCH, lanes_b)
    width = -(-(PATCH + 1) // 128) * 128
    payload = jnp.concatenate(
        [
            jnp.swapaxes(columns, 1, 2)[:, :buckets],
            bucket_code.astype(jnp.bfloat16),
            jnp.zeros((windows, buckets, width - PATCH - 1), jnp.bfloat16),
        ],
        axis=2,
    ).reshape(windows, slab_count, capacity, width)
    arrived = lax.all_to_all(payload, "space", split_axis=1, concat_axis=1, tiled=True).reshape(
        windows, buckets, width
    )
    arrival_slot = arrived[:, :, PATCH].astype(jnp.int32) - 1
    to_slot = (
        arrival_slot[:, None, :] == jnp.arange(OWN, dtype=jnp.int32)[None, :, None]
    ).astype(jnp.bfloat16)
    chosen = select(to_slot, arrived[:, :, :PATCH]).astype(jnp.bfloat16).reshape(row_total, PATCH)
    full_embed = (
        lax.all_gather(embed_weight, "tm", axis=1, tiled=True)
        .reshape(4, 6, 6, 6, D)
        .transpose(2, 0, 1, 3, 4)
        .reshape(PATCH, D)
    )
    tokens = jnp.dot(chosen, full_embed, preferred_element_type=jnp.float32).astype(jnp.bfloat16)
    widened = tokens.astype(jnp.float32)
    center = widened - jnp.mean(widened, axis=1, keepdims=True)
    inverse = lax.rsqrt(jnp.mean(center * center, axis=1, keepdims=True) + 1e-05)
    normed = center * inverse
    hidden = normed.astype(jnp.bfloat16)
    wide_rows = lax.all_gather(qkv_weight, "tm", axis=1, tiled=True)
    full_qkv = lax.all_gather(wide_rows, "space", axis=0, tiled=True)
    heads = D // HD
    head_qkv = full_qkv.reshape(D, 3, heads, HD).transpose(0, 2, 1, 3).reshape(D, 3 * D)
    packed = jnp.dot(hidden, head_qkv, preferred_element_type=jnp.float32).astype(jnp.bfloat16)
    lanes_out = packed.reshape(windows, OWN, heads, 3 * HD).transpose(2, 0, 1, 3)
    upstream_out = cotangent.reshape(windows, OWN, heads, HD).transpose(2, 0, 1, 3)
    lanes = lax.all_to_all(lanes_out, "space", split_axis=0, concat_axis=0, tiled=True)
    upstream = lax.all_to_all(upstream_out, "space", split_axis=0, concat_axis=0, tiled=True)
    grads = attention_grads(lanes, upstream)
    returned = lax.all_to_all(grads, "space", split_axis=0, concat_axis=0, tiled=True)
    d_packed = (
        returned.reshape(heads, windows, OWN, 3, HD)
        .transpose(1, 2, 3, 0, 4)
        .reshape(row_total, 3 * D)
    )
    my_rows = lax.psum_scatter(
        contract(hidden, d_packed, 0, 0).astype(jnp.bfloat16),
        "space",
        scatter_dimension=0,
        tiled=True,
    )
    row_block = my_rows.shape[0]
    col_block = 3 * D // tm_count
    qkv_parts = lax.all_to_all(
        my_rows.reshape(row_block, tm_count, col_block).transpose(1, 0, 2),
        "tm",
        split_axis=0,
        concat_axis=0,
        tiled=True,
    )
    d_qkv_weight = jnp.sum(qkv_parts.astype(jnp.float32), axis=0)
    d_hidden = contract(d_packed, full_qkv, 1, 1)
    first_mean = jnp.mean(d_hidden, axis=1, keepdims=True)
    second_mean = jnp.mean(d_hidden * normed, axis=1, keepdims=True)
    d_tokens = (inverse * (d_hidden - first_mean - normed * second_mean)).astype(jnp.bfloat16)
    embed_partial = contract(chosen, d_tokens, 0, 0)
    embed_block = D // tm_count
    embed_parts = lax.all_to_all(
        embed_partial.astype(jnp.bfloat16).reshape(PATCH, tm_count, embed_block).transpose(1, 0, 2),
        "tm",
        split_axis=0,
        concat_axis=0,
        tiled=True,
    )
    embed_cols = jnp.sum(embed_parts.astype(jnp.float32), axis=0)
    chunk = -(-PATCH // slab_count)
    padded = jnp.pad(embed_cols, ((0, chunk * slab_count - PATCH), (0, 0)))
    spread = lax.all_to_all(
        padded.reshape(slab_count, chunk, -1), "space", split_axis=0, concat_axis=0, tiled=True
    )
    reduced = jnp.sum(spread, axis=0)
    gathered = lax.all_to_all(
        jnp.broadcast_to(reduced[None], (slab_count,) + reduced.shape),
        "space",
        split_axis=0,
        concat_axis=0,
        tiled=True,
    )
    d_embed_weight = (
        gathered.reshape(chunk * slab_count, -1)[:PATCH]
        .reshape(6, 4, 6, 6, -1)
        .transpose(1, 2, 0, 3, 4)
        .reshape(PATCH, -1)
    )
    return (d_qkv_weight, d_embed_weight)


def solution(mesh):
    placed = (
        P(None, "tm", "space", None),
        P(None, "space"),
        P(None, "space"),
        P(None, "tm"),
        P("space", "tm"),
        P(None, "tm", "space", None),
    )
    return jax.shard_map(
        body,
        mesh=mesh,
        in_specs=placed,
        out_specs=(P("space", "tm"), P(None, "tm")),
        check_vma=False,
    )
```

```python
import jax
import jax.numpy as jnp
from jax import lax
from jax.sharding import PartitionSpec as P
from jax.experimental import pallas as pl
from jax.experimental.pallas import tpu as pltpu

D = 1024
HD = 64
PATCH = 864
GY = 96
GZ = 96
OWN = 128
PSLAB = 256


def for_sending(array):

    def short(part):
        return part.astype(jnp.bfloat16) if part.dtype == jnp.float32 else part

    return jax.tree.map(short, array)


def contract(left, right, left_dim, right_dim):
    return lax.dot_general(
        left, right, (((left_dim,), (right_dim,)), ((), ())), preferred_element_type=jnp.float32
    )


def select(onehot, rows):
    return jnp.einsum("wab,wbc->wac", onehot, rows, preferred_element_type=jnp.float32)


def bucket_index(slots, slab_count, capacity):
    entries = slots.shape[-1]
    owner_of = jnp.where(slots >= 0, slots // OWN, slab_count)
    hits = (owner_of[..., None] == jnp.arange(slab_count, dtype=jnp.int32)).astype(jnp.bfloat16)
    order = jnp.arange(entries, dtype=jnp.int32)
    before = (order[None, :] < order[:, None]).astype(jnp.bfloat16)
    earlier = jnp.einsum("ij,wjo->wio", before, hits, preferred_element_type=jnp.float32)
    position = jnp.sum(earlier * hits.astype(jnp.float32), axis=-1).astype(jnp.int32)
    return jnp.where(slots >= 0, owner_of * capacity + position, slab_count * capacity)


def patch_kernel(rows_ref, pick_ref, keep_ref, fold_ref, out_ref):
    frames = rows_ref.shape[1]
    depth = fold_ref.shape[0] // 6
    lanes_b = out_ref.shape[1]
    span = 6 * fold_ref.shape[0]
    keep = keep_ref[0].astype(jnp.float32)[None]
    for frame in range(frames):
        by_z = jnp.dot(rows_ref[0, frame], pick_ref[0], preferred_element_type=jnp.float32)
        rows_per = by_z.shape[0] // depth
        masked = (by_z.reshape(depth, rows_per, -1) * keep).reshape(depth * rows_per, -1)
        by_y = contract(masked.astype(jnp.bfloat16), fold_ref[...], 0, 1)
        for inner in range(6):
            start = frame * span + inner * fold_ref.shape[0]
            out_ref[0, :, start : start + fold_ref.shape[0]] = by_y[
                inner * lanes_b : (inner + 1) * lanes_b
            ].astype(out_ref.dtype)


def patch_columns(rows, pick_z, keep_y, fold):
    windows = rows.shape[0]
    lanes_b = pick_z.shape[2] // 6
    return pl.pallas_call(
        patch_kernel,
        grid=(windows,),
        in_specs=[
            pl.BlockSpec((1,) + rows.shape[1:], lambda w: (w, 0, 0, 0)),
            pl.BlockSpec((1,) + pick_z.shape[1:], lambda w: (w, 0, 0)),
            pl.BlockSpec((1,) + keep_y.shape[1:], lambda w: (w, 0, 0)),
            pl.BlockSpec(fold.shape, lambda w: (0, 0)),
        ],
        out_specs=pl.BlockSpec((1, lanes_b, PATCH), lambda w: (w, 0, 0)),
        out_shape=jax.ShapeDtypeStruct((windows, lanes_b, PATCH), jnp.bfloat16),
        compiler_params=pltpu.CompilerParams(
            dimension_semantics=("arbitrary",),
            vmem_limit_bytes=48 * 1024 * 1024,
        ),
        cost_estimate=pl.CostEstimate(
            flops=2 * rows.shape[0] * rows.shape[1] * rows.shape[2] * pick_z.shape[1] * pick_z.shape[2] * 2,
            transcendentals=0,
            bytes_accessed=rows.size * 2 + windows * lanes_b * PATCH * 2,
        ),
    )(rows, pick_z, keep_y, fold)


QUERY_BLOCK = 256


def attention_kernel(lanes_ref, g_ref, out_ref, k_s, v_s, dk_acc, dv_acc):
    step = pl.program_id(1)
    owners, _, slots, _ = lanes_ref.shape
    per_block = g_ref.shape[0]
    length = owners * slots
    block = per_block * slots
    factor = HD ** (-0.5)

    @pl.when(step == 0)
    def _():
        k_s[...] = lanes_ref[:, 0, :, HD : 2 * HD].reshape(length, HD)
        v_s[...] = lanes_ref[:, 0, :, 2 * HD : 3 * HD].reshape(length, HD)
        dk_acc[...] = jnp.zeros_like(dk_acc)
        dv_acc[...] = jnp.zeros_like(dv_acc)

    first = pl.multiple_of(step * per_block, per_block)
    queries = lanes_ref[pl.ds(first, per_block), 0, :, 0:HD].reshape(block, HD)
    upstream = g_ref[:, 0, :, :].reshape(block, HD)
    key_rows = k_s[...]
    value_rows = v_s[...]
    scores = contract(queries, key_rows, 1, 1) * factor
    raised = jnp.exp(scores - jnp.max(scores, axis=1, keepdims=True))
    attention = raised / jnp.sum(raised, axis=1, keepdims=True)
    d_attention = contract(upstream, value_rows, 1, 1)
    inner_sum = jnp.sum(attention * d_attention, axis=1, keepdims=True)
    d_scores = (attention * (d_attention - inner_sum) * factor).astype(jnp.bfloat16)
    grad_query = contract(d_scores, key_rows, 1, 0).astype(jnp.bfloat16)
    out_ref[pl.ds(first, per_block), 0, :, 0:HD] = grad_query.reshape(per_block, slots, HD)
    dk_acc[...] += contract(d_scores, queries, 0, 0)
    dv_acc[...] += contract(attention.astype(jnp.bfloat16), upstream, 0, 0)

    @pl.when(step == pl.num_programs(1) - 1)
    def _():
        out_ref[:, 0, :, HD : 2 * HD] = dk_acc[...].astype(jnp.bfloat16).reshape(owners, slots, HD)
        out_ref[:, 0, :, 2 * HD : 3 * HD] = dv_acc[...].astype(jnp.bfloat16).reshape(owners, slots, HD)


def attention_grads(lanes, upstream):
    owners, windows, slots, width = lanes.shape
    length = owners * slots
    per_block = max(1, QUERY_BLOCK // slots)
    lanes_spec = pl.BlockSpec((owners, 1, slots, width), lambda w, i: (0, w, 0, 0))
    g_spec = pl.BlockSpec((per_block, 1, slots, HD), lambda w, i: (i, w, 0, 0))
    flops = 10 * windows * length * length * HD
    return pl.pallas_call(
        attention_kernel,
        grid=(windows, owners // per_block),
        in_specs=[lanes_spec, g_spec],
        out_specs=lanes_spec,
        out_shape=jax.ShapeDtypeStruct(lanes.shape, jnp.bfloat16),
        scratch_shapes=[
            pltpu.VMEM((length, HD), jnp.bfloat16),
            pltpu.VMEM((length, HD), jnp.bfloat16),
            pltpu.VMEM((length, HD), jnp.float32),
            pltpu.VMEM((length, HD), jnp.float32),
        ],
        compiler_params=pltpu.CompilerParams(
            dimension_semantics=("arbitrary", "arbitrary"),
            vmem_limit_bytes=48 * 1024 * 1024,
        ),
        cost_estimate=pl.CostEstimate(
            flops=flops,
            transcendentals=windows * length * length,
            bytes_accessed=7 * windows * length * HD * 2,
        ),
    )(lanes, upstream)


def body(voxels, brain_list, owner_slot, embed_weight, qkv_weight, cotangent):
    slab_count = lax.axis_size("space")
    tm_count = lax.axis_size("tm")
    capacity = 3 * OWN // (2 * slab_count)
    buckets = slab_count * capacity
    windows = voxels.shape[0]
    row_total = windows * OWN
    side_y = GY // 6
    side_z = GZ // 6
    frames = voxels.shape[1]
    depth = voxels.shape[2]
    lanes_b = -(-buckets // 128) * 128
    my_buckets = bucket_index(owner_slot, slab_count, capacity)
    to_bucket = (
        my_buckets[:, None, :] == jnp.arange(lanes_b, dtype=jnp.int32)[None, :, None]
    ).astype(jnp.bfloat16)
    slot_code = (jnp.where(owner_slot >= 0, owner_slot % OWN, -1) + 1).astype(jnp.bfloat16)
    bucket_code = select(to_bucket, slot_code[:, :, None])[:, :buckets]
    patch_code = select(to_bucket, (brain_list + 1).astype(jnp.float32)[:, :, None].astype(jnp.bfloat16))
    patch_of = patch_code[:, :, 0].astype(jnp.int32) - 1
    py_of = jnp.where(patch_of >= 0, patch_of // side_z, -1)
    pz_of = jnp.where(patch_of >= 0, patch_of % side_z, -1)
    z_index = jnp.arange(GZ, dtype=jnp.int32)
    inner = jnp.arange(6, dtype=jnp.int32)
    pick_z = (
        z_index[None, :, None, None]
        == pz_of[:, None, None, :] * 6 + inner[None, None, :, None]
    ).astype(jnp.bfloat16).reshape(windows, GZ, 6 * lanes_b)
    rows = voxels.reshape(windows, frames, depth * GY, GZ)
    y_index = jnp.arange(GY, dtype=jnp.int32)
    keep_y = jnp.broadcast_to(
        (y_index[None, :, None, None] // 6 == py_of[:, None, None, :]),
        (windows, GY, 6, lanes_b),
    ).astype(jnp.bfloat16).reshape(windows, GY, 6 * lanes_b)
    slab_x = jnp.arange(depth, dtype=jnp.int32)
    fold = (
        (slab_x[:, None, None, None] == slab_x[None, None, :, None])
        & (inner[None, :, None, None] == y_index[None, None, None, :] % 6)
    ).astype(jnp.bfloat16).reshape(depth * 6, depth * GY)
    picked = patch_columns(rows, pick_z, keep_y, fold)
    width = -(-(PATCH + 1) // 128) * 128
    payload = jnp.concatenate(
        [
            picked[:, :buckets],
            bucket_code.astype(jnp.bfloat16),
            jnp.zeros((windows, buckets, width - PATCH - 1), jnp.bfloat16),
        ],
        axis=2,
    ).reshape(windows, slab_count, capacity, width)
    arrived = lax.all_to_all(payload, "space", split_axis=1, concat_axis=1, tiled=True).reshape(
        windows, buckets, width
    )
    arrival_slot = arrived[:, :, PATCH].astype(jnp.int32) - 1
    to_slot = (
        arrival_slot[:, None, :] == jnp.arange(OWN, dtype=jnp.int32)[None, :, None]
    ).astype(jnp.bfloat16)
    chosen = select(to_slot, arrived[:, :, :PATCH]).astype(jnp.bfloat16).reshape(row_total, PATCH)
    full_embed = (
        lax.all_gather(embed_weight, "tm", axis=1, tiled=True)
        .reshape(4, 6, 6, 6, D)
        .transpose(0, 3, 1, 2, 4)
        .reshape(PATCH, D)
    )
    tokens = jnp.dot(chosen, full_embed, preferred_element_type=jnp.float32).astype(jnp.bfloat16)
    widened = tokens.astype(jnp.float32)
    center = widened - jnp.mean(widened, axis=1, keepdims=True)
    inverse = lax.rsqrt(jnp.mean(center * center, axis=1, keepdims=True) + 1e-05)
    normed = center * inverse
    hidden = normed.astype(jnp.bfloat16)
    wide_rows = lax.all_gather(qkv_weight, "tm", axis=1, tiled=True)
    full_qkv = lax.all_gather(wide_rows, "space", axis=0, tiled=True)
    heads = D // HD
    head_qkv = full_qkv.reshape(D, 3, heads, HD).transpose(0, 2, 1, 3).reshape(D, 3 * D)
    packed = jnp.dot(hidden, head_qkv, preferred_element_type=jnp.float32).astype(jnp.bfloat16)
    lanes_out = packed.reshape(windows, OWN, heads, 3 * HD).transpose(2, 0, 1, 3)
    upstream_out = cotangent.reshape(windows, OWN, heads, HD).transpose(2, 0, 1, 3)
    lanes = lax.all_to_all(lanes_out, "space", split_axis=0, concat_axis=0, tiled=True)
    upstream = lax.all_to_all(upstream_out, "space", split_axis=0, concat_axis=0, tiled=True)
    grads = attention_grads(lanes, upstream)
    returned = lax.all_to_all(grads, "space", split_axis=0, concat_axis=0, tiled=True)
    d_packed = (
        returned.reshape(heads, windows, OWN, 3, HD)
        .transpose(1, 2, 3, 0, 4)
        .reshape(row_total, 3 * D)
    )
    my_rows = lax.psum_scatter(
        contract(hidden, d_packed, 0, 0).astype(jnp.bfloat16),
        "space",
        scatter_dimension=0,
        tiled=True,
    )
    row_block = my_rows.shape[0]
    col_block = 3 * D // tm_count
    qkv_parts = lax.all_to_all(
        my_rows.reshape(row_block, tm_count, col_block).transpose(1, 0, 2),
        "tm",
        split_axis=0,
        concat_axis=0,
        tiled=True,
    )
    d_qkv_weight = jnp.sum(qkv_parts.astype(jnp.float32), axis=0)
    d_hidden = contract(d_packed, full_qkv, 1, 1)
    first_mean = jnp.mean(d_hidden, axis=1, keepdims=True)
    second_mean = jnp.mean(d_hidden * normed, axis=1, keepdims=True)
    d_tokens = (inverse * (d_hidden - first_mean - normed * second_mean)).astype(jnp.bfloat16)
    embed_partial = contract(chosen, d_tokens, 0, 0)
    embed_block = D // tm_count
    embed_parts = lax.all_to_all(
        embed_partial.astype(jnp.bfloat16).reshape(PATCH, tm_count, embed_block).transpose(1, 0, 2),
        "tm",
        split_axis=0,
        concat_axis=0,
        tiled=True,
    )
    embed_cols = jnp.sum(embed_parts.astype(jnp.float32), axis=0)
    chunk = -(-PATCH // slab_count)
    padded = jnp.pad(embed_cols, ((0, chunk * slab_count - PATCH), (0, 0)))
    spread = lax.all_to_all(
        padded.reshape(slab_count, chunk, -1), "space", split_axis=0, concat_axis=0, tiled=True
    )
    reduced = jnp.sum(spread, axis=0)
    gathered = lax.all_to_all(
        jnp.broadcast_to(reduced[None], (slab_count,) + reduced.shape),
        "space",
        split_axis=0,
        concat_axis=0,
        tiled=True,
    )
    d_embed_weight = (
        gathered.reshape(chunk * slab_count, -1)[:PATCH]
        .reshape(4, 6, 6, 6, -1)
        .transpose(0, 2, 3, 1, 4)
        .reshape(PATCH, -1)
    )
    return (d_qkv_weight, d_embed_weight)


def solution(mesh):
    placed = (
        P(None, "tm", "space", None),
        P(None, "space"),
        P(None, "space"),
        P(None, "tm"),
        P("space", "tm"),
        P(None, "tm", "space", None),
    )
    return jax.shard_map(
        body,
        mesh=mesh,
        in_specs=placed,
        out_specs=(P("space", "tm"), P(None, "tm")),
        check_vma=False,
    )
```

```python
import jax
import jax.numpy as jnp
from jax import lax
from jax.sharding import PartitionSpec as P
from jax.experimental import pallas as pl
from jax.experimental.pallas import tpu as pltpu

D = 1024
HD = 64
PATCH = 864
GY = 96
GZ = 96
OWN = 128
PSLAB = 256


def for_sending(array):

    def short(part):
        return part.astype(jnp.bfloat16) if part.dtype == jnp.float32 else part

    return jax.tree.map(short, array)


def contract(left, right, left_dim, right_dim):
    return lax.dot_general(
        left, right, (((left_dim,), (right_dim,)), ((), ())), preferred_element_type=jnp.float32
    )


def select(onehot, rows):
    return jnp.einsum("wab,wbc->wac", onehot, rows, preferred_element_type=jnp.float32)


def bucket_index(slots, slab_count, capacity):
    entries = slots.shape[-1]
    owner_of = jnp.where(slots >= 0, slots // OWN, slab_count)
    hits = (owner_of[..., None] == jnp.arange(slab_count, dtype=jnp.int32)).astype(jnp.bfloat16)
    order = jnp.arange(entries, dtype=jnp.int32)
    before = (order[None, :] < order[:, None]).astype(jnp.bfloat16)
    earlier = jnp.einsum("ij,wjo->wio", before, hits, preferred_element_type=jnp.float32)
    position = jnp.sum(earlier * hits.astype(jnp.float32), axis=-1).astype(jnp.int32)
    return jnp.where(slots >= 0, owner_of * capacity + position, slab_count * capacity)


def patch_kernel(rows_ref, pick_ref, keep_ref, fold_ref, out_ref):
    frames = rows_ref.shape[1]
    depth = fold_ref.shape[0] // 6
    lanes_b = out_ref.shape[1]
    span = 6 * fold_ref.shape[0]
    keep = keep_ref[0].astype(jnp.float32)[None]
    for frame in range(frames):
        by_z = jnp.dot(rows_ref[0, frame], pick_ref[0], preferred_element_type=jnp.float32)
        rows_per = by_z.shape[0] // depth
        masked = (by_z.reshape(depth, rows_per, -1) * keep).reshape(depth * rows_per, -1)
        by_y = contract(masked.astype(jnp.bfloat16), fold_ref[...], 0, 1)
        for inner in range(6):
            start = frame * span + inner * fold_ref.shape[0]
            out_ref[0, :, start : start + fold_ref.shape[0]] = by_y[
                inner * lanes_b : (inner + 1) * lanes_b
            ].astype(out_ref.dtype)


def patch_columns(rows, pick_z, keep_y, fold):
    windows = rows.shape[0]
    lanes_b = pick_z.shape[2] // 6
    return pl.pallas_call(
        patch_kernel,
        grid=(windows,),
        in_specs=[
            pl.BlockSpec((1,) + rows.shape[1:], lambda w: (w, 0, 0, 0)),
            pl.BlockSpec((1,) + pick_z.shape[1:], lambda w: (w, 0, 0)),
            pl.BlockSpec((1,) + keep_y.shape[1:], lambda w: (w, 0, 0)),
            pl.BlockSpec(fold.shape, lambda w: (0, 0)),
        ],
        out_specs=pl.BlockSpec((1, lanes_b, PATCH), lambda w: (w, 0, 0)),
        out_shape=jax.ShapeDtypeStruct((windows, lanes_b, PATCH), jnp.bfloat16),
        compiler_params=pltpu.CompilerParams(
            dimension_semantics=("arbitrary",),
            vmem_limit_bytes=48 * 1024 * 1024,
        ),
        cost_estimate=pl.CostEstimate(
            flops=2 * rows.shape[0] * rows.shape[1] * rows.shape[2] * pick_z.shape[1] * pick_z.shape[2] * 2,
            transcendentals=0,
            bytes_accessed=rows.size * 2 + windows * lanes_b * PATCH * 2,
        ),
    )(rows, pick_z, keep_y, fold)


QUERY_BLOCK = 256


def attention_kernel(lanes_ref, g_ref, out_ref, k_s, v_s, dk_acc, dv_acc):
    step = pl.program_id(1)
    owners, _, slots, _ = lanes_ref.shape
    per_block = g_ref.shape[0]
    length = owners * slots
    block = per_block * slots
    factor = HD ** (-0.5)

    @pl.when(step == 0)
    def _():
        k_s[...] = lanes_ref[:, 0, :, HD : 2 * HD].reshape(length, HD)
        v_s[...] = lanes_ref[:, 0, :, 2 * HD : 3 * HD].reshape(length, HD)
        dk_acc[...] = jnp.zeros_like(dk_acc)
        dv_acc[...] = jnp.zeros_like(dv_acc)

    first = pl.multiple_of(step * per_block, per_block)
    queries = lanes_ref[pl.ds(first, per_block), 0, :, 0:HD].reshape(block, HD)
    upstream = g_ref[:, 0, :, :].reshape(block, HD)
    key_rows = k_s[...]
    value_rows = v_s[...]
    scores = contract(queries * jnp.asarray(factor, queries.dtype), key_rows, 1, 1)
    raised = jnp.exp(scores - jnp.max(scores, axis=1, keepdims=True))
    attention = raised / jnp.sum(raised, axis=1, keepdims=True)
    d_attention = contract(upstream, value_rows, 1, 1)
    inner_sum = jnp.sum(attention * d_attention, axis=1, keepdims=True)
    d_scores = (attention * (d_attention - inner_sum)).astype(jnp.bfloat16)
    grad_query = contract(d_scores, key_rows, 1, 0) * factor
    out_ref[pl.ds(first, per_block), 0, :, 0:HD] = grad_query.astype(jnp.bfloat16).reshape(
        per_block, slots, HD
    )
    dk_acc[...] += contract(d_scores, queries, 0, 0)
    dv_acc[...] += contract(attention.astype(jnp.bfloat16), upstream, 0, 0)

    @pl.when(step == pl.num_programs(1) - 1)
    def _():
        out_ref[:, 0, :, HD : 2 * HD] = (dk_acc[...] * factor).astype(jnp.bfloat16).reshape(
            owners, slots, HD
        )
        out_ref[:, 0, :, 2 * HD : 3 * HD] = dv_acc[...].astype(jnp.bfloat16).reshape(owners, slots, HD)


def attention_grads(lanes, upstream):
    owners, windows, slots, width = lanes.shape
    length = owners * slots
    per_block = max(1, QUERY_BLOCK // slots)
    lanes_spec = pl.BlockSpec((owners, 1, slots, width), lambda w, i: (0, w, 0, 0))
    g_spec = pl.BlockSpec((per_block, 1, slots, HD), lambda w, i: (i, w, 0, 0))
    flops = 10 * windows * length * length * HD
    return pl.pallas_call(
        attention_kernel,
        grid=(windows, owners // per_block),
        in_specs=[lanes_spec, g_spec],
        out_specs=lanes_spec,
        out_shape=jax.ShapeDtypeStruct(lanes.shape, jnp.bfloat16),
        scratch_shapes=[
            pltpu.VMEM((length, HD), jnp.bfloat16),
            pltpu.VMEM((length, HD), jnp.bfloat16),
            pltpu.VMEM((length, HD), jnp.float32),
            pltpu.VMEM((length, HD), jnp.float32),
        ],
        compiler_params=pltpu.CompilerParams(
            dimension_semantics=("arbitrary", "arbitrary"),
            vmem_limit_bytes=48 * 1024 * 1024,
        ),
        cost_estimate=pl.CostEstimate(
            flops=flops,
            transcendentals=windows * length * length,
            bytes_accessed=7 * windows * length * HD * 2,
        ),
    )(lanes, upstream)


def body(voxels, brain_list, owner_slot, embed_weight, qkv_weight, cotangent):
    slab_count = lax.axis_size("space")
    tm_count = lax.axis_size("tm")
    capacity = 3 * OWN // (2 * slab_count)
    buckets = slab_count * capacity
    windows = voxels.shape[0]
    row_total = windows * OWN
    side_y = GY // 6
    side_z = GZ // 6
    frames = voxels.shape[1]
    depth = voxels.shape[2]
    lanes_b = -(-buckets // 128) * 128
    my_buckets = bucket_index(owner_slot, slab_count, capacity)
    to_bucket = (
        my_buckets[:, None, :] == jnp.arange(lanes_b, dtype=jnp.int32)[None, :, None]
    ).astype(jnp.bfloat16)
    slot_code = (jnp.where(owner_slot >= 0, owner_slot % OWN, -1) + 1).astype(jnp.bfloat16)
    bucket_code = select(to_bucket, slot_code[:, :, None])[:, :buckets]
    patch_code = select(to_bucket, (brain_list + 1).astype(jnp.float32)[:, :, None].astype(jnp.bfloat16))
    patch_of = patch_code[:, :, 0].astype(jnp.int32) - 1
    py_of = jnp.where(patch_of >= 0, patch_of // side_z, -1)
    pz_of = jnp.where(patch_of >= 0, patch_of % side_z, -1)
    z_index = jnp.arange(GZ, dtype=jnp.int32)
    inner = jnp.arange(6, dtype=jnp.int32)
    pick_z = (
        z_index[None, :, None, None]
        == pz_of[:, None, None, :] * 6 + inner[None, None, :, None]
    ).astype(jnp.bfloat16).reshape(windows, GZ, 6 * lanes_b)
    rows = voxels.reshape(windows, frames, depth * GY, GZ)
    y_index = jnp.arange(GY, dtype=jnp.int32)
    keep_y = jnp.broadcast_to(
        (y_index[None, :, None, None] // 6 == py_of[:, None, None, :]),
        (windows, GY, 6, lanes_b),
    ).astype(jnp.bfloat16).reshape(windows, GY, 6 * lanes_b)
    slab_x = jnp.arange(depth, dtype=jnp.int32)
    fold = (
        (slab_x[:, None, None, None] == slab_x[None, None, :, None])
        & (inner[None, :, None, None] == y_index[None, None, None, :] % 6)
    ).astype(jnp.bfloat16).reshape(depth * 6, depth * GY)
    picked = patch_columns(rows, pick_z, keep_y, fold)
    width = -(-(PATCH + 1) // 128) * 128
    payload = jnp.concatenate(
        [
            picked[:, :buckets],
            bucket_code.astype(jnp.bfloat16),
            jnp.zeros((windows, buckets, width - PATCH - 1), jnp.bfloat16),
        ],
        axis=2,
    ).reshape(windows, slab_count, capacity, width)
    arrived = lax.all_to_all(payload, "space", split_axis=1, concat_axis=1, tiled=True).reshape(
        windows, buckets, width
    )
    arrival_slot = arrived[:, :, PATCH].astype(jnp.int32) - 1
    to_slot = (
        arrival_slot[:, None, :] == jnp.arange(OWN, dtype=jnp.int32)[None, :, None]
    ).astype(jnp.bfloat16)
    chosen = select(to_slot, arrived[:, :, :PATCH]).astype(jnp.bfloat16).reshape(row_total, PATCH)
    full_embed = (
        lax.all_gather(embed_weight, "tm", axis=1, tiled=True)
        .reshape(4, 6, 6, 6, D)
        .transpose(0, 3, 1, 2, 4)
        .reshape(PATCH, D)
    )
    tokens = jnp.dot(chosen, full_embed, preferred_element_type=jnp.float32).astype(jnp.bfloat16)
    widened = tokens.astype(jnp.float32)
    center = widened - jnp.mean(widened, axis=1, keepdims=True)
    inverse = lax.rsqrt(jnp.mean(center * center, axis=1, keepdims=True) + 1e-05)
    normed = center * inverse
    hidden = normed.astype(jnp.bfloat16)
    wide_rows = lax.all_gather(qkv_weight, "tm", axis=1, tiled=True)
    full_qkv = lax.all_gather(wide_rows, "space", axis=0, tiled=True)
    heads = D // HD
    head_qkv = full_qkv.reshape(D, 3, heads, HD).transpose(0, 2, 1, 3).reshape(D, 3 * D)
    packed = jnp.dot(hidden, head_qkv, preferred_element_type=jnp.float32).astype(jnp.bfloat16)
    lanes_out = packed.reshape(windows, OWN, heads, 3 * HD).transpose(2, 0, 1, 3)
    upstream_out = cotangent.reshape(windows, OWN, heads, HD).transpose(2, 0, 1, 3)
    lanes = lax.all_to_all(lanes_out, "space", split_axis=0, concat_axis=0, tiled=True)
    upstream = lax.all_to_all(upstream_out, "space", split_axis=0, concat_axis=0, tiled=True)
    grads = attention_grads(lanes, upstream)
    returned = lax.all_to_all(grads, "space", split_axis=0, concat_axis=0, tiled=True)
    d_packed = (
        returned.reshape(heads, windows, OWN, 3, HD)
        .transpose(1, 2, 3, 0, 4)
        .reshape(row_total, 3 * D)
    )
    col_block = 3 * D // tm_count
    parity = lax.axis_index("tm") % 2
    partial = contract(hidden, d_packed, 0, 0).reshape(D, tm_count // 2, 2, col_block)
    kept = jnp.where(parity == 0, partial[:, :, 0], partial[:, :, 1])
    given = jnp.where(parity == 0, partial[:, :, 1], partial[:, :, 0]).astype(jnp.bfloat16)
    partner = [(index, index ^ 1) for index in range(tm_count)]
    pair_sum = (kept + lax.ppermute(given, "tm", partner).astype(jnp.float32)).astype(jnp.bfloat16)
    my_rows = lax.psum_scatter(pair_sum, "space", scatter_dimension=0, tiled=True)
    row_block = my_rows.shape[0]
    side = (jnp.arange(2, dtype=jnp.int32) == parity)[None, :, None, None]
    outgoing = jnp.where(side, my_rows.transpose(1, 0, 2)[:, None], jnp.zeros((), jnp.bfloat16))
    qkv_parts = lax.all_to_all(
        outgoing.reshape(tm_count, row_block, col_block),
        "tm",
        split_axis=0,
        concat_axis=0,
        tiled=True,
    )
    d_qkv_weight = jnp.sum(qkv_parts.astype(jnp.float32), axis=0)
    d_hidden = contract(d_packed, full_qkv, 1, 1)
    first_mean = jnp.mean(d_hidden, axis=1, keepdims=True)
    second_mean = jnp.mean(d_hidden * normed, axis=1, keepdims=True)
    d_tokens = (inverse * (d_hidden - first_mean - normed * second_mean)).astype(jnp.bfloat16)
    embed_partial = contract(chosen, d_tokens, 0, 0)
    embed_block = D // tm_count
    embed_parts = lax.all_to_all(
        embed_partial.astype(jnp.bfloat16).reshape(PATCH, tm_count, embed_block).transpose(1, 0, 2),
        "tm",
        split_axis=0,
        concat_axis=0,
        tiled=True,
    )
    embed_cols = jnp.sum(embed_parts.astype(jnp.float32), axis=0)
    chunk = -(-PATCH // slab_count)
    padded = jnp.pad(embed_cols, ((0, chunk * slab_count - PATCH), (0, 0)))
    spread = lax.all_to_all(
        padded.reshape(slab_count, chunk, -1), "space", split_axis=0, concat_axis=0, tiled=True
    )
    reduced = jnp.sum(spread, axis=0)
    gathered = lax.all_to_all(
        jnp.broadcast_to(reduced[None], (slab_count,) + reduced.shape),
        "space",
        split_axis=0,
        concat_axis=0,
        tiled=True,
    )
    d_embed_weight = (
        gathered.reshape(chunk * slab_count, -1)[:PATCH]
        .reshape(4, 6, 6, 6, -1)
        .transpose(0, 2, 3, 1, 4)
        .reshape(PATCH, -1)
    )
    return (d_qkv_weight, d_embed_weight)


def solution(mesh):
    placed = (
        P(None, "tm", "space", None),
        P(None, "space"),
        P(None, "space"),
        P(None, "tm"),
        P("space", "tm"),
        P(None, "tm", "space", None),
    )
    return jax.shard_map(
        body,
        mesh=mesh,
        in_specs=placed,
        out_specs=(P("space", "tm"), P(None, "tm")),
        check_vma=False,
    )
```

```python
import jax
import jax.numpy as jnp
from jax import lax
from jax.sharding import PartitionSpec as P
from jax.experimental import pallas as pl
from jax.experimental.pallas import tpu as pltpu

D = 1024
HD = 64
PATCH = 864
GY = 96
GZ = 96
OWN = 128
PSLAB = 256


def for_sending(array):

    def short(part):
        return part.astype(jnp.bfloat16) if part.dtype == jnp.float32 else part

    return jax.tree.map(short, array)


def contract(left, right, left_dim, right_dim):
    return lax.dot_general(
        left, right, (((left_dim,), (right_dim,)), ((), ())), preferred_element_type=jnp.float32
    )


def select(onehot, rows):
    return jnp.einsum("wab,wbc->wac", onehot, rows, preferred_element_type=jnp.float32)


def bucket_index(slots, slab_count, capacity):
    entries = slots.shape[-1]
    owner_of = jnp.where(slots >= 0, slots // OWN, slab_count)
    hits = (owner_of[..., None] == jnp.arange(slab_count, dtype=jnp.int32)).astype(jnp.bfloat16)
    order = jnp.arange(entries, dtype=jnp.int32)
    before = (order[None, :] < order[:, None]).astype(jnp.bfloat16)
    earlier = jnp.einsum("ij,wjo->wio", before, hits, preferred_element_type=jnp.float32)
    position = jnp.sum(earlier * hits.astype(jnp.float32), axis=-1).astype(jnp.int32)
    return jnp.where(slots >= 0, owner_of * capacity + position, slab_count * capacity)


def patch_kernel(rows_ref, pick_ref, keep_ref, fold_ref, out_ref):
    frames = rows_ref.shape[1]
    depth = fold_ref.shape[0] // 6
    lanes_b = out_ref.shape[1]
    span = 6 * fold_ref.shape[0]
    keep = keep_ref[0].astype(jnp.float32)[None]
    for frame in range(frames):
        by_z = jnp.dot(rows_ref[0, frame], pick_ref[0], preferred_element_type=jnp.float32)
        rows_per = by_z.shape[0] // depth
        masked = (by_z.reshape(depth, rows_per, -1) * keep).reshape(depth * rows_per, -1)
        by_y = contract(masked.astype(jnp.bfloat16), fold_ref[...], 0, 1)
        for inner in range(6):
            start = frame * span + inner * fold_ref.shape[0]
            out_ref[0, :, start : start + fold_ref.shape[0]] = by_y[
                inner * lanes_b : (inner + 1) * lanes_b
            ].astype(out_ref.dtype)


def patch_columns(rows, pick_z, keep_y, fold):
    windows = rows.shape[0]
    lanes_b = pick_z.shape[2] // 6
    return pl.pallas_call(
        patch_kernel,
        grid=(windows,),
        in_specs=[
            pl.BlockSpec((1,) + rows.shape[1:], lambda w: (w, 0, 0, 0)),
            pl.BlockSpec((1,) + pick_z.shape[1:], lambda w: (w, 0, 0)),
            pl.BlockSpec((1,) + keep_y.shape[1:], lambda w: (w, 0, 0)),
            pl.BlockSpec(fold.shape, lambda w: (0, 0)),
        ],
        out_specs=pl.BlockSpec((1, lanes_b, PATCH), lambda w: (w, 0, 0)),
        out_shape=jax.ShapeDtypeStruct((windows, lanes_b, PATCH), jnp.bfloat16),
        compiler_params=pltpu.CompilerParams(
            dimension_semantics=("arbitrary",),
            vmem_limit_bytes=48 * 1024 * 1024,
        ),
        cost_estimate=pl.CostEstimate(
            flops=2 * rows.shape[0] * rows.shape[1] * rows.shape[2] * pick_z.shape[1] * pick_z.shape[2] * 2,
            transcendentals=0,
            bytes_accessed=rows.size * 2 + windows * lanes_b * PATCH * 2,
        ),
    )(rows, pick_z, keep_y, fold)


def halving_sum(array, steps):
    for axis_name, count, bit, axis in steps:
        index = lax.axis_index(axis_name)
        side = (index >> bit) & 1
        keep = jnp.squeeze(lax.dynamic_slice_in_dim(array, side, 1, axis=axis), axis)
        send = jnp.squeeze(lax.dynamic_slice_in_dim(array, 1 - side, 1, axis=axis), axis)
        partner = [(i, i ^ (1 << bit)) for i in range(count)]
        array = keep + lax.ppermute(send.astype(jnp.bfloat16), axis_name, partner).astype(jnp.float32)
    return array


def bits_of(count):
    return count.bit_length() - 1


QUERY_BLOCK = 256


def attention_kernel(lanes_ref, g_ref, out_ref, k_s, v_s, dk_acc, dv_acc):
    step = pl.program_id(1)
    owners, _, slots, _ = lanes_ref.shape
    per_block = g_ref.shape[0]
    length = owners * slots
    block = per_block * slots
    factor = HD ** (-0.5)

    @pl.when(step == 0)
    def _():
        k_s[...] = lanes_ref[:, 0, :, HD : 2 * HD].reshape(length, HD)
        v_s[...] = lanes_ref[:, 0, :, 2 * HD : 3 * HD].reshape(length, HD)
        dk_acc[...] = jnp.zeros_like(dk_acc)
        dv_acc[...] = jnp.zeros_like(dv_acc)

    first = pl.multiple_of(step * per_block, per_block)
    queries = lanes_ref[pl.ds(first, per_block), 0, :, 0:HD].reshape(block, HD)
    upstream = g_ref[:, 0, :, :].reshape(block, HD)
    key_rows = k_s[...]
    value_rows = v_s[...]
    scores = contract(queries * jnp.asarray(factor, queries.dtype), key_rows, 1, 1)
    raised = jnp.exp(scores - jnp.max(scores, axis=1, keepdims=True))
    attention = raised / jnp.sum(raised, axis=1, keepdims=True)
    d_attention = contract(upstream, value_rows, 1, 1)
    inner_sum = jnp.sum(attention * d_attention, axis=1, keepdims=True)
    d_scores = (attention * (d_attention - inner_sum)).astype(jnp.bfloat16)
    grad_query = contract(d_scores, key_rows, 1, 0) * factor
    out_ref[pl.ds(first, per_block), 0, :, 0:HD] = grad_query.astype(jnp.bfloat16).reshape(
        per_block, slots, HD
    )
    dk_acc[...] += contract(d_scores, queries, 0, 0)
    dv_acc[...] += contract(attention.astype(jnp.bfloat16), upstream, 0, 0)

    @pl.when(step == pl.num_programs(1) - 1)
    def _():
        out_ref[:, 0, :, HD : 2 * HD] = (dk_acc[...] * factor).astype(jnp.bfloat16).reshape(
            owners, slots, HD
        )
        out_ref[:, 0, :, 2 * HD : 3 * HD] = dv_acc[...].astype(jnp.bfloat16).reshape(owners, slots, HD)


def attention_grads(lanes, upstream):
    owners, windows, slots, width = lanes.shape
    length = owners * slots
    per_block = max(1, QUERY_BLOCK // slots)
    lanes_spec = pl.BlockSpec((owners, 1, slots, width), lambda w, i: (0, w, 0, 0))
    g_spec = pl.BlockSpec((per_block, 1, slots, HD), lambda w, i: (i, w, 0, 0))
    flops = 10 * windows * length * length * HD
    return pl.pallas_call(
        attention_kernel,
        grid=(windows, owners // per_block),
        in_specs=[lanes_spec, g_spec],
        out_specs=lanes_spec,
        out_shape=jax.ShapeDtypeStruct(lanes.shape, jnp.bfloat16),
        scratch_shapes=[
            pltpu.VMEM((length, HD), jnp.bfloat16),
            pltpu.VMEM((length, HD), jnp.bfloat16),
            pltpu.VMEM((length, HD), jnp.float32),
            pltpu.VMEM((length, HD), jnp.float32),
        ],
        compiler_params=pltpu.CompilerParams(
            dimension_semantics=("arbitrary", "arbitrary"),
            vmem_limit_bytes=48 * 1024 * 1024,
        ),
        cost_estimate=pl.CostEstimate(
            flops=flops,
            transcendentals=windows * length * length,
            bytes_accessed=7 * windows * length * HD * 2,
        ),
    )(lanes, upstream)


def body(voxels, brain_list, owner_slot, embed_weight, qkv_weight, cotangent):
    slab_count = lax.axis_size("space")
    tm_count = lax.axis_size("tm")
    capacity = 3 * OWN // (2 * slab_count)
    buckets = slab_count * capacity
    windows = voxels.shape[0]
    row_total = windows * OWN
    side_y = GY // 6
    side_z = GZ // 6
    frames = voxels.shape[1]
    depth = voxels.shape[2]
    lanes_b = -(-buckets // 128) * 128
    my_buckets = bucket_index(owner_slot, slab_count, capacity)
    to_bucket = (
        my_buckets[:, None, :] == jnp.arange(lanes_b, dtype=jnp.int32)[None, :, None]
    ).astype(jnp.bfloat16)
    slot_code = (jnp.where(owner_slot >= 0, owner_slot % OWN, -1) + 1).astype(jnp.bfloat16)
    bucket_code = select(to_bucket, slot_code[:, :, None])[:, :buckets]
    patch_code = select(to_bucket, (brain_list + 1).astype(jnp.float32)[:, :, None].astype(jnp.bfloat16))
    patch_of = patch_code[:, :, 0].astype(jnp.int32) - 1
    py_of = jnp.where(patch_of >= 0, patch_of // side_z, -1)
    pz_of = jnp.where(patch_of >= 0, patch_of % side_z, -1)
    z_index = jnp.arange(GZ, dtype=jnp.int32)
    inner = jnp.arange(6, dtype=jnp.int32)
    pick_z = (
        z_index[None, :, None, None]
        == pz_of[:, None, None, :] * 6 + inner[None, None, :, None]
    ).astype(jnp.bfloat16).reshape(windows, GZ, 6 * lanes_b)
    rows = voxels.reshape(windows, frames, depth * GY, GZ)
    y_index = jnp.arange(GY, dtype=jnp.int32)
    keep_y = jnp.broadcast_to(
        (y_index[None, :, None, None] // 6 == py_of[:, None, None, :]),
        (windows, GY, 6, lanes_b),
    ).astype(jnp.bfloat16).reshape(windows, GY, 6 * lanes_b)
    slab_x = jnp.arange(depth, dtype=jnp.int32)
    fold = (
        (slab_x[:, None, None, None] == slab_x[None, None, :, None])
        & (inner[None, :, None, None] == y_index[None, None, None, :] % 6)
    ).astype(jnp.bfloat16).reshape(depth * 6, depth * GY)
    picked = patch_columns(rows, pick_z, keep_y, fold)
    width = -(-(PATCH + 1) // 128) * 128
    payload = jnp.concatenate(
        [
            picked[:, :buckets],
            bucket_code.astype(jnp.bfloat16),
            jnp.zeros((windows, buckets, width - PATCH - 1), jnp.bfloat16),
        ],
        axis=2,
    ).reshape(windows, slab_count, capacity, width)
    arrived = lax.all_to_all(payload, "space", split_axis=1, concat_axis=1, tiled=True).reshape(
        windows, buckets, width
    )
    arrival_slot = arrived[:, :, PATCH].astype(jnp.int32) - 1
    to_slot = (
        arrival_slot[:, None, :] == jnp.arange(OWN, dtype=jnp.int32)[None, :, None]
    ).astype(jnp.bfloat16)
    chosen = select(to_slot, arrived[:, :, :PATCH]).astype(jnp.bfloat16).reshape(row_total, PATCH)
    full_embed = (
        lax.all_gather(embed_weight, "tm", axis=1, tiled=True)
        .reshape(4, 6, 6, 6, D)
        .transpose(0, 3, 1, 2, 4)
        .reshape(PATCH, D)
    )
    tokens = jnp.dot(chosen, full_embed, preferred_element_type=jnp.float32).astype(jnp.bfloat16)
    widened = tokens.astype(jnp.float32)
    center = widened - jnp.mean(widened, axis=1, keepdims=True)
    inverse = lax.rsqrt(jnp.mean(center * center, axis=1, keepdims=True) + 1e-05)
    normed = center * inverse
    hidden = normed.astype(jnp.bfloat16)
    wide_rows = lax.all_gather(qkv_weight, "tm", axis=1, tiled=True)
    full_qkv = lax.all_gather(wide_rows, "space", axis=0, tiled=True)
    heads = D // HD
    head_qkv = full_qkv.reshape(D, 3, heads, HD).transpose(0, 2, 1, 3).reshape(D, 3 * D)
    packed = jnp.dot(hidden, head_qkv, preferred_element_type=jnp.float32).astype(jnp.bfloat16)
    lanes_out = packed.reshape(windows, OWN, heads, 3 * HD).transpose(2, 0, 1, 3)
    upstream_out = cotangent.reshape(windows, OWN, heads, HD).transpose(2, 0, 1, 3)
    lanes = lax.all_to_all(lanes_out, "space", split_axis=0, concat_axis=0, tiled=True)
    upstream = lax.all_to_all(upstream_out, "space", split_axis=0, concat_axis=0, tiled=True)
    grads = attention_grads(lanes, upstream)
    returned = lax.all_to_all(grads, "space", split_axis=0, concat_axis=0, tiled=True)
    d_packed = (
        returned.reshape(heads, windows, OWN, 3, HD)
        .transpose(1, 2, 3, 0, 4)
        .reshape(row_total, 3 * D)
    )
    space_bits = bits_of(slab_count)
    tm_bits = bits_of(tm_count)
    assert (1 << space_bits) == slab_count and (1 << tm_bits) == tm_count
    partial = contract(hidden, d_packed, 0, 0).reshape(
        (2,) * space_bits + (D // slab_count,) + (2,) * tm_bits + (3 * D // tm_count,)
    )

    def space_axis(bit):
        return space_bits - 1 - bit

    def tm_axis(bit):
        return space_bits + 1 + tm_bits - 1 - bit

    order = [("tm", 0)] + [("space", b) for b in range(space_bits - 2, -1, -2)]
    order += [("tm", b) for b in range(1, tm_bits - 1)]
    order += [("space", b) for b in range(space_bits - 1, -1, -2)]
    order += [("tm", b) for b in range(max(1, tm_bits - 1), tm_bits)]
    steps = []
    removed = []
    for name, bit in order:
        axis = space_axis(bit) if name == "space" else tm_axis(bit)
        shift = sum(1 for done in removed if done < axis)
        steps.append((name, slab_count if name == "space" else tm_count, bit, axis - shift))
        removed.append(axis)
    d_qkv_weight = halving_sum(partial, steps)
    d_hidden = contract(d_packed, full_qkv, 1, 1)
    first_mean = jnp.mean(d_hidden, axis=1, keepdims=True)
    second_mean = jnp.mean(d_hidden * normed, axis=1, keepdims=True)
    d_tokens = (inverse * (d_hidden - first_mean - normed * second_mean)).astype(jnp.bfloat16)
    embed_partial = contract(chosen, d_tokens, 0, 0)
    embed_partial = embed_partial.reshape((PATCH,) + (2,) * tm_bits + (D // tm_count,))
    embed_steps = []
    for bit in range(tm_bits):
        embed_steps.append(("tm", tm_count, bit, tm_bits - bit))
    embed_cols = halving_sum(embed_partial, embed_steps)
    chunk = -(-PATCH // slab_count)
    padded = jnp.pad(embed_cols, ((0, chunk * slab_count - PATCH), (0, 0)))
    spread = lax.all_to_all(
        padded.reshape(slab_count, chunk, -1), "space", split_axis=0, concat_axis=0, tiled=True
    )
    reduced = jnp.sum(spread, axis=0)
    gathered = lax.all_to_all(
        jnp.broadcast_to(reduced[None], (slab_count,) + reduced.shape),
        "space",
        split_axis=0,
        concat_axis=0,
        tiled=True,
    )
    d_embed_weight = (
        gathered.reshape(chunk * slab_count, -1)[:PATCH]
        .reshape(4, 6, 6, 6, -1)
        .transpose(0, 2, 3, 1, 4)
        .reshape(PATCH, -1)
    )
    return (d_qkv_weight, d_embed_weight)


def solution(mesh):
    placed = (
        P(None, "tm", "space", None),
        P(None, "space"),
        P(None, "space"),
        P(None, "tm"),
        P("space", "tm"),
        P(None, "tm", "space", None),
    )
    return jax.shard_map(
        body,
        mesh=mesh,
        in_specs=placed,
        out_specs=(P("space", "tm"), P(None, "tm")),
        check_vma=False,
    )
```

```python
import jax
import jax.numpy as jnp
from jax import lax
from jax.sharding import PartitionSpec as P
from jax.experimental import pallas as pl
from jax.experimental.pallas import tpu as pltpu

D = 1024
HD = 64
PATCH = 864
GY = 96
GZ = 96
OWN = 128
PSLAB = 256


def for_sending(array):

    def short(part):
        return part.astype(jnp.bfloat16) if part.dtype == jnp.float32 else part

    return jax.tree.map(short, array)


def contract(left, right, left_dim, right_dim):
    return lax.dot_general(
        left, right, (((left_dim,), (right_dim,)), ((), ())), preferred_element_type=jnp.float32
    )


def select(onehot, rows):
    return jnp.einsum("wab,wbc->wac", onehot, rows, preferred_element_type=jnp.float32)


def bucket_index(slots, slab_count, capacity):
    entries = slots.shape[-1]
    owner_of = jnp.where(slots >= 0, slots // OWN, slab_count)
    hits = (owner_of[..., None] == jnp.arange(slab_count, dtype=jnp.int32)).astype(jnp.bfloat16)
    order = jnp.arange(entries, dtype=jnp.int32)
    before = (order[None, :] < order[:, None]).astype(jnp.bfloat16)
    earlier = jnp.einsum("ij,wjo->wio", before, hits, preferred_element_type=jnp.float32)
    position = jnp.sum(earlier * hits.astype(jnp.float32), axis=-1).astype(jnp.int32)
    return jnp.where(slots >= 0, owner_of * capacity + position, slab_count * capacity)


def patch_kernel(rows_ref, pick_ref, keep_ref, fold_ref, out_ref):
    frames = rows_ref.shape[1]
    depth = fold_ref.shape[0] // 6
    lanes_b = out_ref.shape[1]
    span = 6 * fold_ref.shape[0]
    keep = keep_ref[0].astype(jnp.float32)[None]
    for frame in range(frames):
        by_z = jnp.dot(rows_ref[0, frame], pick_ref[0], preferred_element_type=jnp.float32)
        rows_per = by_z.shape[0] // depth
        masked = (by_z.reshape(depth, rows_per, -1) * keep).reshape(depth * rows_per, -1)
        by_y = contract(masked.astype(jnp.bfloat16), fold_ref[...], 0, 1)
        for inner in range(6):
            start = frame * span + inner * fold_ref.shape[0]
            out_ref[0, :, start : start + fold_ref.shape[0]] = by_y[
                inner * lanes_b : (inner + 1) * lanes_b
            ].astype(out_ref.dtype)


def patch_columns(rows, pick_z, keep_y, fold):
    windows = rows.shape[0]
    lanes_b = pick_z.shape[2] // 6
    return pl.pallas_call(
        patch_kernel,
        grid=(windows,),
        in_specs=[
            pl.BlockSpec((1,) + rows.shape[1:], lambda w: (w, 0, 0, 0)),
            pl.BlockSpec((1,) + pick_z.shape[1:], lambda w: (w, 0, 0)),
            pl.BlockSpec((1,) + keep_y.shape[1:], lambda w: (w, 0, 0)),
            pl.BlockSpec(fold.shape, lambda w: (0, 0)),
        ],
        out_specs=pl.BlockSpec((1, lanes_b, PATCH), lambda w: (w, 0, 0)),
        out_shape=jax.ShapeDtypeStruct((windows, lanes_b, PATCH), jnp.bfloat16),
        compiler_params=pltpu.CompilerParams(
            dimension_semantics=("arbitrary",),
            vmem_limit_bytes=48 * 1024 * 1024,
        ),
        cost_estimate=pl.CostEstimate(
            flops=2 * rows.shape[0] * rows.shape[1] * rows.shape[2] * pick_z.shape[1] * pick_z.shape[2] * 2,
            transcendentals=0,
            bytes_accessed=rows.size * 2 + windows * lanes_b * PATCH * 2,
        ),
    )(rows, pick_z, keep_y, fold)


QUERY_BLOCK = 256


def attention_kernel(lanes_ref, g_ref, out_ref, k_s, v_s, dk_acc, dv_acc):
    step = pl.program_id(1)
    owners, _, slots, _ = lanes_ref.shape
    per_block = g_ref.shape[0]
    length = owners * slots
    block = per_block * slots
    factor = HD ** (-0.5)

    @pl.when(step == 0)
    def _():
        k_s[...] = lanes_ref[:, 0, :, HD : 2 * HD].reshape(length, HD)
        v_s[...] = lanes_ref[:, 0, :, 2 * HD : 3 * HD].reshape(length, HD)
        dk_acc[...] = jnp.zeros_like(dk_acc)
        dv_acc[...] = jnp.zeros_like(dv_acc)

    first = pl.multiple_of(step * per_block, per_block)
    queries = lanes_ref[pl.ds(first, per_block), 0, :, 0:HD].reshape(block, HD)
    upstream = g_ref[:, 0, :, :].reshape(block, HD)
    key_rows = k_s[...]
    value_rows = v_s[...]
    scores = contract(queries * jnp.asarray(factor, queries.dtype), key_rows, 1, 1)
    raised = jnp.exp(scores - jnp.max(scores, axis=1, keepdims=True))
    attention = raised / jnp.sum(raised, axis=1, keepdims=True)
    d_attention = contract(upstream, value_rows, 1, 1)
    inner_sum = jnp.sum(attention * d_attention, axis=1, keepdims=True)
    d_scores = (attention * (d_attention - inner_sum)).astype(jnp.bfloat16)
    grad_query = contract(d_scores, key_rows, 1, 0) * factor
    out_ref[pl.ds(first, per_block), 0, :, 0:HD] = grad_query.astype(jnp.bfloat16).reshape(
        per_block, slots, HD
    )
    dk_acc[...] += contract(d_scores, queries, 0, 0)
    dv_acc[...] += contract(attention.astype(jnp.bfloat16), upstream, 0, 0)

    @pl.when(step == pl.num_programs(1) - 1)
    def _():
        out_ref[:, 0, :, HD : 2 * HD] = (dk_acc[...] * factor).astype(jnp.bfloat16).reshape(
            owners, slots, HD
        )
        out_ref[:, 0, :, 2 * HD : 3 * HD] = dv_acc[...].astype(jnp.bfloat16).reshape(owners, slots, HD)


def attention_grads(lanes, upstream):
    owners, windows, slots, width = lanes.shape
    length = owners * slots
    per_block = max(1, QUERY_BLOCK // slots)
    lanes_spec = pl.BlockSpec((owners, 1, slots, width), lambda w, i: (0, w, 0, 0))
    g_spec = pl.BlockSpec((per_block, 1, slots, HD), lambda w, i: (i, w, 0, 0))
    flops = 10 * windows * length * length * HD
    return pl.pallas_call(
        attention_kernel,
        grid=(windows, owners // per_block),
        in_specs=[lanes_spec, g_spec],
        out_specs=lanes_spec,
        out_shape=jax.ShapeDtypeStruct(lanes.shape, jnp.bfloat16),
        scratch_shapes=[
            pltpu.VMEM((length, HD), jnp.bfloat16),
            pltpu.VMEM((length, HD), jnp.bfloat16),
            pltpu.VMEM((length, HD), jnp.float32),
            pltpu.VMEM((length, HD), jnp.float32),
        ],
        compiler_params=pltpu.CompilerParams(
            dimension_semantics=("arbitrary", "arbitrary"),
            vmem_limit_bytes=48 * 1024 * 1024,
        ),
        cost_estimate=pl.CostEstimate(
            flops=flops,
            transcendentals=windows * length * length,
            bytes_accessed=7 * windows * length * HD * 2,
        ),
    )(lanes, upstream)


def body(voxels, brain_list, owner_slot, embed_weight, qkv_weight, cotangent):
    slab_count = lax.axis_size("space")
    tm_count = lax.axis_size("tm")
    capacity = 3 * OWN // (2 * slab_count)
    buckets = slab_count * capacity
    windows = voxels.shape[0]
    row_total = windows * OWN
    side_y = GY // 6
    side_z = GZ // 6
    frames = voxels.shape[1]
    depth = voxels.shape[2]
    lanes_b = -(-buckets // 128) * 128
    my_buckets = bucket_index(owner_slot, slab_count, capacity)
    to_bucket = (
        my_buckets[:, None, :] == jnp.arange(lanes_b, dtype=jnp.int32)[None, :, None]
    ).astype(jnp.bfloat16)
    slot_code = (jnp.where(owner_slot >= 0, owner_slot % OWN, -1) + 1).astype(jnp.bfloat16)
    bucket_code = select(to_bucket, slot_code[:, :, None])[:, :buckets]
    patch_code = select(to_bucket, (brain_list + 1).astype(jnp.float32)[:, :, None].astype(jnp.bfloat16))
    patch_of = patch_code[:, :, 0].astype(jnp.int32) - 1
    py_of = jnp.where(patch_of >= 0, patch_of // side_z, -1)
    pz_of = jnp.where(patch_of >= 0, patch_of % side_z, -1)
    z_index = jnp.arange(GZ, dtype=jnp.int32)
    inner = jnp.arange(6, dtype=jnp.int32)
    pick_z = (
        z_index[None, :, None, None]
        == pz_of[:, None, None, :] * 6 + inner[None, None, :, None]
    ).astype(jnp.bfloat16).reshape(windows, GZ, 6 * lanes_b)
    rows = voxels.reshape(windows, frames, depth * GY, GZ)
    y_index = jnp.arange(GY, dtype=jnp.int32)
    keep_y = jnp.broadcast_to(
        (y_index[None, :, None, None] // 6 == py_of[:, None, None, :]),
        (windows, GY, 6, lanes_b),
    ).astype(jnp.bfloat16).reshape(windows, GY, 6 * lanes_b)
    slab_x = jnp.arange(depth, dtype=jnp.int32)
    fold = (
        (slab_x[:, None, None, None] == slab_x[None, None, :, None])
        & (inner[None, :, None, None] == y_index[None, None, None, :] % 6)
    ).astype(jnp.bfloat16).reshape(depth * 6, depth * GY)
    picked = patch_columns(rows, pick_z, keep_y, fold)
    width = -(-(PATCH + 1) // 128) * 128
    payload = jnp.concatenate(
        [
            picked[:, :buckets],
            bucket_code.astype(jnp.bfloat16),
            jnp.zeros((windows, buckets, width - PATCH - 1), jnp.bfloat16),
        ],
        axis=2,
    ).reshape(windows, slab_count, capacity, width)
    arrived = lax.all_to_all(payload, "space", split_axis=1, concat_axis=1, tiled=True).reshape(
        windows, buckets, width
    )
    arrival_slot = arrived[:, :, PATCH].astype(jnp.int32) - 1
    to_slot = (
        arrival_slot[:, None, :] == jnp.arange(OWN, dtype=jnp.int32)[None, :, None]
    ).astype(jnp.bfloat16)
    chosen = select(to_slot, arrived[:, :, :PATCH]).astype(jnp.bfloat16).reshape(row_total, PATCH)
    full_embed = (
        lax.all_to_all(
            jnp.broadcast_to(embed_weight[None], (tm_count,) + embed_weight.shape),
            "tm",
            split_axis=0,
            concat_axis=0,
            tiled=True,
        )
        .transpose(1, 0, 2)
        .reshape(4, 6, 6, 6, D)
        .transpose(0, 3, 1, 2, 4)
        .reshape(PATCH, D)
    )
    tokens = jnp.dot(chosen, full_embed, preferred_element_type=jnp.float32).astype(jnp.bfloat16)
    widened = tokens.astype(jnp.float32)
    center = widened - jnp.mean(widened, axis=1, keepdims=True)
    inverse = lax.rsqrt(jnp.mean(center * center, axis=1, keepdims=True) + 1e-05)
    normed = center * inverse
    hidden = normed.astype(jnp.bfloat16)
    wide_rows = lax.all_gather(qkv_weight, "tm", axis=1, tiled=True)
    full_qkv = lax.all_gather(wide_rows, "space", axis=0, tiled=True)
    heads = D // HD
    head_qkv = full_qkv.reshape(D, 3, heads, HD).transpose(0, 2, 1, 3).reshape(D, 3 * D)
    packed = jnp.dot(hidden, head_qkv, preferred_element_type=jnp.float32).astype(jnp.bfloat16)
    lanes_out = packed.reshape(windows, OWN, heads, 3 * HD).transpose(2, 0, 1, 3)
    upstream_out = cotangent.reshape(windows, OWN, heads, HD).transpose(2, 0, 1, 3)
    lanes = lax.all_to_all(lanes_out, "space", split_axis=0, concat_axis=0, tiled=True)
    upstream = lax.all_to_all(upstream_out, "space", split_axis=0, concat_axis=0, tiled=True)
    grads = attention_grads(lanes, upstream)
    returned = lax.all_to_all(grads, "space", split_axis=0, concat_axis=0, tiled=True)
    d_packed = (
        returned.reshape(heads, windows, OWN, 3, HD)
        .transpose(1, 2, 3, 0, 4)
        .reshape(row_total, 3 * D)
    )
    my_rows = lax.psum_scatter(
        contract(hidden, d_packed, 0, 0).astype(jnp.bfloat16),
        "space",
        scatter_dimension=0,
        tiled=True,
    )
    row_block = my_rows.shape[0]
    col_block = 3 * D // tm_count
    qkv_parts = lax.all_to_all(
        my_rows.reshape(row_block, tm_count, col_block).transpose(1, 0, 2),
        "tm",
        split_axis=0,
        concat_axis=0,
        tiled=True,
    )
    d_qkv_weight = jnp.sum(qkv_parts.astype(jnp.float32), axis=0)
    d_hidden = contract(d_packed, full_qkv, 1, 1)
    first_mean = jnp.mean(d_hidden, axis=1, keepdims=True)
    second_mean = jnp.mean(d_hidden * normed, axis=1, keepdims=True)
    d_tokens = (inverse * (d_hidden - first_mean - normed * second_mean)).astype(jnp.bfloat16)
    embed_partial = contract(chosen, d_tokens, 0, 0)
    embed_block = D // tm_count
    embed_parts = lax.all_to_all(
        embed_partial.astype(jnp.bfloat16).reshape(PATCH, tm_count, embed_block).transpose(1, 0, 2),
        "tm",
        split_axis=0,
        concat_axis=0,
        tiled=True,
    )
    embed_cols = jnp.sum(embed_parts.astype(jnp.float32), axis=0)
    chunk = -(-PATCH // slab_count)
    padded = jnp.pad(embed_cols, ((0, chunk * slab_count - PATCH), (0, 0)))
    spread = lax.all_to_all(
        padded.reshape(slab_count, chunk, -1), "space", split_axis=0, concat_axis=0, tiled=True
    )
    reduced = jnp.sum(spread, axis=0)
    gathered = lax.all_to_all(
        jnp.broadcast_to(reduced[None], (slab_count,) + reduced.shape),
        "space",
        split_axis=0,
        concat_axis=0,
        tiled=True,
    )
    d_embed_weight = (
        gathered.reshape(chunk * slab_count, -1)[:PATCH]
        .reshape(4, 6, 6, 6, -1)
        .transpose(0, 2, 3, 1, 4)
        .reshape(PATCH, -1)
    )
    return (d_qkv_weight, d_embed_weight)


def solution(mesh):
    placed = (
        P(None, "tm", "space", None),
        P(None, "space"),
        P(None, "space"),
        P(None, "tm"),
        P("space", "tm"),
        P(None, "tm", "space", None),
    )
    return jax.shard_map(
        body,
        mesh=mesh,
        in_specs=placed,
        out_specs=(P("space", "tm"), P(None, "tm")),
        check_vma=False,
    )
```

```python
import jax
import jax.numpy as jnp
from jax import lax
from jax.sharding import PartitionSpec as P
from jax.experimental import pallas as pl
from jax.experimental.pallas import tpu as pltpu

D = 1024
HD = 64
PATCH = 864
GY = 96
GZ = 96
OWN = 128
PSLAB = 256


def for_sending(array):

    def short(part):
        return part.astype(jnp.bfloat16) if part.dtype == jnp.float32 else part

    return jax.tree.map(short, array)


def contract(left, right, left_dim, right_dim):
    return lax.dot_general(
        left, right, (((left_dim,), (right_dim,)), ((), ())), preferred_element_type=jnp.float32
    )


def select(onehot, rows):
    return jnp.einsum("wab,wbc->wac", onehot, rows, preferred_element_type=jnp.float32)


def bucket_index(slots, slab_count, capacity):
    entries = slots.shape[-1]
    owner_of = jnp.where(slots >= 0, slots // OWN, slab_count)
    hits = (owner_of[..., None] == jnp.arange(slab_count, dtype=jnp.int32)).astype(jnp.bfloat16)
    order = jnp.arange(entries, dtype=jnp.int32)
    before = (order[None, :] < order[:, None]).astype(jnp.bfloat16)
    earlier = jnp.einsum("ij,wjo->wio", before, hits, preferred_element_type=jnp.float32)
    position = jnp.sum(earlier * hits.astype(jnp.float32), axis=-1).astype(jnp.int32)
    return jnp.where(slots >= 0, owner_of * capacity + position, slab_count * capacity)


def patch_kernel(rows_ref, pick_ref, keep_ref, fold_ref, out_ref):
    frames = rows_ref.shape[1]
    depth = fold_ref.shape[0] // 6
    lanes_b = out_ref.shape[1]
    span = 6 * fold_ref.shape[0]
    keep = keep_ref[0].astype(jnp.float32)[None]
    for frame in range(frames):
        by_z = jnp.dot(rows_ref[0, frame], pick_ref[0], preferred_element_type=jnp.float32)
        rows_per = by_z.shape[0] // depth
        masked = (by_z.reshape(depth, rows_per, -1) * keep).reshape(depth * rows_per, -1)
        by_y = contract(masked.astype(jnp.bfloat16), fold_ref[...], 0, 1)
        for inner in range(6):
            start = frame * span + inner * fold_ref.shape[0]
            out_ref[0, :, start : start + fold_ref.shape[0]] = by_y[
                inner * lanes_b : (inner + 1) * lanes_b
            ].astype(out_ref.dtype)


def patch_columns(rows, pick_z, keep_y, fold):
    windows = rows.shape[0]
    lanes_b = pick_z.shape[2] // 6
    return pl.pallas_call(
        patch_kernel,
        grid=(windows,),
        in_specs=[
            pl.BlockSpec((1,) + rows.shape[1:], lambda w: (w, 0, 0, 0)),
            pl.BlockSpec((1,) + pick_z.shape[1:], lambda w: (w, 0, 0)),
            pl.BlockSpec((1,) + keep_y.shape[1:], lambda w: (w, 0, 0)),
            pl.BlockSpec(fold.shape, lambda w: (0, 0)),
        ],
        out_specs=pl.BlockSpec((1, lanes_b, PATCH), lambda w: (w, 0, 0)),
        out_shape=jax.ShapeDtypeStruct((windows, lanes_b, PATCH), jnp.bfloat16),
        compiler_params=pltpu.CompilerParams(
            dimension_semantics=("arbitrary",),
            vmem_limit_bytes=48 * 1024 * 1024,
        ),
        cost_estimate=pl.CostEstimate(
            flops=2 * rows.shape[0] * rows.shape[1] * rows.shape[2] * pick_z.shape[1] * pick_z.shape[2] * 2,
            transcendentals=0,
            bytes_accessed=rows.size * 2 + windows * lanes_b * PATCH * 2,
        ),
    )(rows, pick_z, keep_y, fold)


QUERY_BLOCK = 256


def attention_kernel(lanes_ref, g_ref, out_ref, k_s, v_s, dk_acc, dv_acc):
    step = pl.program_id(1)
    owners, _, slots, _ = lanes_ref.shape
    per_block = g_ref.shape[0]
    length = owners * slots
    block = per_block * slots
    factor = HD ** (-0.5)

    @pl.when(step == 0)
    def _():
        k_s[...] = lanes_ref[:, 0, :, HD : 2 * HD].reshape(length, HD)
        v_s[...] = lanes_ref[:, 0, :, 2 * HD : 3 * HD].reshape(length, HD)
        dk_acc[...] = jnp.zeros_like(dk_acc)
        dv_acc[...] = jnp.zeros_like(dv_acc)

    first = pl.multiple_of(step * per_block, per_block)
    queries = lanes_ref[pl.ds(first, per_block), 0, :, 0:HD].reshape(block, HD)
    upstream = g_ref[:, 0, :, :].reshape(block, HD)
    key_rows = k_s[...]
    value_rows = v_s[...]
    scores = contract(queries * jnp.asarray(factor, queries.dtype), key_rows, 1, 1)
    raised = jnp.exp(scores - jnp.max(scores, axis=1, keepdims=True))
    attention = raised / jnp.sum(raised, axis=1, keepdims=True)
    d_attention = contract(upstream, value_rows, 1, 1)
    inner_sum = jnp.sum(attention * d_attention, axis=1, keepdims=True)
    d_scores = (attention * (d_attention - inner_sum)).astype(jnp.bfloat16)
    grad_query = contract(d_scores, key_rows, 1, 0) * factor
    out_ref[pl.ds(first, per_block), 0, :, 0:HD] = grad_query.astype(jnp.bfloat16).reshape(
        per_block, slots, HD
    )
    dk_acc[...] += contract(d_scores, queries, 0, 0)
    dv_acc[...] += contract(attention.astype(jnp.bfloat16), upstream, 0, 0)

    @pl.when(step == pl.num_programs(1) - 1)
    def _():
        out_ref[:, 0, :, HD : 2 * HD] = (dk_acc[...] * factor).astype(jnp.bfloat16).reshape(
            owners, slots, HD
        )
        out_ref[:, 0, :, 2 * HD : 3 * HD] = dv_acc[...].astype(jnp.bfloat16).reshape(owners, slots, HD)


def attention_grads(lanes, upstream):
    owners, windows, slots, width = lanes.shape
    length = owners * slots
    per_block = max(1, QUERY_BLOCK // slots)
    lanes_spec = pl.BlockSpec((owners, 1, slots, width), lambda w, i: (0, w, 0, 0))
    g_spec = pl.BlockSpec((per_block, 1, slots, HD), lambda w, i: (i, w, 0, 0))
    flops = 10 * windows * length * length * HD
    return pl.pallas_call(
        attention_kernel,
        grid=(windows, owners // per_block),
        in_specs=[lanes_spec, g_spec],
        out_specs=lanes_spec,
        out_shape=jax.ShapeDtypeStruct(lanes.shape, jnp.bfloat16),
        scratch_shapes=[
            pltpu.VMEM((length, HD), jnp.bfloat16),
            pltpu.VMEM((length, HD), jnp.bfloat16),
            pltpu.VMEM((length, HD), jnp.float32),
            pltpu.VMEM((length, HD), jnp.float32),
        ],
        compiler_params=pltpu.CompilerParams(
            dimension_semantics=("arbitrary", "arbitrary"),
            vmem_limit_bytes=48 * 1024 * 1024,
        ),
        cost_estimate=pl.CostEstimate(
            flops=flops,
            transcendentals=windows * length * length,
            bytes_accessed=7 * windows * length * HD * 2,
        ),
    )(lanes, upstream)


def body(voxels, brain_list, owner_slot, embed_weight, qkv_weight, cotangent):
    slab_count = lax.axis_size("space")
    tm_count = lax.axis_size("tm")
    capacity = 3 * OWN // (2 * slab_count)
    buckets = slab_count * capacity
    windows = voxels.shape[0]
    row_total = windows * OWN
    side_y = GY // 6
    side_z = GZ // 6
    frames = voxels.shape[1]
    depth = voxels.shape[2]
    lanes_b = -(-buckets // 128) * 128
    my_buckets = bucket_index(owner_slot, slab_count, capacity)
    to_bucket = (
        my_buckets[:, None, :] == jnp.arange(lanes_b, dtype=jnp.int32)[None, :, None]
    ).astype(jnp.bfloat16)
    slot_code = (jnp.where(owner_slot >= 0, owner_slot % OWN, -1) + 1).astype(jnp.bfloat16)
    bucket_code = select(to_bucket, slot_code[:, :, None])[:, :buckets]
    patch_code = select(to_bucket, (brain_list + 1).astype(jnp.float32)[:, :, None].astype(jnp.bfloat16))
    patch_of = patch_code[:, :, 0].astype(jnp.int32) - 1
    py_of = jnp.where(patch_of >= 0, patch_of // side_z, -1)
    pz_of = jnp.where(patch_of >= 0, patch_of % side_z, -1)
    z_index = jnp.arange(GZ, dtype=jnp.int32)
    inner = jnp.arange(6, dtype=jnp.int32)
    pick_z = (
        z_index[None, :, None, None]
        == pz_of[:, None, None, :] * 6 + inner[None, None, :, None]
    ).astype(jnp.bfloat16).reshape(windows, GZ, 6 * lanes_b)
    rows = voxels.reshape(windows, frames, depth * GY, GZ)
    y_index = jnp.arange(GY, dtype=jnp.int32)
    keep_y = jnp.broadcast_to(
        (y_index[None, :, None, None] // 6 == py_of[:, None, None, :]),
        (windows, GY, 6, lanes_b),
    ).astype(jnp.bfloat16).reshape(windows, GY, 6 * lanes_b)
    slab_x = jnp.arange(depth, dtype=jnp.int32)
    fold = (
        (slab_x[:, None, None, None] == slab_x[None, None, :, None])
        & (inner[None, :, None, None] == y_index[None, None, None, :] % 6)
    ).astype(jnp.bfloat16).reshape(depth * 6, depth * GY)
    picked = patch_columns(rows, pick_z, keep_y, fold)
    width = -(-(PATCH + 1) // 128) * 128
    payload = jnp.concatenate(
        [
            picked[:, :buckets],
            bucket_code.astype(jnp.bfloat16),
            jnp.zeros((windows, buckets, width - PATCH - 1), jnp.bfloat16),
        ],
        axis=2,
    ).reshape(windows, slab_count, capacity, width)
    arrived = lax.all_to_all(payload, "space", split_axis=1, concat_axis=1, tiled=True).reshape(
        windows, buckets, width
    )
    arrival_slot = arrived[:, :, PATCH].astype(jnp.int32) - 1
    to_slot = (
        arrival_slot[:, None, :] == jnp.arange(OWN, dtype=jnp.int32)[None, :, None]
    ).astype(jnp.bfloat16)
    chosen = select(to_slot, arrived[:, :, :PATCH]).astype(jnp.bfloat16).reshape(row_total, PATCH)
    full_embed = (
        lax.all_to_all(
            jnp.broadcast_to(embed_weight[None], (tm_count,) + embed_weight.shape),
            "tm",
            split_axis=0,
            concat_axis=0,
            tiled=True,
        )
        .transpose(1, 0, 2)
        .reshape(4, 6, 6, 6, D)
        .transpose(0, 3, 1, 2, 4)
        .reshape(PATCH, D)
    )
    tokens = jnp.dot(chosen, full_embed, preferred_element_type=jnp.float32).astype(jnp.bfloat16)
    widened = tokens.astype(jnp.float32)
    center = widened - jnp.mean(widened, axis=1, keepdims=True)
    inverse = lax.rsqrt(jnp.mean(center * center, axis=1, keepdims=True) + 1e-05)
    normed = center * inverse
    hidden = normed.astype(jnp.bfloat16)
    wide_rows = lax.all_gather(qkv_weight, "tm", axis=1, tiled=True)
    full_qkv = lax.all_gather(wide_rows, "space", axis=0, tiled=True)
    heads = D // HD
    packed = jnp.dot(hidden, full_qkv, preferred_element_type=jnp.float32).astype(jnp.bfloat16)
    lanes_out = (
        packed.reshape(windows, OWN, 3, heads, HD)
        .transpose(3, 0, 1, 2, 4)
        .reshape(heads, windows, OWN, 3 * HD)
    )
    upstream_out = cotangent.reshape(windows, OWN, heads, HD).transpose(2, 0, 1, 3)
    lanes = lax.all_to_all(lanes_out, "space", split_axis=0, concat_axis=0, tiled=True)
    upstream = lax.all_to_all(upstream_out, "space", split_axis=0, concat_axis=0, tiled=True)
    grads = attention_grads(lanes, upstream)
    returned = lax.all_to_all(grads, "space", split_axis=0, concat_axis=0, tiled=True)
    d_packed = (
        returned.reshape(heads, windows, OWN, 3, HD)
        .transpose(1, 2, 3, 0, 4)
        .reshape(row_total, 3 * D)
    )
    my_rows = lax.psum_scatter(
        contract(hidden, d_packed, 0, 0).astype(jnp.bfloat16),
        "space",
        scatter_dimension=0,
        tiled=True,
    )
    row_block = my_rows.shape[0]
    col_block = 3 * D // tm_count
    qkv_parts = lax.all_to_all(
        my_rows.reshape(row_block, tm_count, col_block).transpose(1, 0, 2),
        "tm",
        split_axis=0,
        concat_axis=0,
        tiled=True,
    )
    d_qkv_weight = jnp.sum(qkv_parts.astype(jnp.float32), axis=0)
    d_hidden = contract(d_packed, full_qkv, 1, 1)
    first_mean = jnp.mean(d_hidden, axis=1, keepdims=True)
    second_mean = jnp.mean(d_hidden * normed, axis=1, keepdims=True)
    d_tokens = (inverse * (d_hidden - first_mean - normed * second_mean)).astype(jnp.bfloat16)
    embed_partial = contract(chosen, d_tokens, 0, 0)
    embed_block = D // tm_count
    embed_parts = lax.all_to_all(
        embed_partial.astype(jnp.bfloat16).reshape(PATCH, tm_count, embed_block).transpose(1, 0, 2),
        "tm",
        split_axis=0,
        concat_axis=0,
        tiled=True,
    )
    embed_cols = jnp.sum(embed_parts.astype(jnp.float32), axis=0)
    chunk = -(-PATCH // slab_count)
    padded = jnp.pad(embed_cols, ((0, chunk * slab_count - PATCH), (0, 0)))
    spread = lax.all_to_all(
        padded.reshape(slab_count, chunk, -1), "space", split_axis=0, concat_axis=0, tiled=True
    )
    reduced = jnp.sum(spread, axis=0)
    gathered = lax.all_to_all(
        jnp.broadcast_to(reduced[None], (slab_count,) + reduced.shape),
        "space",
        split_axis=0,
        concat_axis=0,
        tiled=True,
    )
    d_embed_weight = (
        gathered.reshape(chunk * slab_count, -1)[:PATCH]
        .reshape(4, 6, 6, 6, -1)
        .transpose(0, 2, 3, 1, 4)
        .reshape(PATCH, -1)
    )
    return (d_qkv_weight, d_embed_weight)


def solution(mesh):
    placed = (
        P(None, "tm", "space", None),
        P(None, "space"),
        P(None, "space"),
        P(None, "tm"),
        P("space", "tm"),
        P(None, "tm", "space", None),
    )
    return jax.shard_map(
        body,
        mesh=mesh,
        in_specs=placed,
        out_specs=(P("space", "tm"), P(None, "tm")),
        check_vma=False,
    )
```

```python
import jax
import jax.numpy as jnp
from jax import lax
from jax.sharding import PartitionSpec as P
from jax.experimental import pallas as pl
from jax.experimental.pallas import tpu as pltpu

D = 1024
HD = 64
PATCH = 864
GY = 96
GZ = 96
OWN = 128
PSLAB = 256


def for_sending(array):

    def short(part):
        return part.astype(jnp.bfloat16) if part.dtype == jnp.float32 else part

    return jax.tree.map(short, array)


def contract(left, right, left_dim, right_dim):
    return lax.dot_general(
        left, right, (((left_dim,), (right_dim,)), ((), ())), preferred_element_type=jnp.float32
    )


def select(onehot, rows):
    return jnp.einsum("wab,wbc->wac", onehot, rows, preferred_element_type=jnp.float32)


def bucket_index(slots, slab_count, capacity):
    entries = slots.shape[-1]
    owner_of = jnp.where(slots >= 0, slots // OWN, slab_count)
    hits = (owner_of[..., None] == jnp.arange(slab_count, dtype=jnp.int32)).astype(jnp.bfloat16)
    order = jnp.arange(entries, dtype=jnp.int32)
    before = (order[None, :] < order[:, None]).astype(jnp.bfloat16)
    earlier = jnp.einsum("ij,wjo->wio", before, hits, preferred_element_type=jnp.float32)
    position = jnp.sum(earlier * hits.astype(jnp.float32), axis=-1).astype(jnp.int32)
    return jnp.where(slots >= 0, owner_of * capacity + position, slab_count * capacity)


def patch_kernel(rows_ref, pick_ref, keep_ref, fold_ref, out_ref):
    frames = rows_ref.shape[1]
    depth = fold_ref.shape[0] // 6
    lanes_b = out_ref.shape[1]
    span = 6 * fold_ref.shape[0]
    keep = keep_ref[0].astype(jnp.float32)[None]
    for frame in range(frames):
        by_z = jnp.dot(rows_ref[0, frame], pick_ref[0], preferred_element_type=jnp.float32)
        rows_per = by_z.shape[0] // depth
        masked = (by_z.reshape(depth, rows_per, -1) * keep).reshape(depth * rows_per, -1)
        by_y = contract(masked.astype(jnp.bfloat16), fold_ref[...], 0, 1)
        for inner in range(6):
            start = frame * span + inner * fold_ref.shape[0]
            out_ref[0, :, start : start + fold_ref.shape[0]] = by_y[
                inner * lanes_b : (inner + 1) * lanes_b
            ].astype(out_ref.dtype)


def patch_columns(rows, pick_z, keep_y, fold):
    windows = rows.shape[0]
    lanes_b = pick_z.shape[2] // 6
    return pl.pallas_call(
        patch_kernel,
        grid=(windows,),
        in_specs=[
            pl.BlockSpec((1,) + rows.shape[1:], lambda w: (w, 0, 0, 0)),
            pl.BlockSpec((1,) + pick_z.shape[1:], lambda w: (w, 0, 0)),
            pl.BlockSpec((1,) + keep_y.shape[1:], lambda w: (w, 0, 0)),
            pl.BlockSpec(fold.shape, lambda w: (0, 0)),
        ],
        out_specs=pl.BlockSpec((1, lanes_b, PATCH), lambda w: (w, 0, 0)),
        out_shape=jax.ShapeDtypeStruct((windows, lanes_b, PATCH), jnp.bfloat16),
        compiler_params=pltpu.CompilerParams(
            dimension_semantics=("arbitrary",),
            vmem_limit_bytes=48 * 1024 * 1024,
        ),
        cost_estimate=pl.CostEstimate(
            flops=2 * rows.shape[0] * rows.shape[1] * rows.shape[2] * pick_z.shape[1] * pick_z.shape[2] * 2,
            transcendentals=0,
            bytes_accessed=rows.size * 2 + windows * lanes_b * PATCH * 2,
        ),
    )(rows, pick_z, keep_y, fold)


QUERY_BLOCK = 256


def attention_kernel(lanes_ref, out_ref, k_s, v_s, dk_acc, dv_acc):
    step = pl.program_id(1)
    owners, _, slots, _ = lanes_ref.shape
    per_block = max(1, QUERY_BLOCK // slots)
    length = owners * slots
    block = per_block * slots
    factor = HD ** (-0.5)

    @pl.when(step == 0)
    def _():
        k_s[...] = lanes_ref[:, 0, :, HD : 2 * HD].reshape(length, HD)
        v_s[...] = lanes_ref[:, 0, :, 2 * HD : 3 * HD].reshape(length, HD)
        dk_acc[...] = jnp.zeros_like(dk_acc)
        dv_acc[...] = jnp.zeros_like(dv_acc)

    first = pl.multiple_of(step * per_block, per_block)
    queries = lanes_ref[pl.ds(first, per_block), 0, :, 0:HD].reshape(block, HD)
    upstream = lanes_ref[pl.ds(first, per_block), 0, :, 3 * HD : 4 * HD].reshape(block, HD)
    key_rows = k_s[...]
    value_rows = v_s[...]
    scores = contract(queries * jnp.asarray(factor, queries.dtype), key_rows, 1, 1)
    raised = jnp.exp(scores - jnp.max(scores, axis=1, keepdims=True))
    attention = raised / jnp.sum(raised, axis=1, keepdims=True)
    d_attention = contract(upstream, value_rows, 1, 1)
    inner_sum = jnp.sum(attention * d_attention, axis=1, keepdims=True)
    d_scores = (attention * (d_attention - inner_sum)).astype(jnp.bfloat16)
    grad_query = contract(d_scores, key_rows, 1, 0) * factor
    out_ref[pl.ds(first, per_block), 0, :, 0:HD] = grad_query.astype(jnp.bfloat16).reshape(
        per_block, slots, HD
    )
    dk_acc[...] += contract(d_scores, queries, 0, 0)
    dv_acc[...] += contract(attention.astype(jnp.bfloat16), upstream, 0, 0)

    @pl.when(step == pl.num_programs(1) - 1)
    def _():
        out_ref[:, 0, :, HD : 2 * HD] = (dk_acc[...] * factor).astype(jnp.bfloat16).reshape(
            owners, slots, HD
        )
        out_ref[:, 0, :, 2 * HD : 3 * HD] = dv_acc[...].astype(jnp.bfloat16).reshape(owners, slots, HD)


def attention_grads(lanes):
    owners, windows, slots, width = lanes.shape
    length = owners * slots
    per_block = max(1, QUERY_BLOCK // slots)
    lanes_spec = pl.BlockSpec((owners, 1, slots, width), lambda w, i: (0, w, 0, 0))
    out_spec = pl.BlockSpec((owners, 1, slots, 3 * HD), lambda w, i: (0, w, 0, 0))
    flops = 10 * windows * length * length * HD
    return pl.pallas_call(
        attention_kernel,
        grid=(windows, owners // per_block),
        in_specs=[lanes_spec],
        out_specs=out_spec,
        out_shape=jax.ShapeDtypeStruct((owners, windows, slots, 3 * HD), jnp.bfloat16),
        scratch_shapes=[
            pltpu.VMEM((length, HD), jnp.bfloat16),
            pltpu.VMEM((length, HD), jnp.bfloat16),
            pltpu.VMEM((length, HD), jnp.float32),
            pltpu.VMEM((length, HD), jnp.float32),
        ],
        compiler_params=pltpu.CompilerParams(
            dimension_semantics=("arbitrary", "arbitrary"),
            vmem_limit_bytes=48 * 1024 * 1024,
        ),
        cost_estimate=pl.CostEstimate(
            flops=flops,
            transcendentals=windows * length * length,
            bytes_accessed=7 * windows * length * HD * 2,
        ),
    )(lanes)


def body(voxels, brain_list, owner_slot, embed_weight, qkv_weight, cotangent):
    slab_count = lax.axis_size("space")
    tm_count = lax.axis_size("tm")
    capacity = 3 * OWN // (2 * slab_count)
    buckets = slab_count * capacity
    windows = voxels.shape[0]
    row_total = windows * OWN
    side_y = GY // 6
    side_z = GZ // 6
    frames = voxels.shape[1]
    depth = voxels.shape[2]
    lanes_b = -(-buckets // 128) * 128
    my_buckets = bucket_index(owner_slot, slab_count, capacity)
    to_bucket = (
        my_buckets[:, None, :] == jnp.arange(lanes_b, dtype=jnp.int32)[None, :, None]
    ).astype(jnp.bfloat16)
    slot_code = (jnp.where(owner_slot >= 0, owner_slot % OWN, -1) + 1).astype(jnp.bfloat16)
    bucket_code = select(to_bucket, slot_code[:, :, None])[:, :buckets]
    patch_code = select(to_bucket, (brain_list + 1).astype(jnp.float32)[:, :, None].astype(jnp.bfloat16))
    patch_of = patch_code[:, :, 0].astype(jnp.int32) - 1
    py_of = jnp.where(patch_of >= 0, patch_of // side_z, -1)
    pz_of = jnp.where(patch_of >= 0, patch_of % side_z, -1)
    z_index = jnp.arange(GZ, dtype=jnp.int32)
    inner = jnp.arange(6, dtype=jnp.int32)
    pick_z = (
        z_index[None, :, None, None]
        == pz_of[:, None, None, :] * 6 + inner[None, None, :, None]
    ).astype(jnp.bfloat16).reshape(windows, GZ, 6 * lanes_b)
    rows = voxels.reshape(windows, frames, depth * GY, GZ)
    y_index = jnp.arange(GY, dtype=jnp.int32)
    keep_y = jnp.broadcast_to(
        (y_index[None, :, None, None] // 6 == py_of[:, None, None, :]),
        (windows, GY, 6, lanes_b),
    ).astype(jnp.bfloat16).reshape(windows, GY, 6 * lanes_b)
    slab_x = jnp.arange(depth, dtype=jnp.int32)
    fold = (
        (slab_x[:, None, None, None] == slab_x[None, None, :, None])
        & (inner[None, :, None, None] == y_index[None, None, None, :] % 6)
    ).astype(jnp.bfloat16).reshape(depth * 6, depth * GY)
    picked = patch_columns(rows, pick_z, keep_y, fold)
    width = -(-(PATCH + 1) // 128) * 128
    payload = jnp.concatenate(
        [
            picked[:, :buckets],
            bucket_code.astype(jnp.bfloat16),
            jnp.zeros((windows, buckets, width - PATCH - 1), jnp.bfloat16),
        ],
        axis=2,
    ).reshape(windows, slab_count, capacity, width)
    arrived = lax.all_to_all(payload, "space", split_axis=1, concat_axis=1, tiled=True).reshape(
        windows, buckets, width
    )
    arrival_slot = arrived[:, :, PATCH].astype(jnp.int32) - 1
    to_slot = (
        arrival_slot[:, None, :] == jnp.arange(OWN, dtype=jnp.int32)[None, :, None]
    ).astype(jnp.bfloat16)
    chosen = select(to_slot, arrived[:, :, :PATCH]).astype(jnp.bfloat16).reshape(row_total, PATCH)
    local_embed = (
        embed_weight.reshape(4, 6, 6, 6, -1).transpose(0, 3, 1, 2, 4).reshape(PATCH, -1)
    )
    embed_blocks = lax.all_to_all(
        jnp.broadcast_to(local_embed[None], (tm_count,) + local_embed.shape),
        "tm",
        split_axis=0,
        concat_axis=0,
        tiled=True,
    )
    tokens = (
        jnp.einsum("nr,trc->ntc", chosen, embed_blocks, preferred_element_type=jnp.float32)
        .astype(jnp.bfloat16)
        .reshape(row_total, D)
    )
    widened = tokens.astype(jnp.float32)
    center = widened - jnp.mean(widened, axis=1, keepdims=True)
    inverse = lax.rsqrt(jnp.mean(center * center, axis=1, keepdims=True) + 1e-05)
    normed = center * inverse
    hidden = normed.astype(jnp.bfloat16)
    wide_rows = lax.all_gather(qkv_weight, "tm", axis=1, tiled=True)
    full_qkv = lax.all_gather(wide_rows, "space", axis=0, tiled=True)
    heads = D // HD
    packed = jnp.dot(hidden, full_qkv, preferred_element_type=jnp.float32).astype(jnp.bfloat16)
    lanes_out = jnp.concatenate(
        [packed.reshape(windows, OWN, 3, heads, HD), cotangent.reshape(windows, OWN, 1, heads, HD)],
        axis=2,
    ).transpose(3, 0, 1, 2, 4).reshape(heads, windows, OWN, 4 * HD)
    lanes = lax.all_to_all(lanes_out, "space", split_axis=0, concat_axis=0, tiled=True)
    grads = attention_grads(lanes)
    returned = lax.all_to_all(grads, "space", split_axis=0, concat_axis=0, tiled=True)
    d_packed = (
        returned.reshape(heads, windows, OWN, 3, HD)
        .transpose(1, 2, 3, 0, 4)
        .reshape(row_total, 3 * D)
    )
    my_rows = lax.psum_scatter(
        contract(hidden, d_packed, 0, 0).astype(jnp.bfloat16),
        "space",
        scatter_dimension=0,
        tiled=True,
    )
    row_block = my_rows.shape[0]
    col_block = 3 * D // tm_count
    qkv_parts = lax.all_to_all(
        my_rows.reshape(row_block, tm_count, col_block).transpose(1, 0, 2),
        "tm",
        split_axis=0,
        concat_axis=0,
        tiled=True,
    )
    d_qkv_weight = jnp.sum(qkv_parts.astype(jnp.float32), axis=0)
    d_hidden = contract(d_packed, full_qkv, 1, 1)
    first_mean = jnp.mean(d_hidden, axis=1, keepdims=True)
    second_mean = jnp.mean(d_hidden * normed, axis=1, keepdims=True)
    d_tokens = (inverse * (d_hidden - first_mean - normed * second_mean)).astype(jnp.bfloat16)
    embed_partial = contract(chosen, d_tokens, 0, 0)
    embed_block = D // tm_count
    embed_parts = lax.all_to_all(
        embed_partial.astype(jnp.bfloat16).reshape(PATCH, tm_count, embed_block).transpose(1, 0, 2),
        "tm",
        split_axis=0,
        concat_axis=0,
        tiled=True,
    )
    embed_cols = jnp.sum(embed_parts.astype(jnp.float32), axis=0)
    chunk = -(-PATCH // slab_count)
    padded = jnp.pad(embed_cols, ((0, chunk * slab_count - PATCH), (0, 0)))
    spread = lax.all_to_all(
        padded.reshape(slab_count, chunk, -1), "space", split_axis=0, concat_axis=0, tiled=True
    )
    reduced = jnp.sum(spread, axis=0)
    gathered = lax.all_to_all(
        jnp.broadcast_to(reduced[None], (slab_count,) + reduced.shape),
        "space",
        split_axis=0,
        concat_axis=0,
        tiled=True,
    )
    d_embed_weight = (
        gathered.reshape(chunk * slab_count, -1)[:PATCH]
        .reshape(4, 6, 6, 6, -1)
        .transpose(0, 2, 3, 1, 4)
        .reshape(PATCH, -1)
    )
    return (d_qkv_weight, d_embed_weight)


def solution(mesh):
    placed = (
        P(None, "tm", "space", None),
        P(None, "space"),
        P(None, "space"),
        P(None, "tm"),
        P("space", "tm"),
        P(None, "tm", "space", None),
    )
    return jax.shard_map(
        body,
        mesh=mesh,
        in_specs=placed,
        out_specs=(P("space", "tm"), P(None, "tm")),
        check_vma=False,
    )
```

```python
import jax
import jax.numpy as jnp
from jax import lax
from jax.sharding import PartitionSpec as P
from jax.experimental import pallas as pl
from jax.experimental.pallas import tpu as pltpu

D = 1024
HD = 64
PATCH = 864
GY = 96
GZ = 96
OWN = 128
PSLAB = 256


def for_sending(array):

    def short(part):
        return part.astype(jnp.bfloat16) if part.dtype == jnp.float32 else part

    return jax.tree.map(short, array)


def contract(left, right, left_dim, right_dim):
    return lax.dot_general(
        left, right, (((left_dim,), (right_dim,)), ((), ())), preferred_element_type=jnp.float32
    )


def select(onehot, rows):
    return jnp.einsum("wab,wbc->wac", onehot, rows, preferred_element_type=jnp.float32)


def bucket_index(slots, slab_count, capacity):
    entries = slots.shape[-1]
    owner_of = jnp.where(slots >= 0, slots // OWN, slab_count)
    hits = (owner_of[..., None] == jnp.arange(slab_count, dtype=jnp.int32)).astype(jnp.bfloat16)
    order = jnp.arange(entries, dtype=jnp.int32)
    before = (order[None, :] < order[:, None]).astype(jnp.bfloat16)
    earlier = jnp.einsum("ij,wjo->wio", before, hits, preferred_element_type=jnp.float32)
    position = jnp.sum(earlier * hits.astype(jnp.float32), axis=-1).astype(jnp.int32)
    return jnp.where(slots >= 0, owner_of * capacity + position, slab_count * capacity)


def patch_kernel(rows_ref, pick_ref, keep_ref, fold_ref, out_ref):
    frames = rows_ref.shape[1]
    depth = fold_ref.shape[0] // 6
    lanes_b = out_ref.shape[1]
    span = 6 * fold_ref.shape[0]
    keep = keep_ref[0].astype(jnp.float32)[None]
    for frame in range(frames):
        by_z = jnp.dot(rows_ref[0, frame], pick_ref[0], preferred_element_type=jnp.float32)
        rows_per = by_z.shape[0] // depth
        masked = (by_z.reshape(depth, rows_per, -1) * keep).reshape(depth * rows_per, -1)
        by_y = contract(masked.astype(jnp.bfloat16), fold_ref[...], 0, 1)
        for inner in range(6):
            start = frame * span + inner * fold_ref.shape[0]
            out_ref[0, :, start : start + fold_ref.shape[0]] = by_y[
                inner * lanes_b : (inner + 1) * lanes_b
            ].astype(out_ref.dtype)


def patch_columns(rows, pick_z, keep_y, fold):
    windows = rows.shape[0]
    lanes_b = pick_z.shape[2] // 6
    return pl.pallas_call(
        patch_kernel,
        grid=(windows,),
        in_specs=[
            pl.BlockSpec((1,) + rows.shape[1:], lambda w: (w, 0, 0, 0)),
            pl.BlockSpec((1,) + pick_z.shape[1:], lambda w: (w, 0, 0)),
            pl.BlockSpec((1,) + keep_y.shape[1:], lambda w: (w, 0, 0)),
            pl.BlockSpec(fold.shape, lambda w: (0, 0)),
        ],
        out_specs=pl.BlockSpec((1, lanes_b, PATCH), lambda w: (w, 0, 0)),
        out_shape=jax.ShapeDtypeStruct((windows, lanes_b, PATCH), jnp.bfloat16),
        compiler_params=pltpu.CompilerParams(
            dimension_semantics=("arbitrary",),
            vmem_limit_bytes=48 * 1024 * 1024,
        ),
        cost_estimate=pl.CostEstimate(
            flops=2 * rows.shape[0] * rows.shape[1] * rows.shape[2] * pick_z.shape[1] * pick_z.shape[2] * 2,
            transcendentals=0,
            bytes_accessed=rows.size * 2 + windows * lanes_b * PATCH * 2,
        ),
    )(rows, pick_z, keep_y, fold)


QUERY_BLOCK = 512


def attention_kernel(lanes_ref, out_ref, k_s, v_s, dk_acc, dv_acc):
    step = pl.program_id(1)
    owners, _, slots, _ = lanes_ref.shape
    per_block = max(1, QUERY_BLOCK // slots)
    length = owners * slots
    block = per_block * slots
    factor = HD ** (-0.5)

    @pl.when(step == 0)
    def _():
        k_s[...] = lanes_ref[:, 0, :, HD : 2 * HD].reshape(length, HD)
        v_s[...] = lanes_ref[:, 0, :, 2 * HD : 3 * HD].reshape(length, HD)
        dk_acc[...] = jnp.zeros_like(dk_acc)
        dv_acc[...] = jnp.zeros_like(dv_acc)

    first = pl.multiple_of(step * per_block, per_block)
    queries = lanes_ref[pl.ds(first, per_block), 0, :, 0:HD].reshape(block, HD)
    upstream = lanes_ref[pl.ds(first, per_block), 0, :, 3 * HD : 4 * HD].reshape(block, HD)
    key_rows = k_s[...]
    value_rows = v_s[...]
    scores = contract(queries * jnp.asarray(factor, queries.dtype), key_rows, 1, 1)
    raised = jnp.exp(scores - jnp.max(scores, axis=1, keepdims=True))
    attention = raised * (1.0 / jnp.sum(raised, axis=1, keepdims=True))
    d_attention = contract(upstream, value_rows, 1, 1)
    inner_sum = jnp.sum(attention * d_attention, axis=1, keepdims=True)
    d_scores = (attention * (d_attention - inner_sum)).astype(jnp.bfloat16)
    grad_query = contract(d_scores, key_rows, 1, 0) * factor
    out_ref[pl.ds(first, per_block), 0, :, 0:HD] = grad_query.astype(jnp.bfloat16).reshape(
        per_block, slots, HD
    )
    dk_acc[...] += contract(d_scores, queries, 0, 0)
    dv_acc[...] += contract(attention.astype(jnp.bfloat16), upstream, 0, 0)

    @pl.when(step == pl.num_programs(1) - 1)
    def _():
        out_ref[:, 0, :, HD : 2 * HD] = (dk_acc[...] * factor).astype(jnp.bfloat16).reshape(
            owners, slots, HD
        )
        out_ref[:, 0, :, 2 * HD : 3 * HD] = dv_acc[...].astype(jnp.bfloat16).reshape(owners, slots, HD)


def attention_grads(lanes):
    owners, windows, slots, width = lanes.shape
    length = owners * slots
    per_block = max(1, QUERY_BLOCK // slots)
    lanes_spec = pl.BlockSpec((owners, 1, slots, width), lambda w, i: (0, w, 0, 0))
    out_spec = pl.BlockSpec((owners, 1, slots, 3 * HD), lambda w, i: (0, w, 0, 0))
    flops = 10 * windows * length * length * HD
    return pl.pallas_call(
        attention_kernel,
        grid=(windows, owners // per_block),
        in_specs=[lanes_spec],
        out_specs=out_spec,
        out_shape=jax.ShapeDtypeStruct((owners, windows, slots, 3 * HD), jnp.bfloat16),
        scratch_shapes=[
            pltpu.VMEM((length, HD), jnp.bfloat16),
            pltpu.VMEM((length, HD), jnp.bfloat16),
            pltpu.VMEM((length, HD), jnp.float32),
            pltpu.VMEM((length, HD), jnp.float32),
        ],
        compiler_params=pltpu.CompilerParams(
            dimension_semantics=("arbitrary", "arbitrary"),
            vmem_limit_bytes=48 * 1024 * 1024,
        ),
        cost_estimate=pl.CostEstimate(
            flops=flops,
            transcendentals=windows * length * length,
            bytes_accessed=7 * windows * length * HD * 2,
        ),
    )(lanes)


def body(voxels, brain_list, owner_slot, embed_weight, qkv_weight, cotangent):
    slab_count = lax.axis_size("space")
    tm_count = lax.axis_size("tm")
    capacity = 3 * OWN // (2 * slab_count)
    buckets = slab_count * capacity
    windows = voxels.shape[0]
    row_total = windows * OWN
    side_y = GY // 6
    side_z = GZ // 6
    frames = voxels.shape[1]
    depth = voxels.shape[2]
    lanes_b = -(-buckets // 128) * 128
    my_buckets = bucket_index(owner_slot, slab_count, capacity)
    to_bucket = (
        my_buckets[:, None, :] == jnp.arange(lanes_b, dtype=jnp.int32)[None, :, None]
    ).astype(jnp.bfloat16)
    slot_code = (jnp.where(owner_slot >= 0, owner_slot % OWN, -1) + 1).astype(jnp.bfloat16)
    bucket_code = select(to_bucket, slot_code[:, :, None])[:, :buckets]
    patch_code = select(to_bucket, (brain_list + 1).astype(jnp.float32)[:, :, None].astype(jnp.bfloat16))
    patch_of = patch_code[:, :, 0].astype(jnp.int32) - 1
    py_of = jnp.where(patch_of >= 0, patch_of // side_z, -1)
    pz_of = jnp.where(patch_of >= 0, patch_of % side_z, -1)
    z_index = jnp.arange(GZ, dtype=jnp.int32)
    inner = jnp.arange(6, dtype=jnp.int32)
    pick_z = (
        z_index[None, :, None, None]
        == pz_of[:, None, None, :] * 6 + inner[None, None, :, None]
    ).astype(jnp.bfloat16).reshape(windows, GZ, 6 * lanes_b)
    rows = voxels.reshape(windows, frames, depth * GY, GZ)
    y_index = jnp.arange(GY, dtype=jnp.int32)
    keep_y = jnp.broadcast_to(
        (y_index[None, :, None, None] // 6 == py_of[:, None, None, :]),
        (windows, GY, 6, lanes_b),
    ).astype(jnp.bfloat16).reshape(windows, GY, 6 * lanes_b)
    slab_x = jnp.arange(depth, dtype=jnp.int32)
    fold = (
        (slab_x[:, None, None, None] == slab_x[None, None, :, None])
        & (inner[None, :, None, None] == y_index[None, None, None, :] % 6)
    ).astype(jnp.bfloat16).reshape(depth * 6, depth * GY)
    picked = patch_columns(rows, pick_z, keep_y, fold)
    width = -(-(PATCH + 1) // 128) * 128
    payload = jnp.concatenate(
        [
            picked[:, :buckets],
            bucket_code.astype(jnp.bfloat16),
            jnp.zeros((windows, buckets, width - PATCH - 1), jnp.bfloat16),
        ],
        axis=2,
    ).reshape(windows, slab_count, capacity, width)
    arrived = lax.all_to_all(payload, "space", split_axis=1, concat_axis=1, tiled=True).reshape(
        windows, buckets, width
    )
    arrival_slot = arrived[:, :, PATCH].astype(jnp.int32) - 1
    to_slot = (
        arrival_slot[:, None, :] == jnp.arange(OWN, dtype=jnp.int32)[None, :, None]
    ).astype(jnp.bfloat16)
    chosen = select(to_slot, arrived[:, :, :PATCH]).astype(jnp.bfloat16).reshape(row_total, PATCH)
    local_embed = (
        embed_weight.reshape(4, 6, 6, 6, -1).transpose(0, 3, 1, 2, 4).reshape(PATCH, -1)
    )
    embed_blocks = lax.all_to_all(
        jnp.broadcast_to(local_embed[None], (tm_count,) + local_embed.shape),
        "tm",
        split_axis=0,
        concat_axis=0,
        tiled=True,
    )
    tokens = (
        jnp.einsum("nr,trc->ntc", chosen, embed_blocks, preferred_element_type=jnp.float32)
        .astype(jnp.bfloat16)
        .reshape(row_total, D)
    )
    widened = tokens.astype(jnp.float32)
    center = widened - jnp.mean(widened, axis=1, keepdims=True)
    inverse = lax.rsqrt(jnp.mean(center * center, axis=1, keepdims=True) + 1e-05)
    normed = center * inverse
    hidden = normed.astype(jnp.bfloat16)
    wide_rows = lax.all_gather(qkv_weight, "tm", axis=1, tiled=True)
    full_qkv = lax.all_gather(wide_rows, "space", axis=0, tiled=True)
    heads = D // HD
    packed = jnp.dot(hidden, full_qkv, preferred_element_type=jnp.float32).astype(jnp.bfloat16)
    lanes_out = jnp.concatenate(
        [packed.reshape(windows, OWN, 3, heads, HD), cotangent.reshape(windows, OWN, 1, heads, HD)],
        axis=2,
    ).transpose(3, 0, 1, 2, 4).reshape(heads, windows, OWN, 4 * HD)
    lanes = lax.all_to_all(lanes_out, "space", split_axis=0, concat_axis=0, tiled=True)
    grads = attention_grads(lanes)
    returned = lax.all_to_all(grads, "space", split_axis=0, concat_axis=0, tiled=True)
    d_packed = (
        returned.reshape(heads, windows, OWN, 3, HD)
        .transpose(1, 2, 3, 0, 4)
        .reshape(row_total, 3 * D)
    )
    my_rows = lax.psum_scatter(
        contract(hidden, d_packed, 0, 0).astype(jnp.bfloat16),
        "space",
        scatter_dimension=0,
        tiled=True,
    )
    row_block = my_rows.shape[0]
    col_block = 3 * D // tm_count
    qkv_parts = lax.all_to_all(
        my_rows.reshape(row_block, tm_count, col_block).transpose(1, 0, 2),
        "tm",
        split_axis=0,
        concat_axis=0,
        tiled=True,
    )
    d_qkv_weight = jnp.sum(qkv_parts.astype(jnp.float32), axis=0)
    d_hidden = contract(d_packed, full_qkv, 1, 1)
    first_mean = jnp.mean(d_hidden, axis=1, keepdims=True)
    second_mean = jnp.mean(d_hidden * normed, axis=1, keepdims=True)
    d_tokens = (inverse * (d_hidden - first_mean - normed * second_mean)).astype(jnp.bfloat16)
    embed_partial = contract(chosen, d_tokens, 0, 0)
    embed_block = D // tm_count
    embed_parts = lax.all_to_all(
        embed_partial.astype(jnp.bfloat16).reshape(PATCH, tm_count, embed_block).transpose(1, 0, 2),
        "tm",
        split_axis=0,
        concat_axis=0,
        tiled=True,
    )
    embed_cols = jnp.sum(embed_parts.astype(jnp.float32), axis=0)
    chunk = -(-PATCH // slab_count)
    padded = jnp.pad(embed_cols, ((0, chunk * slab_count - PATCH), (0, 0)))
    spread = lax.all_to_all(
        padded.reshape(slab_count, chunk, -1), "space", split_axis=0, concat_axis=0, tiled=True
    )
    reduced = jnp.sum(spread, axis=0)
    gathered = lax.all_to_all(
        jnp.broadcast_to(reduced[None], (slab_count,) + reduced.shape),
        "space",
        split_axis=0,
        concat_axis=0,
        tiled=True,
    )
    d_embed_weight = (
        gathered.reshape(chunk * slab_count, -1)[:PATCH]
        .reshape(4, 6, 6, 6, -1)
        .transpose(0, 2, 3, 1, 4)
        .reshape(PATCH, -1)
    )
    return (d_qkv_weight, d_embed_weight)


def solution(mesh):
    placed = (
        P(None, "tm", "space", None),
        P(None, "space"),
        P(None, "space"),
        P(None, "tm"),
        P("space", "tm"),
        P(None, "tm", "space", None),
    )
    return jax.shard_map(
        body,
        mesh=mesh,
        in_specs=placed,
        out_specs=(P("space", "tm"), P(None, "tm")),
        check_vma=False,
    )
```

```python
import jax
import jax.numpy as jnp
from jax import lax
from jax.sharding import PartitionSpec as P
from jax.experimental import pallas as pl
from jax.experimental.pallas import tpu as pltpu

D = 1024
HD = 64
PATCH = 864
GY = 96
GZ = 96
OWN = 128
PSLAB = 256


def for_sending(array):

    def short(part):
        return part.astype(jnp.bfloat16) if part.dtype == jnp.float32 else part

    return jax.tree.map(short, array)


def contract(left, right, left_dim, right_dim):
    return lax.dot_general(
        left, right, (((left_dim,), (right_dim,)), ((), ())), preferred_element_type=jnp.float32
    )


def select(onehot, rows):
    return jnp.einsum("wab,wbc->wac", onehot, rows, preferred_element_type=jnp.float32)


def bucket_index(slots, slab_count, capacity):
    entries = slots.shape[-1]
    owner_of = jnp.where(slots >= 0, slots // OWN, slab_count)
    hits = (owner_of[..., None] == jnp.arange(slab_count, dtype=jnp.int32)).astype(jnp.bfloat16)
    order = jnp.arange(entries, dtype=jnp.int32)
    before = (order[None, :] < order[:, None]).astype(jnp.bfloat16)
    earlier = jnp.einsum("ij,wjo->wio", before, hits, preferred_element_type=jnp.float32)
    position = jnp.sum(earlier * hits.astype(jnp.float32), axis=-1).astype(jnp.int32)
    return jnp.where(slots >= 0, owner_of * capacity + position, slab_count * capacity)


def patch_kernel(rows_ref, pick_ref, keep_ref, fold_ref, out_ref):
    frames = rows_ref.shape[1]
    depth = fold_ref.shape[0] // 6
    lanes_b = out_ref.shape[1]
    span = 6 * fold_ref.shape[0]
    keep = keep_ref[0].astype(jnp.float32)[None]
    for frame in range(frames):
        by_z = jnp.dot(rows_ref[0, frame], pick_ref[0], preferred_element_type=jnp.float32)
        rows_per = by_z.shape[0] // depth
        masked = (by_z.reshape(depth, rows_per, -1) * keep).reshape(depth * rows_per, -1)
        by_y = contract(masked.astype(jnp.bfloat16), fold_ref[...], 0, 1)
        for inner in range(6):
            start = frame * span + inner * fold_ref.shape[0]
            out_ref[0, :, start : start + fold_ref.shape[0]] = by_y[
                inner * lanes_b : (inner + 1) * lanes_b
            ].astype(out_ref.dtype)


def patch_columns(rows, pick_z, keep_y, fold):
    windows = rows.shape[0]
    lanes_b = pick_z.shape[2] // 6
    return pl.pallas_call(
        patch_kernel,
        grid=(windows,),
        in_specs=[
            pl.BlockSpec((1,) + rows.shape[1:], lambda w: (w, 0, 0, 0)),
            pl.BlockSpec((1,) + pick_z.shape[1:], lambda w: (w, 0, 0)),
            pl.BlockSpec((1,) + keep_y.shape[1:], lambda w: (w, 0, 0)),
            pl.BlockSpec(fold.shape, lambda w: (0, 0)),
        ],
        out_specs=pl.BlockSpec((1, lanes_b, PATCH), lambda w: (w, 0, 0)),
        out_shape=jax.ShapeDtypeStruct((windows, lanes_b, PATCH), jnp.bfloat16),
        compiler_params=pltpu.CompilerParams(
            dimension_semantics=("arbitrary",),
            vmem_limit_bytes=48 * 1024 * 1024,
        ),
        cost_estimate=pl.CostEstimate(
            flops=2 * rows.shape[0] * rows.shape[1] * rows.shape[2] * pick_z.shape[1] * pick_z.shape[2] * 2,
            transcendentals=0,
            bytes_accessed=rows.size * 2 + windows * lanes_b * PATCH * 2,
        ),
    )(rows, pick_z, keep_y, fold)


QUERY_BLOCK = 512


def attention_kernel(lanes_ref, out_ref, k_s, v_s, dk_acc, dv_acc):
    step = pl.program_id(1)
    owners, _, slots, _ = lanes_ref.shape
    per_block = max(1, QUERY_BLOCK // slots)
    length = owners * slots
    block = per_block * slots
    factor = HD ** (-0.5)

    @pl.when(step == 0)
    def _():
        k_s[...] = lanes_ref[:, 0, :, HD : 2 * HD].reshape(length, HD)
        v_s[...] = lanes_ref[:, 0, :, 2 * HD : 3 * HD].reshape(length, HD)
        dk_acc[...] = jnp.zeros_like(dk_acc)
        dv_acc[...] = jnp.zeros_like(dv_acc)

    first = pl.multiple_of(step * per_block, per_block)
    queries = lanes_ref[pl.ds(first, per_block), 0, :, 0:HD].reshape(block, HD)
    upstream = lanes_ref[pl.ds(first, per_block), 0, :, 3 * HD : 4 * HD].reshape(block, HD)
    key_rows = k_s[...]
    value_rows = v_s[...]
    scores = contract(queries * jnp.asarray(factor, queries.dtype), key_rows, 1, 1)
    raised = jnp.exp(scores - jnp.max(scores, axis=1, keepdims=True))
    attention = raised * (1.0 / jnp.sum(raised, axis=1, keepdims=True))
    d_attention = contract(upstream, value_rows, 1, 1)
    inner_sum = jnp.sum(attention * d_attention, axis=1, keepdims=True)
    d_scores = (attention * (d_attention - inner_sum)).astype(jnp.bfloat16)
    grad_query = contract(d_scores, key_rows, 1, 0) * factor
    out_ref[pl.ds(first, per_block), 0, :, 0:HD] = grad_query.astype(jnp.bfloat16).reshape(
        per_block, slots, HD
    )
    dk_acc[...] += contract(d_scores, queries, 0, 0)
    dv_acc[...] += contract(attention.astype(jnp.bfloat16), upstream, 0, 0)

    @pl.when(step == pl.num_programs(1) - 1)
    def _():
        out_ref[:, 0, :, HD : 2 * HD] = (dk_acc[...] * factor).astype(jnp.bfloat16).reshape(
            owners, slots, HD
        )
        out_ref[:, 0, :, 2 * HD : 3 * HD] = dv_acc[...].astype(jnp.bfloat16).reshape(owners, slots, HD)


def attention_grads(lanes):
    owners, windows, slots, width = lanes.shape
    length = owners * slots
    per_block = max(1, QUERY_BLOCK // slots)
    lanes_spec = pl.BlockSpec((owners, 1, slots, width), lambda w, i: (0, w, 0, 0))
    out_spec = pl.BlockSpec((owners, 1, slots, 3 * HD), lambda w, i: (0, w, 0, 0))
    flops = 10 * windows * length * length * HD
    return pl.pallas_call(
        attention_kernel,
        grid=(windows, owners // per_block),
        in_specs=[lanes_spec],
        out_specs=out_spec,
        out_shape=jax.ShapeDtypeStruct((owners, windows, slots, 3 * HD), jnp.bfloat16),
        scratch_shapes=[
            pltpu.VMEM((length, HD), jnp.bfloat16),
            pltpu.VMEM((length, HD), jnp.bfloat16),
            pltpu.VMEM((length, HD), jnp.float32),
            pltpu.VMEM((length, HD), jnp.float32),
        ],
        compiler_params=pltpu.CompilerParams(
            dimension_semantics=("arbitrary", "arbitrary"),
            vmem_limit_bytes=48 * 1024 * 1024,
        ),
        cost_estimate=pl.CostEstimate(
            flops=flops,
            transcendentals=windows * length * length,
            bytes_accessed=7 * windows * length * HD * 2,
        ),
    )(lanes)


def body(voxels, brain_list, owner_slot, embed_weight, qkv_weight, cotangent):
    slab_count = lax.axis_size("space")
    tm_count = lax.axis_size("tm")
    capacity = 3 * OWN // (2 * slab_count)
    buckets = slab_count * capacity
    windows = voxels.shape[0]
    row_total = windows * OWN
    side_y = GY // 6
    side_z = GZ // 6
    frames = voxels.shape[1]
    depth = voxels.shape[2]
    lanes_b = -(-buckets // 128) * 128
    my_buckets = bucket_index(owner_slot, slab_count, capacity)
    to_bucket = (
        my_buckets[:, None, :] == jnp.arange(lanes_b, dtype=jnp.int32)[None, :, None]
    ).astype(jnp.bfloat16)
    slot_code = (jnp.where(owner_slot >= 0, owner_slot % OWN, -1) + 1).astype(jnp.bfloat16)
    bucket_code = select(to_bucket, slot_code[:, :, None])[:, :buckets]
    patch_code = select(to_bucket, (brain_list + 1).astype(jnp.float32)[:, :, None].astype(jnp.bfloat16))
    patch_of = patch_code[:, :, 0].astype(jnp.int32) - 1
    py_of = jnp.where(patch_of >= 0, patch_of // side_z, -1)
    pz_of = jnp.where(patch_of >= 0, patch_of % side_z, -1)
    z_index = jnp.arange(GZ, dtype=jnp.int32)
    inner = jnp.arange(6, dtype=jnp.int32)
    pick_z = (
        z_index[None, :, None, None]
        == pz_of[:, None, None, :] * 6 + inner[None, None, :, None]
    ).astype(jnp.bfloat16).reshape(windows, GZ, 6 * lanes_b)
    rows = voxels.reshape(windows, frames, depth * GY, GZ)
    y_index = jnp.arange(GY, dtype=jnp.int32)
    keep_y = jnp.broadcast_to(
        (y_index[None, :, None, None] // 6 == py_of[:, None, None, :]),
        (windows, GY, 6, lanes_b),
    ).astype(jnp.bfloat16).reshape(windows, GY, 6 * lanes_b)
    slab_x = jnp.arange(depth, dtype=jnp.int32)
    fold = (
        (slab_x[:, None, None, None] == slab_x[None, None, :, None])
        & (inner[None, :, None, None] == y_index[None, None, None, :] % 6)
    ).astype(jnp.bfloat16).reshape(depth * 6, depth * GY)
    picked = patch_columns(rows, pick_z, keep_y, fold)
    width = -(-(PATCH + 1) // 128) * 128
    payload = jnp.concatenate(
        [
            picked[:, :buckets],
            bucket_code.astype(jnp.bfloat16),
            jnp.zeros((windows, buckets, width - PATCH - 1), jnp.bfloat16),
        ],
        axis=2,
    ).reshape(windows, slab_count, capacity, width)
    arrived = lax.all_to_all(payload, "space", split_axis=1, concat_axis=1, tiled=True).reshape(
        windows, buckets, width
    )
    arrival_slot = arrived[:, :, PATCH].astype(jnp.int32) - 1
    to_slot = (
        arrival_slot[:, None, :] == jnp.arange(OWN, dtype=jnp.int32)[None, :, None]
    ).astype(jnp.bfloat16)
    chosen = select(to_slot, arrived[:, :, :PATCH]).astype(jnp.bfloat16).reshape(row_total, PATCH)
    local_embed = (
        embed_weight.reshape(4, 6, 6, 6, -1).transpose(0, 3, 1, 2, 4).reshape(PATCH, -1)
    )
    embed_blocks = lax.all_to_all(
        jnp.broadcast_to(local_embed[None], (tm_count,) + local_embed.shape),
        "tm",
        split_axis=0,
        concat_axis=0,
        tiled=True,
    )
    tokens = (
        jnp.einsum("nr,trc->ntc", chosen, embed_blocks, preferred_element_type=jnp.float32)
        .astype(jnp.bfloat16)
        .reshape(row_total, D)
    )
    widened = tokens.astype(jnp.float32)
    center = widened - jnp.mean(widened, axis=1, keepdims=True)
    inverse = lax.rsqrt(jnp.mean(center * center, axis=1, keepdims=True) + 1e-05)
    normed = center * inverse
    hidden = normed.astype(jnp.bfloat16)
    wide_rows = lax.all_gather(qkv_weight, "tm", axis=1, tiled=True)
    full_qkv = lax.all_gather(wide_rows, "space", axis=0, tiled=True)
    heads = D // HD
    packed = jnp.dot(hidden, full_qkv, preferred_element_type=jnp.float32).astype(jnp.bfloat16)
    lanes_out = jnp.concatenate(
        [packed.reshape(windows, OWN, 3, heads, HD), cotangent.reshape(windows, OWN, 1, heads, HD)],
        axis=2,
    ).transpose(3, 0, 1, 2, 4).reshape(heads, windows, OWN, 4 * HD)
    lanes = lax.all_to_all(lanes_out, "space", split_axis=0, concat_axis=0, tiled=True)
    returned = jnp.concatenate(
        [
            lax.all_to_all(
                attention_grads(lanes[:, window : window + 1]),
                "space",
                split_axis=0,
                concat_axis=0,
                tiled=True,
            )
            for window in range(windows)
        ],
        axis=1,
    )
    d_packed = (
        returned.reshape(heads, windows, OWN, 3, HD)
        .transpose(1, 2, 3, 0, 4)
        .reshape(row_total, 3 * D)
    )
    my_rows = lax.psum_scatter(
        contract(hidden, d_packed, 0, 0).astype(jnp.bfloat16),
        "space",
        scatter_dimension=0,
        tiled=True,
    )
    row_block = my_rows.shape[0]
    col_block = 3 * D // tm_count
    qkv_parts = lax.all_to_all(
        my_rows.reshape(row_block, tm_count, col_block).transpose(1, 0, 2),
        "tm",
        split_axis=0,
        concat_axis=0,
        tiled=True,
    )
    d_qkv_weight = jnp.sum(qkv_parts.astype(jnp.float32), axis=0)
    d_hidden = contract(d_packed, full_qkv, 1, 1)
    first_mean = jnp.mean(d_hidden, axis=1, keepdims=True)
    second_mean = jnp.mean(d_hidden * normed, axis=1, keepdims=True)
    d_tokens = (inverse * (d_hidden - first_mean - normed * second_mean)).astype(jnp.bfloat16)
    embed_partial = contract(chosen, d_tokens, 0, 0)
    embed_block = D // tm_count
    embed_parts = lax.all_to_all(
        embed_partial.astype(jnp.bfloat16).reshape(PATCH, tm_count, embed_block).transpose(1, 0, 2),
        "tm",
        split_axis=0,
        concat_axis=0,
        tiled=True,
    )
    embed_cols = jnp.sum(embed_parts.astype(jnp.float32), axis=0)
    chunk = -(-PATCH // slab_count)
    padded = jnp.pad(embed_cols, ((0, chunk * slab_count - PATCH), (0, 0)))
    spread = lax.all_to_all(
        padded.reshape(slab_count, chunk, -1), "space", split_axis=0, concat_axis=0, tiled=True
    )
    reduced = jnp.sum(spread, axis=0)
    gathered = lax.all_to_all(
        jnp.broadcast_to(reduced[None], (slab_count,) + reduced.shape),
        "space",
        split_axis=0,
        concat_axis=0,
        tiled=True,
    )
    d_embed_weight = (
        gathered.reshape(chunk * slab_count, -1)[:PATCH]
        .reshape(4, 6, 6, 6, -1)
        .transpose(0, 2, 3, 1, 4)
        .reshape(PATCH, -1)
    )
    return (d_qkv_weight, d_embed_weight)


def solution(mesh):
    placed = (
        P(None, "tm", "space", None),
        P(None, "space"),
        P(None, "space"),
        P(None, "tm"),
        P("space", "tm"),
        P(None, "tm", "space", None),
    )
    return jax.shard_map(
        body,
        mesh=mesh,
        in_specs=placed,
        out_specs=(P("space", "tm"), P(None, "tm")),
        check_vma=False,
    )
```

```python
import jax
import jax.numpy as jnp
from jax import lax
from jax.sharding import PartitionSpec as P
from jax.experimental import pallas as pl
from jax.experimental.pallas import tpu as pltpu

D = 1024
HD = 64
PATCH = 864
GY = 96
GZ = 96
OWN = 128
PSLAB = 256


def for_sending(array):

    def short(part):
        return part.astype(jnp.bfloat16) if part.dtype == jnp.float32 else part

    return jax.tree.map(short, array)


def contract(left, right, left_dim, right_dim):
    return lax.dot_general(
        left, right, (((left_dim,), (right_dim,)), ((), ())), preferred_element_type=jnp.float32
    )


def select(onehot, rows):
    return jnp.einsum("wab,wbc->wac", onehot, rows, preferred_element_type=jnp.float32)


def bucket_index(slots, slab_count, capacity):
    entries = slots.shape[-1]
    owner_of = jnp.where(slots >= 0, slots // OWN, slab_count)
    hits = (owner_of[..., None] == jnp.arange(slab_count, dtype=jnp.int32)).astype(jnp.bfloat16)
    order = jnp.arange(entries, dtype=jnp.int32)
    before = (order[None, :] < order[:, None]).astype(jnp.bfloat16)
    earlier = jnp.einsum("ij,wjo->wio", before, hits, preferred_element_type=jnp.float32)
    position = jnp.sum(earlier * hits.astype(jnp.float32), axis=-1).astype(jnp.int32)
    return jnp.where(slots >= 0, owner_of * capacity + position, slab_count * capacity)


def patch_kernel(rows_ref, pick_ref, keep_ref, fold_ref, out_ref):
    frames = rows_ref.shape[1]
    depth = fold_ref.shape[0] // 6
    lanes_b = out_ref.shape[1]
    span = 6 * fold_ref.shape[0]
    keep = keep_ref[0].astype(jnp.float32)[None]
    for frame in range(frames):
        by_z = jnp.dot(rows_ref[0, frame], pick_ref[0], preferred_element_type=jnp.float32)
        rows_per = by_z.shape[0] // depth
        masked = (by_z.reshape(depth, rows_per, -1) * keep).reshape(depth * rows_per, -1)
        by_y = contract(masked.astype(jnp.bfloat16), fold_ref[...], 0, 1)
        for inner in range(6):
            start = frame * span + inner * fold_ref.shape[0]
            out_ref[0, :, start : start + fold_ref.shape[0]] = by_y[
                inner * lanes_b : (inner + 1) * lanes_b
            ].astype(out_ref.dtype)


def patch_columns(rows, pick_z, keep_y, fold):
    windows = rows.shape[0]
    lanes_b = pick_z.shape[2] // 6
    return pl.pallas_call(
        patch_kernel,
        grid=(windows,),
        in_specs=[
            pl.BlockSpec((1,) + rows.shape[1:], lambda w: (w, 0, 0, 0)),
            pl.BlockSpec((1,) + pick_z.shape[1:], lambda w: (w, 0, 0)),
            pl.BlockSpec((1,) + keep_y.shape[1:], lambda w: (w, 0, 0)),
            pl.BlockSpec(fold.shape, lambda w: (0, 0)),
        ],
        out_specs=pl.BlockSpec((1, lanes_b, PATCH), lambda w: (w, 0, 0)),
        out_shape=jax.ShapeDtypeStruct((windows, lanes_b, PATCH), jnp.bfloat16),
        compiler_params=pltpu.CompilerParams(
            dimension_semantics=("arbitrary",),
            vmem_limit_bytes=48 * 1024 * 1024,
        ),
        cost_estimate=pl.CostEstimate(
            flops=2 * rows.shape[0] * rows.shape[1] * rows.shape[2] * pick_z.shape[1] * pick_z.shape[2] * 2,
            transcendentals=0,
            bytes_accessed=rows.size * 2 + windows * lanes_b * PATCH * 2,
        ),
    )(rows, pick_z, keep_y, fold)


QUERY_BLOCK = 512


def attention_kernel(lanes_ref, out_ref, k_s, v_s, dk_acc, dv_acc):
    step = pl.program_id(1)
    owners, _, slots, _ = lanes_ref.shape
    per_block = max(1, QUERY_BLOCK // slots)
    length = owners * slots
    block = per_block * slots
    factor = HD ** (-0.5)

    @pl.when(step == 0)
    def _():
        k_s[...] = lanes_ref[:, 0, :, HD : 2 * HD].reshape(length, HD)
        v_s[...] = lanes_ref[:, 0, :, 2 * HD : 3 * HD].reshape(length, HD)
        dk_acc[...] = jnp.zeros_like(dk_acc)
        dv_acc[...] = jnp.zeros_like(dv_acc)

    first = pl.multiple_of(step * per_block, per_block)
    queries = lanes_ref[pl.ds(first, per_block), 0, :, 0:HD].reshape(block, HD)
    upstream = lanes_ref[pl.ds(first, per_block), 0, :, 3 * HD : 4 * HD].reshape(block, HD)
    key_rows = k_s[...]
    value_rows = v_s[...]
    scores = contract(queries * jnp.asarray(factor, queries.dtype), key_rows, 1, 1)
    raised = jnp.exp(scores - jnp.max(scores, axis=1, keepdims=True))
    attention = raised * (1.0 / jnp.sum(raised, axis=1, keepdims=True))
    d_attention = contract(upstream, value_rows, 1, 1)
    inner_sum = jnp.sum(attention * d_attention, axis=1, keepdims=True)
    d_scores = (attention * (d_attention - inner_sum)).astype(jnp.bfloat16)
    grad_query = contract(d_scores, key_rows, 1, 0) * factor
    out_ref[pl.ds(first, per_block), 0, :, 0:HD] = grad_query.astype(jnp.bfloat16).reshape(
        per_block, slots, HD
    )
    dk_acc[...] += contract(d_scores, queries, 0, 0)
    dv_acc[...] += contract(attention.astype(jnp.bfloat16), upstream, 0, 0)

    @pl.when(step == pl.num_programs(1) - 1)
    def _():
        out_ref[:, 0, :, HD : 2 * HD] = (dk_acc[...] * factor).astype(jnp.bfloat16).reshape(
            owners, slots, HD
        )
        out_ref[:, 0, :, 2 * HD : 3 * HD] = dv_acc[...].astype(jnp.bfloat16).reshape(owners, slots, HD)


def attention_grads(lanes):
    owners, windows, slots, width = lanes.shape
    length = owners * slots
    per_block = max(1, QUERY_BLOCK // slots)
    lanes_spec = pl.BlockSpec((owners, 1, slots, width), lambda w, i: (0, w, 0, 0))
    out_spec = pl.BlockSpec((owners, 1, slots, 3 * HD), lambda w, i: (0, w, 0, 0))
    flops = 10 * windows * length * length * HD
    return pl.pallas_call(
        attention_kernel,
        grid=(windows, owners // per_block),
        in_specs=[lanes_spec],
        out_specs=out_spec,
        out_shape=jax.ShapeDtypeStruct((owners, windows, slots, 3 * HD), jnp.bfloat16),
        scratch_shapes=[
            pltpu.VMEM((length, HD), jnp.bfloat16),
            pltpu.VMEM((length, HD), jnp.bfloat16),
            pltpu.VMEM((length, HD), jnp.float32),
            pltpu.VMEM((length, HD), jnp.float32),
        ],
        compiler_params=pltpu.CompilerParams(
            dimension_semantics=("arbitrary", "arbitrary"),
            vmem_limit_bytes=48 * 1024 * 1024,
        ),
        cost_estimate=pl.CostEstimate(
            flops=flops,
            transcendentals=windows * length * length,
            bytes_accessed=7 * windows * length * HD * 2,
        ),
    )(lanes)


def body(voxels, brain_list, owner_slot, embed_weight, qkv_weight, cotangent):
    slab_count = lax.axis_size("space")
    tm_count = lax.axis_size("tm")
    capacity = 3 * OWN // (2 * slab_count)
    buckets = slab_count * capacity
    windows = voxels.shape[0]
    row_total = windows * OWN
    side_y = GY // 6
    side_z = GZ // 6
    frames = voxels.shape[1]
    depth = voxels.shape[2]
    lanes_b = -(-buckets // 128) * 128
    my_buckets = bucket_index(owner_slot, slab_count, capacity)
    to_bucket = (
        my_buckets[:, None, :] == jnp.arange(lanes_b, dtype=jnp.int32)[None, :, None]
    ).astype(jnp.bfloat16)
    slot_code = (jnp.where(owner_slot >= 0, owner_slot % OWN, -1) + 1).astype(jnp.bfloat16)
    bucket_code = select(to_bucket, slot_code[:, :, None])[:, :buckets]
    patch_code = select(to_bucket, (brain_list + 1).astype(jnp.float32)[:, :, None].astype(jnp.bfloat16))
    patch_of = patch_code[:, :, 0].astype(jnp.int32) - 1
    py_of = jnp.where(patch_of >= 0, patch_of // side_z, -1)
    pz_of = jnp.where(patch_of >= 0, patch_of % side_z, -1)
    z_index = jnp.arange(GZ, dtype=jnp.int32)
    inner = jnp.arange(6, dtype=jnp.int32)
    pick_z = (
        z_index[None, :, None, None]
        == pz_of[:, None, None, :] * 6 + inner[None, None, :, None]
    ).astype(jnp.bfloat16).reshape(windows, GZ, 6 * lanes_b)
    rows = voxels.reshape(windows, frames, depth * GY, GZ)
    y_index = jnp.arange(GY, dtype=jnp.int32)
    keep_y = jnp.broadcast_to(
        (y_index[None, :, None, None] // 6 == py_of[:, None, None, :]),
        (windows, GY, 6, lanes_b),
    ).astype(jnp.bfloat16).reshape(windows, GY, 6 * lanes_b)
    slab_x = jnp.arange(depth, dtype=jnp.int32)
    fold = (
        (slab_x[:, None, None, None] == slab_x[None, None, :, None])
        & (inner[None, :, None, None] == y_index[None, None, None, :] % 6)
    ).astype(jnp.bfloat16).reshape(depth * 6, depth * GY)
    picked = patch_columns(rows, pick_z, keep_y, fold)
    width = -(-(PATCH + 1) // 128) * 128
    payload = jnp.concatenate(
        [
            picked[:, :buckets],
            bucket_code.astype(jnp.bfloat16),
            jnp.zeros((windows, buckets, width - PATCH - 1), jnp.bfloat16),
        ],
        axis=2,
    ).reshape(windows, slab_count, capacity, width)
    arrived = lax.all_to_all(payload, "space", split_axis=1, concat_axis=1, tiled=True).reshape(
        windows, buckets, width
    )
    arrival_slot = arrived[:, :, PATCH].astype(jnp.int32) - 1
    to_slot = (
        arrival_slot[:, None, :] == jnp.arange(OWN, dtype=jnp.int32)[None, :, None]
    ).astype(jnp.bfloat16)
    chosen = select(to_slot, arrived[:, :, :PATCH]).astype(jnp.bfloat16).reshape(row_total, PATCH)
    local_embed = (
        embed_weight.reshape(4, 6, 6, 6, -1).transpose(0, 3, 1, 2, 4).reshape(PATCH, -1)
    )
    embed_blocks = lax.all_to_all(
        jnp.broadcast_to(local_embed[None], (tm_count,) + local_embed.shape),
        "tm",
        split_axis=0,
        concat_axis=0,
        tiled=True,
    )
    tokens = (
        jnp.einsum("nr,trc->ntc", chosen, embed_blocks, preferred_element_type=jnp.float32)
        .astype(jnp.bfloat16)
        .reshape(row_total, D)
    )
    widened = tokens.astype(jnp.float32)
    center = widened - jnp.mean(widened, axis=1, keepdims=True)
    inverse = lax.rsqrt(jnp.mean(center * center, axis=1, keepdims=True) + 1e-05)
    normed = center * inverse
    hidden = normed.astype(jnp.bfloat16)
    wide_rows = (
        lax.all_to_all(
            jnp.broadcast_to(qkv_weight[None], (tm_count,) + qkv_weight.shape),
            "tm",
            split_axis=0,
            concat_axis=0,
            tiled=True,
        )
        .transpose(1, 0, 2)
        .reshape(qkv_weight.shape[0], -1)
    )
    full_qkv = lax.all_gather(wide_rows, "space", axis=0, tiled=True)
    heads = D // HD
    packed = jnp.dot(hidden, full_qkv, preferred_element_type=jnp.float32).astype(jnp.bfloat16)
    lanes_out = jnp.concatenate(
        [packed.reshape(windows, OWN, 3, heads, HD), cotangent.reshape(windows, OWN, 1, heads, HD)],
        axis=2,
    ).transpose(3, 0, 1, 2, 4).reshape(heads, windows, OWN, 4 * HD)
    lanes = lax.all_to_all(lanes_out, "space", split_axis=0, concat_axis=0, tiled=True)
    grads = attention_grads(lanes)
    returned = lax.all_to_all(grads, "space", split_axis=0, concat_axis=0, tiled=True)
    d_packed = (
        returned.reshape(heads, windows, OWN, 3, HD)
        .transpose(1, 2, 3, 0, 4)
        .reshape(row_total, 3 * D)
    )
    my_rows = lax.psum_scatter(
        contract(hidden, d_packed, 0, 0).astype(jnp.bfloat16),
        "space",
        scatter_dimension=0,
        tiled=True,
    )
    row_block = my_rows.shape[0]
    col_block = 3 * D // tm_count
    qkv_parts = lax.all_to_all(
        my_rows.reshape(row_block, tm_count, col_block).transpose(1, 0, 2),
        "tm",
        split_axis=0,
        concat_axis=0,
        tiled=True,
    )
    d_qkv_weight = jnp.sum(qkv_parts.astype(jnp.float32), axis=0)
    d_hidden = contract(d_packed, full_qkv, 1, 1)
    first_mean = jnp.mean(d_hidden, axis=1, keepdims=True)
    second_mean = jnp.mean(d_hidden * normed, axis=1, keepdims=True)
    d_tokens = (inverse * (d_hidden - first_mean - normed * second_mean)).astype(jnp.bfloat16)
    embed_partial = contract(chosen, d_tokens, 0, 0)
    embed_block = D // tm_count
    embed_parts = lax.all_to_all(
        embed_partial.astype(jnp.bfloat16).reshape(PATCH, tm_count, embed_block).transpose(1, 0, 2),
        "tm",
        split_axis=0,
        concat_axis=0,
        tiled=True,
    )
    embed_cols = jnp.sum(embed_parts.astype(jnp.float32), axis=0)
    chunk = -(-PATCH // slab_count)
    padded = jnp.pad(embed_cols, ((0, chunk * slab_count - PATCH), (0, 0)))
    spread = lax.all_to_all(
        padded.reshape(slab_count, chunk, -1), "space", split_axis=0, concat_axis=0, tiled=True
    )
    reduced = jnp.sum(spread, axis=0)
    gathered = lax.all_to_all(
        jnp.broadcast_to(reduced[None], (slab_count,) + reduced.shape),
        "space",
        split_axis=0,
        concat_axis=0,
        tiled=True,
    )
    d_embed_weight = (
        gathered.reshape(chunk * slab_count, -1)[:PATCH]
        .reshape(4, 6, 6, 6, -1)
        .transpose(0, 2, 3, 1, 4)
        .reshape(PATCH, -1)
    )
    return (d_qkv_weight, d_embed_weight)


def solution(mesh):
    placed = (
        P(None, "tm", "space", None),
        P(None, "space"),
        P(None, "space"),
        P(None, "tm"),
        P("space", "tm"),
        P(None, "tm", "space", None),
    )
    return jax.shard_map(
        body,
        mesh=mesh,
        in_specs=placed,
        out_specs=(P("space", "tm"), P(None, "tm")),
        check_vma=False,
    )
```

```python
import jax
import jax.numpy as jnp
from jax import lax
from jax.sharding import PartitionSpec as P
from jax.experimental import pallas as pl
from jax.experimental.pallas import tpu as pltpu

D = 1024
HD = 64
PATCH = 864
GY = 96
GZ = 96
OWN = 128
PSLAB = 256


def for_sending(array):

    def short(part):
        return part.astype(jnp.bfloat16) if part.dtype == jnp.float32 else part

    return jax.tree.map(short, array)


def contract(left, right, left_dim, right_dim):
    return lax.dot_general(
        left, right, (((left_dim,), (right_dim,)), ((), ())), preferred_element_type=jnp.float32
    )


def select(onehot, rows):
    return jnp.einsum("wab,wbc->wac", onehot, rows, preferred_element_type=jnp.float32)


def bucket_index(slots, slab_count, capacity):
    entries = slots.shape[-1]
    owner_of = jnp.where(slots >= 0, slots // OWN, slab_count)
    hits = (owner_of[..., None] == jnp.arange(slab_count, dtype=jnp.int32)).astype(jnp.bfloat16)
    order = jnp.arange(entries, dtype=jnp.int32)
    before = (order[None, :] < order[:, None]).astype(jnp.bfloat16)
    earlier = jnp.einsum("ij,wjo->wio", before, hits, preferred_element_type=jnp.float32)
    position = jnp.sum(earlier * hits.astype(jnp.float32), axis=-1).astype(jnp.int32)
    return jnp.where(slots >= 0, owner_of * capacity + position, slab_count * capacity)


def patch_kernel(rows_ref, pick_ref, keep_ref, fold_ref, out_ref):
    frames = rows_ref.shape[1]
    depth = fold_ref.shape[0] // 6
    lanes_b = out_ref.shape[1]
    span = 6 * fold_ref.shape[0]
    keep = keep_ref[0].astype(jnp.float32)[None]
    for frame in range(frames):
        by_z = jnp.dot(rows_ref[0, frame], pick_ref[0], preferred_element_type=jnp.float32)
        rows_per = by_z.shape[0] // depth
        masked = (by_z.reshape(depth, rows_per, -1) * keep).reshape(depth * rows_per, -1)
        by_y = contract(masked.astype(jnp.bfloat16), fold_ref[...], 0, 1)
        for inner in range(6):
            start = frame * span + inner * fold_ref.shape[0]
            out_ref[0, :, start : start + fold_ref.shape[0]] = by_y[
                inner * lanes_b : (inner + 1) * lanes_b
            ].astype(out_ref.dtype)


def patch_columns(rows, pick_z, keep_y, fold):
    windows = rows.shape[0]
    lanes_b = pick_z.shape[2] // 6
    return pl.pallas_call(
        patch_kernel,
        grid=(windows,),
        in_specs=[
            pl.BlockSpec((1,) + rows.shape[1:], lambda w: (w, 0, 0, 0)),
            pl.BlockSpec((1,) + pick_z.shape[1:], lambda w: (w, 0, 0)),
            pl.BlockSpec((1,) + keep_y.shape[1:], lambda w: (w, 0, 0)),
            pl.BlockSpec(fold.shape, lambda w: (0, 0)),
        ],
        out_specs=pl.BlockSpec((1, lanes_b, PATCH), lambda w: (w, 0, 0)),
        out_shape=jax.ShapeDtypeStruct((windows, lanes_b, PATCH), jnp.bfloat16),
        compiler_params=pltpu.CompilerParams(
            dimension_semantics=("arbitrary",),
            vmem_limit_bytes=48 * 1024 * 1024,
        ),
        cost_estimate=pl.CostEstimate(
            flops=2 * rows.shape[0] * rows.shape[1] * rows.shape[2] * pick_z.shape[1] * pick_z.shape[2] * 2,
            transcendentals=0,
            bytes_accessed=rows.size * 2 + windows * lanes_b * PATCH * 2,
        ),
    )(rows, pick_z, keep_y, fold)


QUERY_BLOCK = 1024


def attention_kernel(lanes_ref, out_ref, k_s, v_s, dk_acc, dv_acc):
    step = pl.program_id(1)
    owners, _, slots, _ = lanes_ref.shape
    per_block = max(1, QUERY_BLOCK // slots)
    length = owners * slots
    block = per_block * slots
    factor = HD ** (-0.5)

    @pl.when(step == 0)
    def _():
        k_s[...] = lanes_ref[:, 0, :, HD : 2 * HD].reshape(length, HD)
        v_s[...] = lanes_ref[:, 0, :, 2 * HD : 3 * HD].reshape(length, HD)
        dk_acc[...] = jnp.zeros_like(dk_acc)
        dv_acc[...] = jnp.zeros_like(dv_acc)

    first = pl.multiple_of(step * per_block, per_block)
    queries = lanes_ref[pl.ds(first, per_block), 0, :, 0:HD].reshape(block, HD)
    upstream = lanes_ref[pl.ds(first, per_block), 0, :, 3 * HD : 4 * HD].reshape(block, HD)
    key_rows = k_s[...]
    value_rows = v_s[...]
    scores = contract(queries * jnp.asarray(factor, queries.dtype), key_rows, 1, 1)
    raised = jnp.exp(scores - jnp.max(scores, axis=1, keepdims=True))
    attention = raised * (1.0 / jnp.sum(raised, axis=1, keepdims=True))
    d_attention = contract(upstream, value_rows, 1, 1)
    inner_sum = jnp.sum(attention * d_attention, axis=1, keepdims=True)
    d_scores = (attention * (d_attention - inner_sum)).astype(jnp.bfloat16)
    grad_query = contract(d_scores, key_rows, 1, 0) * factor
    out_ref[pl.ds(first, per_block), 0, :, 0:HD] = grad_query.astype(jnp.bfloat16).reshape(
        per_block, slots, HD
    )
    dk_acc[...] += contract(d_scores, queries, 0, 0)
    dv_acc[...] += contract(attention.astype(jnp.bfloat16), upstream, 0, 0)

    @pl.when(step == pl.num_programs(1) - 1)
    def _():
        out_ref[:, 0, :, HD : 2 * HD] = (dk_acc[...] * factor).astype(jnp.bfloat16).reshape(
            owners, slots, HD
        )
        out_ref[:, 0, :, 2 * HD : 3 * HD] = dv_acc[...].astype(jnp.bfloat16).reshape(owners, slots, HD)


def attention_grads(lanes):
    owners, windows, slots, width = lanes.shape
    length = owners * slots
    per_block = max(1, QUERY_BLOCK // slots)
    lanes_spec = pl.BlockSpec((owners, 1, slots, width), lambda w, i: (0, w, 0, 0))
    out_spec = pl.BlockSpec((owners, 1, slots, 3 * HD), lambda w, i: (0, w, 0, 0))
    flops = 10 * windows * length * length * HD
    return pl.pallas_call(
        attention_kernel,
        grid=(windows, owners // per_block),
        in_specs=[lanes_spec],
        out_specs=out_spec,
        out_shape=jax.ShapeDtypeStruct((owners, windows, slots, 3 * HD), jnp.bfloat16),
        scratch_shapes=[
            pltpu.VMEM((length, HD), jnp.bfloat16),
            pltpu.VMEM((length, HD), jnp.bfloat16),
            pltpu.VMEM((length, HD), jnp.float32),
            pltpu.VMEM((length, HD), jnp.float32),
        ],
        compiler_params=pltpu.CompilerParams(
            dimension_semantics=("arbitrary", "arbitrary"),
            vmem_limit_bytes=48 * 1024 * 1024,
        ),
        cost_estimate=pl.CostEstimate(
            flops=flops,
            transcendentals=windows * length * length,
            bytes_accessed=7 * windows * length * HD * 2,
        ),
    )(lanes)


def body(voxels, brain_list, owner_slot, embed_weight, qkv_weight, cotangent):
    slab_count = lax.axis_size("space")
    tm_count = lax.axis_size("tm")
    capacity = 3 * OWN // (2 * slab_count)
    buckets = slab_count * capacity
    windows = voxels.shape[0]
    row_total = windows * OWN
    side_y = GY // 6
    side_z = GZ // 6
    frames = voxels.shape[1]
    depth = voxels.shape[2]
    lanes_b = -(-buckets // 128) * 128
    my_buckets = bucket_index(owner_slot, slab_count, capacity)
    to_bucket = (
        my_buckets[:, None, :] == jnp.arange(lanes_b, dtype=jnp.int32)[None, :, None]
    ).astype(jnp.bfloat16)
    slot_code = (jnp.where(owner_slot >= 0, owner_slot % OWN, -1) + 1).astype(jnp.bfloat16)
    bucket_code = select(to_bucket, slot_code[:, :, None])[:, :buckets]
    patch_code = select(to_bucket, (brain_list + 1).astype(jnp.float32)[:, :, None].astype(jnp.bfloat16))
    patch_of = patch_code[:, :, 0].astype(jnp.int32) - 1
    py_of = jnp.where(patch_of >= 0, patch_of // side_z, -1)
    pz_of = jnp.where(patch_of >= 0, patch_of % side_z, -1)
    z_index = jnp.arange(GZ, dtype=jnp.int32)
    inner = jnp.arange(6, dtype=jnp.int32)
    pick_z = (
        z_index[None, :, None, None]
        == pz_of[:, None, None, :] * 6 + inner[None, None, :, None]
    ).astype(jnp.bfloat16).reshape(windows, GZ, 6 * lanes_b)
    rows = voxels.reshape(windows, frames, depth * GY, GZ)
    y_index = jnp.arange(GY, dtype=jnp.int32)
    keep_y = jnp.broadcast_to(
        (y_index[None, :, None, None] // 6 == py_of[:, None, None, :]),
        (windows, GY, 6, lanes_b),
    ).astype(jnp.bfloat16).reshape(windows, GY, 6 * lanes_b)
    slab_x = jnp.arange(depth, dtype=jnp.int32)
    fold = (
        (slab_x[:, None, None, None] == slab_x[None, None, :, None])
        & (inner[None, :, None, None] == y_index[None, None, None, :] % 6)
    ).astype(jnp.bfloat16).reshape(depth * 6, depth * GY)
    picked = patch_columns(rows, pick_z, keep_y, fold)
    width = -(-(PATCH + 1) // 128) * 128
    payload = jnp.concatenate(
        [
            picked[:, :buckets],
            bucket_code.astype(jnp.bfloat16),
            jnp.zeros((windows, buckets, width - PATCH - 1), jnp.bfloat16),
        ],
        axis=2,
    ).reshape(windows, slab_count, capacity, width)
    arrived = lax.all_to_all(payload, "space", split_axis=1, concat_axis=1, tiled=True).reshape(
        windows, buckets, width
    )
    arrival_slot = arrived[:, :, PATCH].astype(jnp.int32) - 1
    to_slot = (
        arrival_slot[:, None, :] == jnp.arange(OWN, dtype=jnp.int32)[None, :, None]
    ).astype(jnp.bfloat16)
    chosen = select(to_slot, arrived[:, :, :PATCH]).astype(jnp.bfloat16).reshape(row_total, PATCH)
    local_embed = (
        embed_weight.reshape(4, 6, 6, 6, -1).transpose(0, 3, 1, 2, 4).reshape(PATCH, -1)
    )
    embed_blocks = lax.all_to_all(
        jnp.broadcast_to(local_embed[None], (tm_count,) + local_embed.shape),
        "tm",
        split_axis=0,
        concat_axis=0,
        tiled=True,
    )
    tokens = (
        jnp.einsum("nr,trc->ntc", chosen, embed_blocks, preferred_element_type=jnp.float32)
        .astype(jnp.bfloat16)
        .reshape(row_total, D)
    )
    widened = tokens.astype(jnp.float32)
    center = widened - jnp.mean(widened, axis=1, keepdims=True)
    inverse = lax.rsqrt(jnp.mean(center * center, axis=1, keepdims=True) + 1e-05)
    normed = center * inverse
    hidden = normed.astype(jnp.bfloat16)
    wide_rows = (
        lax.all_to_all(
            jnp.broadcast_to(qkv_weight[None], (tm_count,) + qkv_weight.shape),
            "tm",
            split_axis=0,
            concat_axis=0,
            tiled=True,
        )
        .transpose(1, 0, 2)
        .reshape(qkv_weight.shape[0], -1)
    )
    full_qkv = lax.all_gather(wide_rows, "space", axis=0, tiled=True)
    heads = D // HD
    packed = jnp.dot(hidden, full_qkv, preferred_element_type=jnp.float32).astype(jnp.bfloat16)
    lanes_out = jnp.concatenate(
        [packed.reshape(windows, OWN, 3, heads, HD), cotangent.reshape(windows, OWN, 1, heads, HD)],
        axis=2,
    ).transpose(3, 0, 1, 2, 4).reshape(heads, windows, OWN, 4 * HD)
    lanes = lax.all_to_all(lanes_out, "space", split_axis=0, concat_axis=0, tiled=True)
    grads = attention_grads(lanes)
    returned = lax.all_to_all(grads, "space", split_axis=0, concat_axis=0, tiled=True)
    d_packed = (
        returned.reshape(heads, windows, OWN, 3, HD)
        .transpose(1, 2, 3, 0, 4)
        .reshape(row_total, 3 * D)
    )
    my_rows = lax.psum_scatter(
        contract(hidden, d_packed, 0, 0).astype(jnp.bfloat16),
        "space",
        scatter_dimension=0,
        tiled=True,
    )
    row_block = my_rows.shape[0]
    col_block = 3 * D // tm_count
    qkv_parts = lax.all_to_all(
        my_rows.reshape(row_block, tm_count, col_block).transpose(1, 0, 2),
        "tm",
        split_axis=0,
        concat_axis=0,
        tiled=True,
    )
    d_qkv_weight = jnp.sum(qkv_parts.astype(jnp.float32), axis=0)
    d_hidden = contract(d_packed, full_qkv, 1, 1)
    first_mean = jnp.mean(d_hidden, axis=1, keepdims=True)
    second_mean = jnp.mean(d_hidden * normed, axis=1, keepdims=True)
    d_tokens = (inverse * (d_hidden - first_mean - normed * second_mean)).astype(jnp.bfloat16)
    embed_partial = contract(chosen, d_tokens, 0, 0)
    embed_block = D // tm_count
    embed_parts = lax.all_to_all(
        embed_partial.astype(jnp.bfloat16).reshape(PATCH, tm_count, embed_block).transpose(1, 0, 2),
        "tm",
        split_axis=0,
        concat_axis=0,
        tiled=True,
    )
    embed_cols = jnp.sum(embed_parts.astype(jnp.float32), axis=0)
    chunk = -(-PATCH // slab_count)
    padded = jnp.pad(embed_cols, ((0, chunk * slab_count - PATCH), (0, 0)))
    spread = lax.all_to_all(
        padded.reshape(slab_count, chunk, -1), "space", split_axis=0, concat_axis=0, tiled=True
    )
    reduced = jnp.sum(spread, axis=0)
    gathered = lax.all_to_all(
        jnp.broadcast_to(reduced[None], (slab_count,) + reduced.shape),
        "space",
        split_axis=0,
        concat_axis=0,
        tiled=True,
    )
    d_embed_weight = (
        gathered.reshape(chunk * slab_count, -1)[:PATCH]
        .reshape(4, 6, 6, 6, -1)
        .transpose(0, 2, 3, 1, 4)
        .reshape(PATCH, -1)
    )
    return (d_qkv_weight, d_embed_weight)


def solution(mesh):
    placed = (
        P(None, "tm", "space", None),
        P(None, "space"),
        P(None, "space"),
        P(None, "tm"),
        P("space", "tm"),
        P(None, "tm", "space", None),
    )
    return jax.shard_map(
        body,
        mesh=mesh,
        in_specs=placed,
        out_specs=(P("space", "tm"), P(None, "tm")),
        check_vma=False,
    )
```
